32 devices in a mesh: layer: 4 (over x, core), row: 4 (over z), col: 2 (over y).
Axes of the slice: x: 2, y: 2, z: 4, core: 2. Of those that a mesh axis runs over, the one named last changes fastest.
Arguments:
- sources: float32 [8, 256, 1024], P('layer', 'row', 'col'), may hold values from -14 to 14
- conduct: float32 [8, 256, 1024], P('layer', 'row', 'col'), may hold values from 0.5 to 4
- via_cond: float32 [8, 256, 1024], P('layer', 'row', 'col'), may hold values from 0.5 to 4
- via_map: int32 [8, 256, 1024], P('layer', 'row', 'col'), may hold values 0 or 1
- pad_map: int32 [256, 1024], P('row', 'col'), may hold values 0 or 1
- port_tile: int32 [4, 512], replicated, may hold values from 0 to 1023
- pivots: float32 [4, 512, 512], P(None, 'col'), may hold values from -1 to 2, as said below
- coupling: float32 [3, 512, 512], P(None, 'col'), may hold values from -0.109375 to 0.109375
Outputs:
- drop: float32 [8, 256, 1024], P('layer', 'row', 'col')
- ports: float32 [4, 512], replicated
The draws below stay inside these ranges and needn't reach their ends.
Inputs may be any that keep to these rules, and one draw needn't show every extreme that they name: `pivots`: each block is symmetric.
All inputs are finite; a program needn't handle non-finite values. No bound on the sum of `via_map` or of `pad_map` on one device may be relied on, other than what follows from the above.
Results may differ from the reference program's by a relative error of at most 0.00023.
Values sent between devices are 32-bit elements; how exact they have to be, the bound alone decides.
No kernel may reach another device: no remote copies, remote signals or barrier semaphores. Data moves between devices by JAX's collectives and lax.ppermute only.
A program may use at most 64 MiB of HBM per device.

```python
import math
import jax
import jax.numpy as jnp
from jax import lax

TILE = 16
PANEL = 512
NPANEL = 4
DEG = 3
ITERS = 2
NL = 8
NR = 256
NC = 1024
NTILES = 1024


def draw_sources(key, part):
    rough_key = jax.random.fold_in(key, 0)
    return jnp.clip(jax.random.normal(rough_key, (NL, NR, NC), jnp.float32), -6.0, 6.0)


def draw_pivots(key, part):
    rough_key, diag_key = jax.random.split(jax.random.fold_in(key, 17))
    spread = jax.random.normal(rough_key, (NPANEL, PANEL, PANEL), jnp.float32) * (0.4 / math.sqrt(PANEL))
    symmetric = (spread + jnp.transpose(spread, (0, 2, 1))) * 0.7071
    leading = jax.random.uniform(diag_key, (NPANEL, PANEL, 1), jnp.float32, 0.5, 1.0)
    identity = (lax_iota_rows() == lax_iota_cols()).astype(jnp.float32)
    return symmetric + identity * leading


def lax_iota_rows():
    return jnp.arange(PANEL, dtype=jnp.int32)[None, :, None]


def lax_iota_cols():
    return jnp.arange(PANEL, dtype=jnp.int32)[None, None, :]


def touch_ends(values, own_key, least, top_value):
    extent = values.shape
    spot = [jax.random.randint(jax.random.fold_in(own_key, axis), (), 0, extent[axis]) for axis in range(len(extent))]
    values = values.at[tuple(spot)].set(least)
    longest = extent.index(max(extent))
    spot[longest] = (spot[longest] + 1) % extent[longest]
    return values.at[tuple(spot)].set(top_value)


def steps_of(key, dims, pieces, least, largest):
    def one(axis_at, blocks):
        draws = jax.random.uniform(jax.random.fold_in(jax.random.fold_in(key, 6), axis_at), (blocks,), jnp.float32, least / len(pieces), largest / len(pieces))
        return jnp.repeat(jnp.exp(draws), dims[axis_at] // blocks).reshape((-1,) + (1,) * (len(dims) - axis_at - 1))

    level = one(*pieces[0])
    for cut in pieces[1:]:
        level = level * one(*cut)
    return level


def noise(stream_key, dims, deviation, limit, cuts=(), held_as=jnp.bfloat16):
    values = jax.random.normal(stream_key, dims, jnp.float32) * deviation
    if len(cuts) > 0:
        values = steps_of(stream_key, dims, cuts, -0.22, 0.18) * values
    return jnp.clip(values, min=-limit, max=limit).astype(held_as)


def setup_inputs(seed: int = 0) -> dict:
    splits = jax.random.split(jax.random.key(seed), 9)
    sources = draw_sources(jax.random.fold_in(splits[8], 71), 0)
    conduct = jnp.clip(jnp.exp(math.log(4.0) - 2.0794415 * jax.random.uniform(splits[1], (NL, NR, NC), jnp.float32) ** steps_of(splits[1], (NL, NR, NC), ((0, 4), (1, 4), (2, 2)), -0.2, 0.2)), 0.5, 4.0)
    via_cond = jnp.clip(jnp.exp(math.log(4.0) - 2.0794415 * jax.random.uniform(splits[2], (NL, NR, NC), jnp.float32) ** steps_of(splits[2], (NL, NR, NC), ((0, 4), (1, 4), (2, 2)), -0.2, 0.2)), 0.5, 4.0)
    via_map = touch_ends((jax.random.randint(splits[3], (NL, NR, NC), 0, 4) < 3).astype(jnp.int32), jax.random.fold_in(splits[3], 1), 0, 1)
    pad_map = touch_ends((jax.random.randint(splits[4], (NR, NC), 0, 16) < 1).astype(jnp.int32), jax.random.fold_in(splits[4], 1), 0, 1)
    port_tile = touch_ends(jax.random.randint(splits[5], (NPANEL, PANEL), 0, NTILES), jax.random.fold_in(splits[5], 1), 0, NTILES - 1).astype(jnp.int32)
    pivots = draw_pivots(jax.random.fold_in(splits[8], 71), 0)
    coupling = noise(splits[7], (NPANEL - 1, PANEL, PANEL), (6 * PANEL) ** -0.5, 0.109375, ((1, 2),), jnp.float32)
    return dict(sources=sources, conduct=conduct, via_cond=via_cond, via_map=via_map, pad_map=pad_map, port_tile=port_tile, pivots=pivots, coupling=coupling)


pad_gain = 8.0
bound_low = 0.1
bound_high = 1.9
restrict_scale = 0.25
prolong_scale = 0.5

def shifted(grown):
    return (grown[2:, 1:-1, 1:-1], grown[:-2, 1:-1, 1:-1], grown[1:-1, 2:, 1:-1], grown[1:-1, :-2, 1:-1], grown[1:-1, 1:-1, 2:], grown[1:-1, 1:-1, :-2])

def apply_grid(field, weights, pad_term):
    result = pad_term * field
    for weight, other in zip(weights, shifted(jnp.pad(field, 1))):
        result = result + weight * (field - other)
    return result

def smooth(resid, weights, pad_term, inverse):
    theta = (bound_high + bound_low) / 2.0
    delta = (bound_high - bound_low) / 2.0
    sigma = theta / delta
    rho = 1.0 / sigma
    change = inverse * resid / theta
    total = change
    for sweep in range(DEG - 1):
        remain = resid - apply_grid(total, weights, pad_term)
        rho_new = 1.0 / (2.0 * sigma - rho)
        change = rho_new * rho * change + 2.0 * rho_new / delta * inverse * remain
        total = total + change
        rho = rho_new
    return total

def coarse(resid, port_tile, pivots, coupling):
    highest = lax.Precision.HIGHEST
    plane = lax.optimization_barrier(jnp.sum(resid, axis=0))
    tiles = plane.reshape(NR // TILE, TILE, NC // TILE, TILE).sum(axis=(1, 3)).reshape(-1)
    rhs = tiles[port_tile] * (restrict_scale / TILE)
    forward = [rhs[0]]
    for section in range(1, NPANEL):
        forward.append(rhs[section] - jnp.dot(coupling[section - 1], forward[-1], precision=highest))
    scaled = [jnp.dot(pivots[section], forward[section], precision=highest) for section in range(NPANEL)]
    results = [scaled[NPANEL - 1]]
    for section in range(NPANEL - 2, -1, -1):
        results.insert(0, scaled[section] - jnp.dot(results[0], coupling[section], precision=highest))
    ports = jnp.stack(results)
    tile_values = jax.ops.segment_sum(ports.reshape(-1), port_tile.reshape(-1).astype(jnp.int32), num_segments=NTILES)
    tile_grid = tile_values.reshape(NR // TILE, 1, NC // TILE, 1)
    field = jnp.broadcast_to(tile_grid, (NR // TILE, TILE, NC // TILE, TILE)).reshape(NR, NC) * prolong_scale
    return (ports, jnp.broadcast_to(field[None], (NL, NR, NC)))

def reference(sources, conduct, via_cond, via_map, pad_map, port_tile, pivots, coupling):
    vertical = via_cond * via_map.astype(jnp.float32)
    near_plane = shifted(jnp.pad(conduct, 1))
    near_vert = shifted(jnp.pad(vertical, 1))
    weights = (jnp.sqrt(vertical * near_vert[0]), jnp.sqrt(vertical * near_vert[1]), jnp.sqrt(conduct * near_plane[2]), jnp.sqrt(conduct * near_plane[3]), jnp.sqrt(conduct * near_plane[4]), jnp.sqrt(conduct * near_plane[5]))
    pad_term = jnp.zeros((NL, NR, NC), jnp.float32).at[NL - 1].set(pad_gain * pad_map.astype(jnp.float32))
    diagonal = pad_term
    for weight in weights:
        diagonal = diagonal + weight
    inverse = 1.0 / diagonal
    drop = jnp.zeros((NL, NR, NC), jnp.float32)
    ports = jnp.zeros((NPANEL, PANEL), jnp.float32)
    for outer in range(ITERS):
        resid = sources - apply_grid(drop, weights, pad_term)
        ports, lifted = coarse(resid, port_tile, pivots, coupling)
        drop = drop + lifted + smooth(resid, weights, pad_term, inverse)
    return (drop, ports)
```

```python
import jax
import jax.numpy as jnp
from jax import lax
from jax.sharding import PartitionSpec as P

TILE = 16
PANEL = 512
NPANEL = 4
DEG = 3
ITERS = 2


pad_gain = 8.0
bound_low = 0.1
bound_high = 1.9
restrict_scale = 0.25
prolong_scale = 0.5

highest = lax.Precision.HIGHEST
GRID_AXES = (("layer", 0), ("row", 1), ("col", 2))


def rims(field, axis, dim):
    count = lax.axis_size(axis)
    size = field.shape[dim]
    head = lax.slice_in_dim(field, 0, 1, axis=dim)
    tail = lax.slice_in_dim(field, size - 1, size, axis=dim)
    below = lax.ppermute(tail, axis, [(i, i + 1) for i in range(count - 1)])
    above = lax.ppermute(head, axis, [(i + 1, i) for i in range(count - 1)])
    return above, below


def neighbours(field, halo):
    out = []
    for (axis, dim), (above, below) in zip(GRID_AXES, halo):
        size = field.shape[dim]
        out.append(jnp.concatenate([lax.slice_in_dim(field, 1, size, axis=dim), above], axis=dim))
        out.append(jnp.concatenate([below, lax.slice_in_dim(field, 0, size - 1, axis=dim)], axis=dim))
    return out


def exchange(field):
    return [rims(field, axis, dim) for axis, dim in GRID_AXES]


def apply_grid(field, near, weights, pad_term):
    result = pad_term * field
    for weight, other in zip(weights, near):
        result = result + weight * (field - other)
    return result


def smooth(resid, weights, pad_term, inverse):
    theta = (bound_high + bound_low) / 2.0
    delta = (bound_high - bound_low) / 2.0
    sigma = theta / delta
    rho = 1.0 / sigma
    change = inverse * resid / theta
    total = change
    for sweep in range(DEG - 1):
        remain = resid - apply_grid(total, neighbours(total, exchange(total)), weights, pad_term)
        rho_new = 1.0 / (2.0 * sigma - rho)
        change = rho_new * rho * change + 2.0 * rho_new / delta * inverse * remain
        total = total + change
        rho = rho_new
    return total


def all_sum(value):
    for axis, _ in GRID_AXES:
        count = lax.axis_size(axis)
        if count & (count - 1):
            value = lax.psum(value, axis)
            continue
        step = 1
        while step < count:
            value = value + lax.ppermute(value, axis, [(i, i ^ step) for i in range(count)])
            step *= 2
    return value


def swap_col(value):
    return lax.ppermute(value, "col", [(0, 1), (1, 0)])


def join_halves(mine, other, low):
    return jnp.where(low, jnp.concatenate([mine, other]), jnp.concatenate([other, mine]))


def coarse_pair(rhs, pivots, coupling):
    share = pivots.shape[1]
    low = lax.axis_index("col") == 0
    start = lax.axis_index("col") * share
    own = lambda vector: lax.dynamic_slice_in_dim(vector, start, share)
    other_half = lambda vector: lax.dynamic_slice_in_dim(vector, share - start, share)
    full = rhs[0]
    forward = [full]
    for section in range(1, NPANEL):
        piece = own(rhs[section]) - jnp.dot(coupling[section - 1], full, precision=highest)
        full = join_halves(piece, swap_col(piece), low)
        forward.append(full)
    scaled = [jnp.dot(pivots[section], forward[section], precision=highest) for section in range(NPANEL)]
    mine = scaled[NPANEL - 1]
    results = [None] * NPANEL
    for section in range(NPANEL - 2, 0, -1):
        partial = jnp.dot(mine, coupling[section], precision=highest)
        got = swap_col(jnp.concatenate([other_half(partial), mine]))
        results[section + 1] = join_halves(mine, got[share:], low)
        mine = scaled[section] - (own(partial) + got[:share])
    partial = jnp.dot(mine, coupling[0], precision=highest)
    got = swap_col(jnp.concatenate([partial, scaled[0], mine]))
    results[1] = join_halves(mine, got[PANEL + share:], low)
    first = join_halves(scaled[0], got[PANEL:PANEL + share], low)
    low_part = jnp.where(low, partial, got[:PANEL])
    high_part = jnp.where(low, got[:PANEL], partial)
    results[0] = first - (low_part + high_part)
    return jnp.stack(results)


def coarse_general(rhs, pivots, coupling):
    share = pivots.shape[1]
    start = lax.axis_index("col") * share
    full = rhs[0]
    forward = [full]
    for section in range(1, NPANEL):
        piece = lax.dynamic_slice_in_dim(rhs[section], start, share) - jnp.dot(
            coupling[section - 1], full, precision=highest
        )
        full = lax.all_gather(piece, "col", axis=0, tiled=True)
        forward.append(full)
    scaled = [jnp.dot(pivots[section], forward[section], precision=highest) for section in range(NPANEL)]
    results = [None] * NPANEL
    for section in range(NPANEL - 1, -1, -1):
        placed = lax.dynamic_update_slice_in_dim(jnp.zeros((PANEL,), jnp.float32), scaled[section], start, 0)
        if section < NPANEL - 1:
            later_rows = lax.dynamic_slice_in_dim(results[section + 1], start, share)
            placed = placed - jnp.dot(later_rows, coupling[section], precision=highest)
        results[section] = lax.psum(placed, "col")
    return jnp.stack(results)


def expand(values, edge):
    inner = values[1:-1] if edge else values
    body = jnp.repeat(inner, TILE, axis=0)
    if edge:
        body = jnp.concatenate([values[:1], body, values[-1:]], axis=0)
    return body


def shards(sources, conduct, via_cond, via_map, pad_map, port_tile, pivots, coupling):
    layer_count = lax.axis_size("layer")
    local_layers, grid_rows, grid_cols = sources.shape
    vertical = via_cond * via_map.astype(jnp.float32)
    vert_above, vert_below = rims(vertical, "layer", 0)
    row_halo = rims(conduct, "row", 1)
    col_halo = rims(conduct, "col", 2)
    near_vert = neighbours(vertical, [(vert_above, vert_below), row_halo, col_halo])
    near_plane = neighbours(conduct, [(vert_above, vert_below), row_halo, col_halo])
    weights = (
        jnp.sqrt(vertical * near_vert[0]),
        jnp.sqrt(vertical * near_vert[1]),
        jnp.sqrt(conduct * near_plane[2]),
        jnp.sqrt(conduct * near_plane[3]),
        jnp.sqrt(conduct * near_plane[4]),
        jnp.sqrt(conduct * near_plane[5]),
    )
    top_flag = (lax.axis_index("layer") == layer_count - 1).astype(jnp.float32)
    top_layer = pad_gain * pad_map.astype(jnp.float32) * top_flag
    pad_term = jnp.concatenate(
        (jnp.zeros((local_layers - 1, grid_rows, grid_cols), jnp.float32), top_layer[None]), 0
    )
    diagonal = pad_term
    for weight in weights:
        diagonal = diagonal + weight
    inverse = 1.0 / diagonal

    col_count = lax.axis_size("col")
    tile_cols = grid_cols * col_count // TILE
    tile_rows = grid_rows * lax.axis_size("row") // TILE
    own_rows = grid_rows // TILE
    own_cols = grid_cols // TILE
    first_row = lax.axis_index("row") * own_rows
    first_col = lax.axis_index("col") * own_cols
    flat_tiles = port_tile.reshape(-1)
    local_ids = (
        (first_row + jnp.arange(own_rows, dtype=jnp.int32))[:, None] * tile_cols
        + (first_col + jnp.arange(own_cols, dtype=jnp.int32))[None, :]
    ).reshape(-1)
    gather_local = (flat_tiles[:, None] == local_ids[None, :]).astype(jnp.float32)
    ring_rows = first_row - 1 + jnp.arange(own_rows + 2, dtype=jnp.int32)
    ring_cols = first_col - 1 + jnp.arange(own_cols + 2, dtype=jnp.int32)
    ring_ok = ((ring_rows >= 0) & (ring_rows < tile_rows))[:, None] & ((ring_cols >= 0) & (ring_cols < tile_cols))[None, :]
    ring_ids = jnp.where(ring_ok, ring_rows[:, None] * tile_cols + ring_cols[None, :], -1).reshape(-1)
    scatter_ring = (ring_ids[:, None] == flat_tiles[None, :]).astype(jnp.float32)
    coarse = coarse_pair if col_count == 2 else coarse_general

    drop = None
    drop_near = None
    for outer in range(ITERS):
        if drop is None:
            resid = sources
        else:
            resid = sources - apply_grid(drop, drop_near, weights, pad_term)
        plane = jnp.sum(resid, axis=0)
        tiles = plane.reshape(own_rows, TILE, own_cols, TILE).sum(axis=(1, 3)).reshape(-1)
        local_rhs = jnp.dot(gather_local, tiles, precision=highest)
        rhs = all_sum(local_rhs).reshape(NPANEL, PANEL) * (restrict_scale / TILE)
        ports = coarse(rhs, pivots, coupling)
        tile_values = jnp.dot(scatter_ring, ports.reshape(-1), precision=highest).reshape(own_rows + 2, own_cols + 2)
        ring = expand(expand(tile_values, True).T, True).T * prolong_scale
        centre = ring[1:-1, 1:-1]
        lifted = jnp.broadcast_to(centre[None], (local_layers, grid_rows, grid_cols))
        total = smooth(resid, weights, pad_term, inverse)
        if outer == ITERS - 1:
            drop = (lifted if drop is None else drop + lifted) + total
            break
        lifted_near = [lifted, lifted]
        for part in (ring[2:, 1:-1], ring[:-2, 1:-1], ring[1:-1, 2:], ring[1:-1, :-2]):
            lifted_near.append(jnp.broadcast_to(part[None], (local_layers, grid_rows, grid_cols)))
        total_near = neighbours(total, exchange(total))
        if drop is None:
            drop = lifted + total
            drop_near = [a + b for a, b in zip(lifted_near, total_near)]
        else:
            drop = drop + lifted + total
            drop_near = [(d + a) + b for d, a, b in zip(drop_near, lifted_near, total_near)]
    return (drop, ports)


def solution(mesh):
    placed = (
        P("layer", "row", "col"),
        P("layer", "row", "col"),
        P("layer", "row", "col"),
        P("layer", "row", "col"),
        P("row", "col"),
        P(),
        P(None, "col", None),
        P(None, "col", None),
    )
    return jax.shard_map(
        shards,
        mesh=mesh,
        in_specs=placed,
        out_specs=(P("layer", "row", "col"), P()),
        check_vma=False,
    )
```

```python
import jax
import jax.numpy as jnp
from jax import lax
from jax.sharding import PartitionSpec as P

TILE = 16
PANEL = 512
NPANEL = 4
DEG = 3
ITERS = 2


pad_gain = 8.0
bound_low = 0.1
bound_high = 1.9
restrict_scale = 0.25
prolong_scale = 0.5

highest = lax.Precision.HIGHEST
GRID_AXES = (("layer", 0), ("row", 1), ("col", 2))
ROW_AXES = ("layer", "row")


def axis_count(axis):
    names = axis if isinstance(axis, tuple) else (axis,)
    count = 1
    for name in names:
        count *= lax.axis_size(name)
    return count


def rims(field, axis, dim):
    size = field.shape[dim]
    head = lax.slice_in_dim(field, 0, 1, axis=dim)
    tail = lax.slice_in_dim(field, size - 1, size, axis=dim)
    if axis is None:
        return jnp.zeros_like(head), jnp.zeros_like(tail)
    count = axis_count(axis)
    place = list(range(count))
    if axis == ROW_AXES:
        layers, rows = lax.axis_size("layer"), lax.axis_size("row")
        place = [(b % layers) * rows + b // layers for b in range(count)]
    if count == 2:
        low = lax.axis_index(axis) == 0
        got = lax.ppermute(jnp.where(low, tail, head), axis, [(0, 1), (1, 0)])
        zero = jnp.zeros_like(got)
        return jnp.where(low, got, zero), jnp.where(low, zero, got)
    below = lax.ppermute(tail, axis, [(place[i], place[i + 1]) for i in range(count - 1)])
    above = lax.ppermute(head, axis, [(place[i + 1], place[i]) for i in range(count - 1)])
    return above, below


def neighbours(field, halo):
    out = []
    for (axis, dim), (above, below) in zip(GRID_AXES, halo):
        size = field.shape[dim]
        out.append(jnp.concatenate([lax.slice_in_dim(field, 1, size, axis=dim), above], axis=dim))
        out.append(jnp.concatenate([below, lax.slice_in_dim(field, 0, size - 1, axis=dim)], axis=dim))
    return out


def exchange(field):
    return [rims(field, axis, dim) for axis, dim in ((None, 0), (ROW_AXES, 1), ("col", 2))]


def apply_grid(field, near, weights, pad_term):
    result = pad_term * field
    for weight, other in zip(weights, near):
        result = result + weight * (field - other)
    return result


def smooth(resid, weights, pad_term, inverse):
    theta = (bound_high + bound_low) / 2.0
    delta = (bound_high - bound_low) / 2.0
    sigma = theta / delta
    rho = 1.0 / sigma
    change = inverse * resid / theta
    total = change
    for sweep in range(DEG - 1):
        remain = resid - apply_grid(total, neighbours(total, exchange(total)), weights, pad_term)
        rho_new = 1.0 / (2.0 * sigma - rho)
        change = rho_new * rho * change + 2.0 * rho_new / delta * inverse * remain
        total = total + change
        rho = rho_new
    return total


def all_sum(value):
    for axis, _ in GRID_AXES:
        count = lax.axis_size(axis)
        if count & (count - 1):
            value = lax.psum(value, axis)
            continue
        step = 1
        while step < count:
            value = value + lax.ppermute(value, axis, [(i, i ^ step) for i in range(count)])
            step *= 2
    return value


def swap_col(value):
    return lax.ppermute(value, "col", [(0, 1), (1, 0)])


def join_halves(mine, other, low):
    return jnp.where(low, jnp.concatenate([mine, other]), jnp.concatenate([other, mine]))


def coarse_pair(rhs, pivots, coupling):
    share = pivots.shape[1]
    low = lax.axis_index("col") == 0
    start = lax.axis_index("col") * share
    own = lambda vector: lax.dynamic_slice_in_dim(vector, start, share)
    other_half = lambda vector: lax.dynamic_slice_in_dim(vector, share - start, share)
    full = rhs[0]
    forward = [full]
    for section in range(1, NPANEL):
        piece = own(rhs[section]) - jnp.dot(coupling[section - 1], full, precision=highest)
        full = join_halves(piece, swap_col(piece), low)
        forward.append(full)
    scaled = [jnp.dot(pivots[section], forward[section], precision=highest) for section in range(NPANEL)]
    mine = scaled[NPANEL - 1]
    results = [None] * NPANEL
    for section in range(NPANEL - 2, 0, -1):
        partial = jnp.dot(mine, coupling[section], precision=highest)
        got = swap_col(jnp.concatenate([other_half(partial), mine]))
        results[section + 1] = join_halves(mine, got[share:], low)
        mine = scaled[section] - (own(partial) + got[:share])
    partial = jnp.dot(mine, coupling[0], precision=highest)
    got = swap_col(jnp.concatenate([partial, scaled[0], mine]))
    results[1] = join_halves(mine, got[PANEL + share:], low)
    first = join_halves(scaled[0], got[PANEL:PANEL + share], low)
    low_part = jnp.where(low, partial, got[:PANEL])
    high_part = jnp.where(low, got[:PANEL], partial)
    results[0] = first - (low_part + high_part)
    return jnp.stack(results)


def coarse_general(rhs, pivots, coupling):
    share = pivots.shape[1]
    start = lax.axis_index("col") * share
    full = rhs[0]
    forward = [full]
    for section in range(1, NPANEL):
        piece = lax.dynamic_slice_in_dim(rhs[section], start, share) - jnp.dot(
            coupling[section - 1], full, precision=highest
        )
        full = lax.all_gather(piece, "col", axis=0, tiled=True)
        forward.append(full)
    scaled = [jnp.dot(pivots[section], forward[section], precision=highest) for section in range(NPANEL)]
    results = [None] * NPANEL
    for section in range(NPANEL - 1, -1, -1):
        placed = lax.dynamic_update_slice_in_dim(jnp.zeros((PANEL,), jnp.float32), scaled[section], start, 0)
        if section < NPANEL - 1:
            later_rows = lax.dynamic_slice_in_dim(results[section + 1], start, share)
            placed = placed - jnp.dot(later_rows, coupling[section], precision=highest)
        results[section] = lax.psum(placed, "col")
    return jnp.stack(results)


def expand(values, edge):
    inner = values[1:-1] if edge else values
    body = jnp.repeat(inner, TILE, axis=0)
    if edge:
        body = jnp.concatenate([values[:1], body, values[-1:]], axis=0)
    return body


def shards(sources, conduct, via_cond, via_map, pad_map, port_tile, pivots, coupling):
    layer_count = lax.axis_size("layer")
    vertical = via_cond * via_map.astype(jnp.float32)
    packed = lax.all_to_all(jnp.stack((sources, conduct, vertical)), "layer", 2, 1, tiled=True)
    sources, conduct, vertical = packed[0], packed[1], packed[2]
    local_layers, grid_rows, grid_cols = sources.shape
    pad_rows = lax.dynamic_slice_in_dim(pad_map, lax.axis_index("layer") * grid_rows, grid_rows, 0)
    row_halo = rims(conduct, ROW_AXES, 1)
    col_halo = rims(conduct, "col", 2)
    layer_halo = rims(vertical, None, 0)
    near_vert = neighbours(vertical, [layer_halo, row_halo, col_halo])
    near_plane = neighbours(conduct, [layer_halo, row_halo, col_halo])
    weights = (
        jnp.sqrt(vertical * near_vert[0]),
        jnp.sqrt(vertical * near_vert[1]),
        jnp.sqrt(conduct * near_plane[2]),
        jnp.sqrt(conduct * near_plane[3]),
        jnp.sqrt(conduct * near_plane[4]),
        jnp.sqrt(conduct * near_plane[5]),
    )
    top_layer = pad_gain * pad_rows.astype(jnp.float32)
    pad_term = jnp.concatenate(
        (jnp.zeros((local_layers - 1, grid_rows, grid_cols), jnp.float32), top_layer[None]), 0
    )
    diagonal = pad_term
    for weight in weights:
        diagonal = diagonal + weight
    inverse = 1.0 / diagonal

    col_count = lax.axis_size("col")
    tile_cols = grid_cols * col_count // TILE
    tile_rows = grid_rows * axis_count(ROW_AXES) // TILE
    own_rows = grid_rows // TILE
    own_cols = grid_cols // TILE
    first_row = (lax.axis_index("row") * layer_count + lax.axis_index("layer")) * own_rows
    first_col = lax.axis_index("col") * own_cols
    flat_tiles = port_tile.reshape(-1)
    local_ids = (
        (first_row + jnp.arange(own_rows, dtype=jnp.int32))[:, None] * tile_cols
        + (first_col + jnp.arange(own_cols, dtype=jnp.int32))[None, :]
    ).reshape(-1)
    gather_local = (flat_tiles[:, None] == local_ids[None, :]).astype(jnp.float32)
    ring_rows = first_row - 1 + jnp.arange(own_rows + 2, dtype=jnp.int32)
    ring_cols = first_col - 1 + jnp.arange(own_cols + 2, dtype=jnp.int32)
    ring_ok = ((ring_rows >= 0) & (ring_rows < tile_rows))[:, None] & ((ring_cols >= 0) & (ring_cols < tile_cols))[None, :]
    ring_ids = jnp.where(ring_ok, ring_rows[:, None] * tile_cols + ring_cols[None, :], -1).reshape(-1)
    scatter_ring = (ring_ids[:, None] == flat_tiles[None, :]).astype(jnp.float32)
    coarse = coarse_pair if col_count == 2 else coarse_general

    drop = None
    drop_near = None
    for outer in range(ITERS):
        if drop is None:
            resid = sources
        else:
            resid = sources - apply_grid(drop, drop_near, weights, pad_term)
        plane = jnp.sum(resid, axis=0)
        tiles = plane.reshape(own_rows, TILE, own_cols, TILE).sum(axis=(1, 3)).reshape(-1)
        local_rhs = jnp.dot(gather_local, tiles, precision=highest)
        rhs = all_sum(local_rhs).reshape(NPANEL, PANEL) * (restrict_scale / TILE)
        ports = coarse(rhs, pivots, coupling)
        tile_values = jnp.dot(scatter_ring, ports.reshape(-1), precision=highest).reshape(own_rows + 2, own_cols + 2)
        ring = expand(expand(tile_values, True).T, True).T * prolong_scale
        centre = ring[1:-1, 1:-1]
        lifted = jnp.broadcast_to(centre[None], (local_layers, grid_rows, grid_cols))
        total = smooth(resid, weights, pad_term, inverse)
        if outer == ITERS - 1:
            drop = (lifted if drop is None else drop + lifted) + total
            break
        lifted_near = [lifted, lifted]
        for part in (ring[2:, 1:-1], ring[:-2, 1:-1], ring[1:-1, 2:], ring[1:-1, :-2]):
            lifted_near.append(jnp.broadcast_to(part[None], (local_layers, grid_rows, grid_cols)))
        total_near = neighbours(total, exchange(total))
        if drop is None:
            drop = lifted + total
            drop_near = [a + b for a, b in zip(lifted_near, total_near)]
        else:
            drop = drop + lifted + total
            drop_near = [(d + a) + b for d, a, b in zip(drop_near, lifted_near, total_near)]
    drop = lax.all_to_all(drop, "layer", 0, 1, tiled=True)
    return (drop, ports)


def solution(mesh):
    placed = (
        P("layer", "row", "col"),
        P("layer", "row", "col"),
        P("layer", "row", "col"),
        P("layer", "row", "col"),
        P("row", "col"),
        P(),
        P(None, "col", None),
        P(None, "col", None),
    )
    return jax.shard_map(
        shards,
        mesh=mesh,
        in_specs=placed,
        out_specs=(P("layer", "row", "col"), P()),
        check_vma=False,
    )
```

```python
import jax
import jax.numpy as jnp
from jax import lax
from jax.sharding import PartitionSpec as P

TILE = 16
PANEL = 512
NPANEL = 4
DEG = 3
ITERS = 2


pad_gain = 8.0
bound_low = 0.1
bound_high = 1.9
restrict_scale = 0.25
prolong_scale = 0.5

highest = lax.Precision.HIGHEST
GRID_AXES = (("layer", 0), ("row", 1), ("col", 2))
ROW_AXES = ("layer", "row")


def axis_count(axis):
    names = axis if isinstance(axis, tuple) else (axis,)
    count = 1
    for name in names:
        count *= lax.axis_size(name)
    return count


def rims(field, axis, dim):
    size = field.shape[dim]
    head = lax.slice_in_dim(field, 0, 1, axis=dim)
    tail = lax.slice_in_dim(field, size - 1, size, axis=dim)
    if axis is None:
        return jnp.zeros_like(head), jnp.zeros_like(tail)
    count = axis_count(axis)
    place = list(range(count))
    if axis == ROW_AXES:
        layers, rows = lax.axis_size("layer"), lax.axis_size("row")
        place = [(b % layers) * rows + b // layers for b in range(count)]
    if count == 2:
        low = lax.axis_index(axis) == 0
        got = lax.ppermute(jnp.where(low, tail, head), axis, [(0, 1), (1, 0)])
        zero = jnp.zeros_like(got)
        return jnp.where(low, got, zero), jnp.where(low, zero, got)
    below = lax.ppermute(tail, axis, [(place[i], place[i + 1]) for i in range(count - 1)])
    above = lax.ppermute(head, axis, [(place[i + 1], place[i]) for i in range(count - 1)])
    return above, below


def neighbours(field, halo):
    out = []
    for (axis, dim), (above, below) in zip(GRID_AXES, halo):
        size = field.shape[dim]
        out.append(jnp.concatenate([lax.slice_in_dim(field, 1, size, axis=dim), above], axis=dim))
        out.append(jnp.concatenate([below, lax.slice_in_dim(field, 0, size - 1, axis=dim)], axis=dim))
    return out


def exchange(field):
    return [rims(field, axis, dim) for axis, dim in ((None, 0), (ROW_AXES, 1), ("col", 2))]


def apply_grid(field, near, weights, pad_term):
    result = pad_term * field
    for weight, other in zip(weights, near):
        result = result + weight * (field - other)
    return result


def smooth(resid, weights, pad_term, inverse):
    theta = (bound_high + bound_low) / 2.0
    delta = (bound_high - bound_low) / 2.0
    sigma = theta / delta
    rho = 1.0 / sigma
    change = inverse * resid / theta
    total = change
    for sweep in range(DEG - 1):
        remain = resid - apply_grid(total, neighbours(total, exchange(total)), weights, pad_term)
        rho_new = 1.0 / (2.0 * sigma - rho)
        change = rho_new * rho * change + 2.0 * rho_new / delta * inverse * remain
        total = total + change
        rho = rho_new
    return total


def all_sum(value):
    for axis, _ in GRID_AXES:
        count = lax.axis_size(axis)
        if count & (count - 1):
            value = lax.psum(value, axis)
            continue
        step = 1
        while step < count:
            value = value + lax.ppermute(value, axis, [(i, i ^ step) for i in range(count)])
            step *= 2
    return value


def swap_col(value):
    return lax.ppermute(value, "col", [(0, 1), (1, 0)])


def join_halves(mine, other, low):
    return jnp.where(low, jnp.concatenate([mine, other]), jnp.concatenate([other, mine]))


def coarse_pair(rhs, pivots, coupling):
    share = pivots.shape[1]
    low = lax.axis_index("col") == 0
    start = lax.axis_index("col") * share
    own = lambda vector: lax.dynamic_slice_in_dim(vector, start, share)
    other_half = lambda vector: lax.dynamic_slice_in_dim(vector, share - start, share)
    full = rhs[0]
    forward = [full]
    for section in range(1, NPANEL):
        piece = own(rhs[section]) - jnp.dot(coupling[section - 1], full, precision=highest)
        full = join_halves(piece, swap_col(piece), low)
        forward.append(full)
    scaled = [jnp.dot(pivots[section], forward[section], precision=highest) for section in range(NPANEL)]
    mine = scaled[NPANEL - 1]
    results = [None] * NPANEL
    for section in range(NPANEL - 2, 0, -1):
        partial = jnp.dot(mine, coupling[section], precision=highest)
        got = swap_col(jnp.concatenate([other_half(partial), mine]))
        results[section + 1] = join_halves(mine, got[share:], low)
        mine = scaled[section] - (own(partial) + got[:share])
    partial = jnp.dot(mine, coupling[0], precision=highest)
    got = swap_col(jnp.concatenate([partial, scaled[0], mine]))
    results[1] = join_halves(mine, got[PANEL + share:], low)
    first = join_halves(scaled[0], got[PANEL:PANEL + share], low)
    low_part = jnp.where(low, partial, got[:PANEL])
    high_part = jnp.where(low, got[:PANEL], partial)
    results[0] = first - (low_part + high_part)
    return jnp.stack(results)


def coarse_general(rhs, pivots, coupling):
    share = pivots.shape[1]
    start = lax.axis_index("col") * share
    full = rhs[0]
    forward = [full]
    for section in range(1, NPANEL):
        piece = lax.dynamic_slice_in_dim(rhs[section], start, share) - jnp.dot(
            coupling[section - 1], full, precision=highest
        )
        full = lax.all_gather(piece, "col", axis=0, tiled=True)
        forward.append(full)
    scaled = [jnp.dot(pivots[section], forward[section], precision=highest) for section in range(NPANEL)]
    results = [None] * NPANEL
    for section in range(NPANEL - 1, -1, -1):
        placed = lax.dynamic_update_slice_in_dim(jnp.zeros((PANEL,), jnp.float32), scaled[section], start, 0)
        if section < NPANEL - 1:
            later_rows = lax.dynamic_slice_in_dim(results[section + 1], start, share)
            placed = placed - jnp.dot(later_rows, coupling[section], precision=highest)
        results[section] = lax.psum(placed, "col")
    return jnp.stack(results)


def expand(values, edge):
    inner = values[1:-1] if edge else values
    body = jnp.repeat(inner, TILE, axis=0)
    if edge:
        body = jnp.concatenate([values[:1], body, values[-1:]], axis=0)
    return body


def shards(sources, conduct, via_cond, via_map, pad_map, port_tile, pivots, coupling):
    layer_count = lax.axis_size("layer")
    col_count = lax.axis_size("col")
    flat_tiles = port_tile.reshape(-1)
    tile_cols = sources.shape[2] * col_count // TILE
    start_rows = sources.shape[1] // TILE
    start_cols = sources.shape[2] // TILE
    start_ids = (
        (lax.axis_index("row") * start_rows + jnp.arange(start_rows, dtype=jnp.int32))[:, None] * tile_cols
        + (lax.axis_index("col") * start_cols + jnp.arange(start_cols, dtype=jnp.int32))[None, :]
    ).reshape(-1)
    start_plane = jnp.sum(sources, axis=0)
    start_tiles = start_plane.reshape(start_rows, TILE, start_cols, TILE).sum(axis=(1, 3)).reshape(-1)
    start_rhs = jnp.dot((flat_tiles[:, None] == start_ids[None, :]).astype(jnp.float32), start_tiles, precision=highest)
    vertical = via_cond * via_map.astype(jnp.float32)
    packed = lax.all_to_all(jnp.stack((sources, conduct, vertical)), "layer", 2, 1, tiled=True)
    sources, conduct, vertical = packed[0], packed[1], packed[2]
    local_layers, grid_rows, grid_cols = sources.shape
    pad_rows = lax.dynamic_slice_in_dim(pad_map, lax.axis_index("layer") * grid_rows, grid_rows, 0)
    row_halo = rims(conduct, ROW_AXES, 1)
    col_halo = rims(conduct, "col", 2)
    layer_halo = rims(vertical, None, 0)
    near_vert = neighbours(vertical, [layer_halo, row_halo, col_halo])
    near_plane = neighbours(conduct, [layer_halo, row_halo, col_halo])
    weights = (
        jnp.sqrt(vertical * near_vert[0]),
        jnp.sqrt(vertical * near_vert[1]),
        jnp.sqrt(conduct * near_plane[2]),
        jnp.sqrt(conduct * near_plane[3]),
        jnp.sqrt(conduct * near_plane[4]),
        jnp.sqrt(conduct * near_plane[5]),
    )
    top_layer = pad_gain * pad_rows.astype(jnp.float32)
    pad_term = jnp.concatenate(
        (jnp.zeros((local_layers - 1, grid_rows, grid_cols), jnp.float32), top_layer[None]), 0
    )
    diagonal = pad_term
    for weight in weights:
        diagonal = diagonal + weight
    inverse = 1.0 / diagonal

    tile_rows = grid_rows * axis_count(ROW_AXES) // TILE
    own_rows = grid_rows // TILE
    own_cols = grid_cols // TILE
    first_row = (lax.axis_index("row") * layer_count + lax.axis_index("layer")) * own_rows
    first_col = lax.axis_index("col") * own_cols
    local_ids = (
        (first_row + jnp.arange(own_rows, dtype=jnp.int32))[:, None] * tile_cols
        + (first_col + jnp.arange(own_cols, dtype=jnp.int32))[None, :]
    ).reshape(-1)
    gather_local = (flat_tiles[:, None] == local_ids[None, :]).astype(jnp.float32)
    ring_rows = first_row - 1 + jnp.arange(own_rows + 2, dtype=jnp.int32)
    ring_cols = first_col - 1 + jnp.arange(own_cols + 2, dtype=jnp.int32)
    ring_ok = ((ring_rows >= 0) & (ring_rows < tile_rows))[:, None] & ((ring_cols >= 0) & (ring_cols < tile_cols))[None, :]
    ring_ids = jnp.where(ring_ok, ring_rows[:, None] * tile_cols + ring_cols[None, :], -1).reshape(-1)
    scatter_ring = (ring_ids[:, None] == flat_tiles[None, :]).astype(jnp.float32)
    coarse = coarse_pair if col_count == 2 else coarse_general

    drop = None
    drop_near = None
    for outer in range(ITERS):
        if drop is None:
            resid = sources
        else:
            resid = sources - apply_grid(drop, drop_near, weights, pad_term)
        if drop is None:
            local_rhs = start_rhs
        else:
            plane = jnp.sum(resid, axis=0)
            tiles = plane.reshape(own_rows, TILE, own_cols, TILE).sum(axis=(1, 3)).reshape(-1)
            local_rhs = jnp.dot(gather_local, tiles, precision=highest)
        rhs = all_sum(local_rhs).reshape(NPANEL, PANEL) * (restrict_scale / TILE)
        ports = coarse(rhs, pivots, coupling)
        tile_values = jnp.dot(scatter_ring, ports.reshape(-1), precision=highest).reshape(own_rows + 2, own_cols + 2)
        ring = expand(expand(tile_values, True).T, True).T * prolong_scale
        centre = ring[1:-1, 1:-1]
        lifted = jnp.broadcast_to(centre[None], (local_layers, grid_rows, grid_cols))
        total = smooth(resid, weights, pad_term, inverse)
        if outer == ITERS - 1:
            drop = (lifted if drop is None else drop + lifted) + total
            break
        lifted_near = [lifted, lifted]
        for part in (ring[2:, 1:-1], ring[:-2, 1:-1], ring[1:-1, 2:], ring[1:-1, :-2]):
            lifted_near.append(jnp.broadcast_to(part[None], (local_layers, grid_rows, grid_cols)))
        total_near = neighbours(total, exchange(total))
        if drop is None:
            drop = lifted + total
            drop_near = [a + b for a, b in zip(lifted_near, total_near)]
        else:
            drop = drop + lifted + total
            drop_near = [(d + a) + b for d, a, b in zip(drop_near, lifted_near, total_near)]
    drop = lax.all_to_all(drop, "layer", 0, 1, tiled=True)
    return (drop, ports)


def solution(mesh):
    placed = (
        P("layer", "row", "col"),
        P("layer", "row", "col"),
        P("layer", "row", "col"),
        P("layer", "row", "col"),
        P("row", "col"),
        P(),
        P(None, "col", None),
        P(None, "col", None),
    )
    return jax.shard_map(
        shards,
        mesh=mesh,
        in_specs=placed,
        out_specs=(P("layer", "row", "col"), P()),
        check_vma=False,
    )
```

```python
import jax
import jax.numpy as jnp
from jax import lax
from jax.sharding import PartitionSpec as P

TILE = 16
PANEL = 512
NPANEL = 4
DEG = 3
ITERS = 2


pad_gain = 8.0
bound_low = 0.1
bound_high = 1.9
restrict_scale = 0.25
prolong_scale = 0.5

highest = lax.Precision.HIGHEST
GRID_AXES = (("layer", 0), ("row", 1), ("col", 2))
ROW_AXES = ("layer", "row")


def axis_count(axis):
    names = axis if isinstance(axis, tuple) else (axis,)
    count = 1
    for name in names:
        count *= lax.axis_size(name)
    return count


def rims(field, axis, dim):
    size = field.shape[dim]
    head = lax.slice_in_dim(field, 0, 1, axis=dim)
    tail = lax.slice_in_dim(field, size - 1, size, axis=dim)
    if axis is None:
        return jnp.zeros_like(head), jnp.zeros_like(tail)
    count = axis_count(axis)
    place = list(range(count))
    if axis == ROW_AXES:
        layers, rows = lax.axis_size("layer"), lax.axis_size("row")
        place = [(b % layers) * rows + b // layers for b in range(count)]
    if count == 2:
        low = lax.axis_index(axis) == 0
        got = lax.ppermute(jnp.where(low, tail, head), axis, [(0, 1), (1, 0)])
        zero = jnp.zeros_like(got)
        return jnp.where(low, got, zero), jnp.where(low, zero, got)
    below = lax.ppermute(tail, axis, [(place[i], place[i + 1]) for i in range(count - 1)])
    above = lax.ppermute(head, axis, [(place[i + 1], place[i]) for i in range(count - 1)])
    return above, below


def neighbours(field, halo):
    out = []
    for (axis, dim), (above, below) in zip(GRID_AXES, halo):
        size = field.shape[dim]
        out.append(jnp.concatenate([lax.slice_in_dim(field, 1, size, axis=dim), above], axis=dim))
        out.append(jnp.concatenate([below, lax.slice_in_dim(field, 0, size - 1, axis=dim)], axis=dim))
    return out


def exchange(field):
    return [rims(field, axis, dim) for axis, dim in ((None, 0), (ROW_AXES, 1), ("col", 2))]


def apply_grid(field, near, weights, pad_term):
    result = pad_term * field
    for weight, other in zip(weights, near):
        result = result + weight * (field - other)
    return result


def smooth(resid, weights, pad_term, inverse):
    theta = (bound_high + bound_low) / 2.0
    delta = (bound_high - bound_low) / 2.0
    sigma = theta / delta
    rho = 1.0 / sigma
    change = inverse * resid / theta
    total = change
    for sweep in range(DEG - 1):
        remain = resid - apply_grid(total, neighbours(total, exchange(total)), weights, pad_term)
        rho_new = 1.0 / (2.0 * sigma - rho)
        change = rho_new * rho * change + 2.0 * rho_new / delta * inverse * remain
        total = total + change
        rho = rho_new
    return total


def all_sum(value):
    for axis, _ in GRID_AXES:
        count = lax.axis_size(axis)
        if count & (count - 1):
            value = lax.psum(value, axis)
            continue
        step = 1
        while step < count:
            value = value + lax.ppermute(value, axis, [(i, i ^ step) for i in range(count)])
            step *= 2
    return value


def swap_col(value):
    return lax.ppermute(value, "col", [(0, 1), (1, 0)])


def join_halves(mine, other, low):
    return jnp.where(low, jnp.concatenate([mine, other]), jnp.concatenate([other, mine]))


def coarse_pair(rhs, pivots, coupling):
    share = pivots.shape[1]
    low = lax.axis_index("col") == 0
    start = lax.axis_index("col") * share
    own = lambda vector: lax.dynamic_slice_in_dim(vector, start, share)
    other_half = lambda vector: lax.dynamic_slice_in_dim(vector, share - start, share)
    full = rhs[0]
    forward = [full]
    for section in range(1, NPANEL):
        piece = own(rhs[section]) - jnp.dot(coupling[section - 1], full, precision=highest)
        full = join_halves(piece, swap_col(piece), low)
        forward.append(full)
    scaled = [jnp.dot(pivots[section], forward[section], precision=highest) for section in range(NPANEL)]
    mine = scaled[NPANEL - 1]
    results = [None] * NPANEL
    for section in range(NPANEL - 2, 0, -1):
        partial = jnp.dot(mine, coupling[section], precision=highest)
        got = swap_col(jnp.concatenate([other_half(partial), mine]))
        results[section + 1] = join_halves(mine, got[share:], low)
        mine = scaled[section] - (own(partial) + got[:share])
    partial = jnp.dot(mine, coupling[0], precision=highest)
    got = swap_col(jnp.concatenate([partial, scaled[0], mine]))
    results[1] = join_halves(mine, got[PANEL + share:], low)
    first = join_halves(scaled[0], got[PANEL:PANEL + share], low)
    low_part = jnp.where(low, partial, got[:PANEL])
    high_part = jnp.where(low, got[:PANEL], partial)
    results[0] = first - (low_part + high_part)
    return jnp.stack(results)


def coarse_full(rhs, pivots, coupling):
    forward = [rhs[0]]
    for section in range(1, NPANEL):
        forward.append(rhs[section] - jnp.dot(coupling[section - 1], forward[-1], precision=highest))
    scaled = [jnp.dot(pivots[section], forward[section], precision=highest) for section in range(NPANEL)]
    results = [scaled[NPANEL - 1]]
    for section in range(NPANEL - 2, -1, -1):
        results.insert(0, scaled[section] - jnp.dot(results[0], coupling[section], precision=highest))
    return jnp.stack(results)


def coarse_general(rhs, pivots, coupling):
    share = pivots.shape[1]
    start = lax.axis_index("col") * share
    full = rhs[0]
    forward = [full]
    for section in range(1, NPANEL):
        piece = lax.dynamic_slice_in_dim(rhs[section], start, share) - jnp.dot(
            coupling[section - 1], full, precision=highest
        )
        full = lax.all_gather(piece, "col", axis=0, tiled=True)
        forward.append(full)
    scaled = [jnp.dot(pivots[section], forward[section], precision=highest) for section in range(NPANEL)]
    results = [None] * NPANEL
    for section in range(NPANEL - 1, -1, -1):
        placed = lax.dynamic_update_slice_in_dim(jnp.zeros((PANEL,), jnp.float32), scaled[section], start, 0)
        if section < NPANEL - 1:
            later_rows = lax.dynamic_slice_in_dim(results[section + 1], start, share)
            placed = placed - jnp.dot(later_rows, coupling[section], precision=highest)
        results[section] = lax.psum(placed, "col")
    return jnp.stack(results)


def expand(values, edge):
    inner = values[1:-1] if edge else values
    body = jnp.repeat(inner, TILE, axis=0)
    if edge:
        body = jnp.concatenate([values[:1], body, values[-1:]], axis=0)
    return body


def shards(sources, conduct, via_cond, via_map, pad_map, port_tile, pivots, coupling):
    layer_count = lax.axis_size("layer")
    vertical = via_cond * via_map.astype(jnp.float32)
    packed = lax.all_to_all(jnp.stack((sources, conduct, vertical)), "layer", 2, 1, tiled=True)
    sources, conduct, vertical = packed[0], packed[1], packed[2]
    local_layers, grid_rows, grid_cols = sources.shape
    pad_rows = lax.dynamic_slice_in_dim(pad_map, lax.axis_index("layer") * grid_rows, grid_rows, 0)
    row_halo = rims(conduct, ROW_AXES, 1)
    col_halo = rims(conduct, "col", 2)
    layer_halo = rims(vertical, None, 0)
    near_vert = neighbours(vertical, [layer_halo, row_halo, col_halo])
    near_plane = neighbours(conduct, [layer_halo, row_halo, col_halo])
    weights = (
        jnp.sqrt(vertical * near_vert[0]),
        jnp.sqrt(vertical * near_vert[1]),
        jnp.sqrt(conduct * near_plane[2]),
        jnp.sqrt(conduct * near_plane[3]),
        jnp.sqrt(conduct * near_plane[4]),
        jnp.sqrt(conduct * near_plane[5]),
    )
    top_layer = pad_gain * pad_rows.astype(jnp.float32)
    pad_term = jnp.concatenate(
        (jnp.zeros((local_layers - 1, grid_rows, grid_cols), jnp.float32), top_layer[None]), 0
    )
    diagonal = pad_term
    for weight in weights:
        diagonal = diagonal + weight
    inverse = 1.0 / diagonal

    col_count = lax.axis_size("col")
    tile_cols = grid_cols * col_count // TILE
    tile_rows = grid_rows * axis_count(ROW_AXES) // TILE
    own_rows = grid_rows // TILE
    own_cols = grid_cols // TILE
    first_row = (lax.axis_index("row") * layer_count + lax.axis_index("layer")) * own_rows
    first_col = lax.axis_index("col") * own_cols
    flat_tiles = port_tile.reshape(-1)
    local_ids = (
        (first_row + jnp.arange(own_rows, dtype=jnp.int32))[:, None] * tile_cols
        + (first_col + jnp.arange(own_cols, dtype=jnp.int32))[None, :]
    ).reshape(-1)
    gather_local = (flat_tiles[:, None] == local_ids[None, :]).astype(jnp.float32)
    ring_rows = first_row - 1 + jnp.arange(own_rows + 2, dtype=jnp.int32)
    ring_cols = first_col - 1 + jnp.arange(own_cols + 2, dtype=jnp.int32)
    ring_ok = ((ring_rows >= 0) & (ring_rows < tile_rows))[:, None] & ((ring_cols >= 0) & (ring_cols < tile_cols))[None, :]
    ring_ids = jnp.where(ring_ok, ring_rows[:, None] * tile_cols + ring_cols[None, :], -1).reshape(-1)
    scatter_ring = (ring_ids[:, None] == flat_tiles[None, :]).astype(jnp.float32)
    coarse = coarse_pair if col_count == 2 else coarse_general
    if col_count == 2:
        low = lax.axis_index("col") == 0
        got = swap_col(jnp.concatenate([pivots, coupling]))
        mine = jnp.concatenate([pivots, coupling])
        whole = jnp.where(low, jnp.concatenate([mine, got], 1), jnp.concatenate([got, mine], 1))
        whole_pivots, whole_coupling = whole[:NPANEL], whole[NPANEL:]

    drop = None
    drop_near = None
    for outer in range(ITERS):
        if drop is None:
            resid = sources
        else:
            resid = sources - apply_grid(drop, drop_near, weights, pad_term)
        plane = jnp.sum(resid, axis=0)
        tiles = plane.reshape(own_rows, TILE, own_cols, TILE).sum(axis=(1, 3)).reshape(-1)
        local_rhs = jnp.dot(gather_local, tiles, precision=highest)
        rhs = all_sum(local_rhs).reshape(NPANEL, PANEL) * (restrict_scale / TILE)
        if col_count == 2 and outer > 0:
            ports = coarse_full(rhs, whole_pivots, whole_coupling)
        else:
            ports = coarse(rhs, pivots, coupling)
        tile_values = jnp.dot(scatter_ring, ports.reshape(-1), precision=highest).reshape(own_rows + 2, own_cols + 2)
        ring = expand(expand(tile_values, True).T, True).T * prolong_scale
        centre = ring[1:-1, 1:-1]
        lifted = jnp.broadcast_to(centre[None], (local_layers, grid_rows, grid_cols))
        total = smooth(resid, weights, pad_term, inverse)
        if outer == ITERS - 1:
            drop = (lifted if drop is None else drop + lifted) + total
            break
        lifted_near = [lifted, lifted]
        for part in (ring[2:, 1:-1], ring[:-2, 1:-1], ring[1:-1, 2:], ring[1:-1, :-2]):
            lifted_near.append(jnp.broadcast_to(part[None], (local_layers, grid_rows, grid_cols)))
        total_near = neighbours(total, exchange(total))
        if drop is None:
            drop = lifted + total
            drop_near = [a + b for a, b in zip(lifted_near, total_near)]
        else:
            drop = drop + lifted + total
            drop_near = [(d + a) + b for d, a, b in zip(drop_near, lifted_near, total_near)]
    drop = lax.all_to_all(drop, "layer", 0, 1, tiled=True)
    return (drop, ports)


def solution(mesh):
    placed = (
        P("layer", "row", "col"),
        P("layer", "row", "col"),
        P("layer", "row", "col"),
        P("layer", "row", "col"),
        P("row", "col"),
        P(),
        P(None, "col", None),
        P(None, "col", None),
    )
    return jax.shard_map(
        shards,
        mesh=mesh,
        in_specs=placed,
        out_specs=(P("layer", "row", "col"), P()),
        check_vma=False,
    )
```

```python
import jax
import numpy as np
import jax.numpy as jnp
from jax import lax
from jax.sharding import PartitionSpec as P

TILE = 16
PANEL = 512
NPANEL = 4
DEG = 3
ITERS = 2


pad_gain = 8.0
bound_low = 0.1
bound_high = 1.9
restrict_scale = 0.25
prolong_scale = 0.5

highest = lax.Precision.HIGHEST
GRID_AXES = (("layer", 0), ("row", 1), ("col", 2))
ROW_AXES = ("layer", "row")


def axis_count(axis):
    names = axis if isinstance(axis, tuple) else (axis,)
    count = 1
    for name in names:
        count *= lax.axis_size(name)
    return count


def rims(field, axis, dim):
    size = field.shape[dim]
    head = lax.slice_in_dim(field, 0, 1, axis=dim)
    tail = lax.slice_in_dim(field, size - 1, size, axis=dim)
    if axis is None:
        return jnp.zeros_like(head), jnp.zeros_like(tail)
    count = axis_count(axis)
    place = list(range(count))
    if axis == ROW_AXES:
        layers, rows = lax.axis_size("layer"), lax.axis_size("row")
        place = [(b % layers) * rows + b // layers for b in range(count)]
    if count == 2:
        low = lax.axis_index(axis) == 0
        got = lax.ppermute(jnp.where(low, tail, head), axis, [(0, 1), (1, 0)])
        zero = jnp.zeros_like(got)
        return jnp.where(low, got, zero), jnp.where(low, zero, got)
    below = lax.ppermute(tail, axis, [(place[i], place[i + 1]) for i in range(count - 1)])
    above = lax.ppermute(head, axis, [(place[i + 1], place[i]) for i in range(count - 1)])
    return above, below


def neighbours(field, halo):
    out = []
    for (axis, dim), (above, below) in zip(GRID_AXES, halo):
        size = field.shape[dim]
        out.append(jnp.concatenate([lax.slice_in_dim(field, 1, size, axis=dim), above], axis=dim))
        out.append(jnp.concatenate([below, lax.slice_in_dim(field, 0, size - 1, axis=dim)], axis=dim))
    return out


def exchange(field):
    return [rims(field, axis, dim) for axis, dim in ((None, 0), (ROW_AXES, 1), ("col", 2))]


def apply_grid(field, near, weights, pad_term):
    result = pad_term * field
    for weight, other in zip(weights, near):
        result = result + weight * (field - other)
    return result


def smooth(resid, weights, pad_term, inverse):
    theta = (bound_high + bound_low) / 2.0
    delta = (bound_high - bound_low) / 2.0
    sigma = theta / delta
    rho = 1.0 / sigma
    change = inverse * resid / theta
    total = change
    for sweep in range(DEG - 1):
        remain = resid - apply_grid(total, neighbours(total, exchange(total)), weights, pad_term)
        rho_new = 1.0 / (2.0 * sigma - rho)
        change = rho_new * rho * change + 2.0 * rho_new / delta * inverse * remain
        total = total + change
        rho = rho_new
    return total


def all_sum(value):
    for axis, _ in GRID_AXES:
        count = lax.axis_size(axis)
        if count & (count - 1):
            value = lax.psum(value, axis)
            continue
        step = 1
        while step < count:
            value = value + lax.ppermute(value, axis, [(i, i ^ step) for i in range(count)])
            step *= 2
    return value


def share_tiles(tiles, own_rows, own_cols):
    layers, rows, cols = (lax.axis_size(axis) for axis, _ in GRID_AXES)
    count = layers * rows * cols
    payload = jnp.broadcast_to(tiles.reshape(1, -1), (count, tiles.size))
    got = lax.all_to_all(payload, ("layer", "row", "col"), 0, 0, tiled=True).reshape(-1)
    tile_cols = cols * own_cols
    where = np.zeros(count * tiles.size, np.int32)
    for l in range(layers):
        for r in range(rows):
            for c in range(cols):
                d = (l * rows + r) * cols + c
                for jr in range(own_rows):
                    for jc in range(own_cols):
                        tile = ((r * layers + l) * own_rows + jr) * tile_cols + c * own_cols + jc
                        where[tile] = d * tiles.size + jr * own_cols + jc
    return got, where


def swap_col(value):
    return lax.ppermute(value, "col", [(0, 1), (1, 0)])


def join_halves(mine, other, low):
    return jnp.where(low, jnp.concatenate([mine, other]), jnp.concatenate([other, mine]))


def coarse_pair(rhs, pivots, coupling):
    share = pivots.shape[1]
    low = lax.axis_index("col") == 0
    start = lax.axis_index("col") * share
    own = lambda vector: lax.dynamic_slice_in_dim(vector, start, share)
    other_half = lambda vector: lax.dynamic_slice_in_dim(vector, share - start, share)
    full = rhs[0]
    forward = [full]
    for section in range(1, NPANEL):
        piece = own(rhs[section]) - jnp.dot(coupling[section - 1], full, precision=highest)
        full = join_halves(piece, swap_col(piece), low)
        forward.append(full)
    scaled = [jnp.dot(pivots[section], forward[section], precision=highest) for section in range(NPANEL)]
    mine = scaled[NPANEL - 1]
    results = [None] * NPANEL
    for section in range(NPANEL - 2, 0, -1):
        partial = jnp.dot(mine, coupling[section], precision=highest)
        got = swap_col(jnp.concatenate([other_half(partial), mine]))
        results[section + 1] = join_halves(mine, got[share:], low)
        mine = scaled[section] - (own(partial) + got[:share])
    partial = jnp.dot(mine, coupling[0], precision=highest)
    got = swap_col(jnp.concatenate([partial, scaled[0], mine]))
    results[1] = join_halves(mine, got[PANEL + share:], low)
    first = join_halves(scaled[0], got[PANEL:PANEL + share], low)
    low_part = jnp.where(low, partial, got[:PANEL])
    high_part = jnp.where(low, got[:PANEL], partial)
    results[0] = first - (low_part + high_part)
    return jnp.stack(results)


def coarse_general(rhs, pivots, coupling):
    share = pivots.shape[1]
    start = lax.axis_index("col") * share
    full = rhs[0]
    forward = [full]
    for section in range(1, NPANEL):
        piece = lax.dynamic_slice_in_dim(rhs[section], start, share) - jnp.dot(
            coupling[section - 1], full, precision=highest
        )
        full = lax.all_gather(piece, "col", axis=0, tiled=True)
        forward.append(full)
    scaled = [jnp.dot(pivots[section], forward[section], precision=highest) for section in range(NPANEL)]
    results = [None] * NPANEL
    for section in range(NPANEL - 1, -1, -1):
        placed = lax.dynamic_update_slice_in_dim(jnp.zeros((PANEL,), jnp.float32), scaled[section], start, 0)
        if section < NPANEL - 1:
            later_rows = lax.dynamic_slice_in_dim(results[section + 1], start, share)
            placed = placed - jnp.dot(later_rows, coupling[section], precision=highest)
        results[section] = lax.psum(placed, "col")
    return jnp.stack(results)


def expand(values, edge):
    inner = values[1:-1] if edge else values
    body = jnp.repeat(inner, TILE, axis=0)
    if edge:
        body = jnp.concatenate([values[:1], body, values[-1:]], axis=0)
    return body


def shards(sources, conduct, via_cond, via_map, pad_map, port_tile, pivots, coupling):
    layer_count = lax.axis_size("layer")
    vertical = via_cond * via_map.astype(jnp.float32)
    packed = lax.all_to_all(jnp.stack((sources, conduct, vertical)), "layer", 2, 1, tiled=True)
    sources, conduct, vertical = packed[0], packed[1], packed[2]
    local_layers, grid_rows, grid_cols = sources.shape
    pad_rows = lax.dynamic_slice_in_dim(pad_map, lax.axis_index("layer") * grid_rows, grid_rows, 0)
    row_halo = rims(conduct, ROW_AXES, 1)
    col_halo = rims(conduct, "col", 2)
    layer_halo = rims(vertical, None, 0)
    near_vert = neighbours(vertical, [layer_halo, row_halo, col_halo])
    near_plane = neighbours(conduct, [layer_halo, row_halo, col_halo])
    weights = (
        jnp.sqrt(vertical * near_vert[0]),
        jnp.sqrt(vertical * near_vert[1]),
        jnp.sqrt(conduct * near_plane[2]),
        jnp.sqrt(conduct * near_plane[3]),
        jnp.sqrt(conduct * near_plane[4]),
        jnp.sqrt(conduct * near_plane[5]),
    )
    top_layer = pad_gain * pad_rows.astype(jnp.float32)
    pad_term = jnp.concatenate(
        (jnp.zeros((local_layers - 1, grid_rows, grid_cols), jnp.float32), top_layer[None]), 0
    )
    diagonal = pad_term
    for weight in weights:
        diagonal = diagonal + weight
    inverse = 1.0 / diagonal

    col_count = lax.axis_size("col")
    tile_cols = grid_cols * col_count // TILE
    tile_rows = grid_rows * axis_count(ROW_AXES) // TILE
    own_rows = grid_rows // TILE
    own_cols = grid_cols // TILE
    first_row = (lax.axis_index("row") * layer_count + lax.axis_index("layer")) * own_rows
    first_col = lax.axis_index("col") * own_cols
    flat_tiles = port_tile.reshape(-1)
    ring_rows = first_row - 1 + jnp.arange(own_rows + 2, dtype=jnp.int32)
    ring_cols = first_col - 1 + jnp.arange(own_cols + 2, dtype=jnp.int32)
    ring_ok = ((ring_rows >= 0) & (ring_rows < tile_rows))[:, None] & ((ring_cols >= 0) & (ring_cols < tile_cols))[None, :]
    ring_ids = jnp.where(ring_ok, ring_rows[:, None] * tile_cols + ring_cols[None, :], -1).reshape(-1)
    scatter_ring = (ring_ids[:, None] == flat_tiles[None, :]).astype(jnp.float32)
    coarse = coarse_pair if col_count == 2 else coarse_general

    drop = None
    drop_near = None
    for outer in range(ITERS):
        if drop is None:
            resid = sources
        else:
            resid = sources - apply_grid(drop, drop_near, weights, pad_term)
        plane = jnp.sum(resid, axis=0)
        tiles = plane.reshape(own_rows, TILE, own_cols, TILE).sum(axis=(1, 3)).reshape(-1)
        got, where = share_tiles(tiles, own_rows, own_cols)
        rhs = got[jnp.asarray(where)[flat_tiles]].reshape(NPANEL, PANEL) * (restrict_scale / TILE)
        ports = coarse(rhs, pivots, coupling)
        tile_values = jnp.dot(scatter_ring, ports.reshape(-1), precision=highest).reshape(own_rows + 2, own_cols + 2)
        ring = expand(expand(tile_values, True).T, True).T * prolong_scale
        centre = ring[1:-1, 1:-1]
        lifted = jnp.broadcast_to(centre[None], (local_layers, grid_rows, grid_cols))
        total = smooth(resid, weights, pad_term, inverse)
        if outer == ITERS - 1:
            drop = (lifted if drop is None else drop + lifted) + total
            break
        lifted_near = [lifted, lifted]
        for part in (ring[2:, 1:-1], ring[:-2, 1:-1], ring[1:-1, 2:], ring[1:-1, :-2]):
            lifted_near.append(jnp.broadcast_to(part[None], (local_layers, grid_rows, grid_cols)))
        total_near = neighbours(total, exchange(total))
        if drop is None:
            drop = lifted + total
            drop_near = [a + b for a, b in zip(lifted_near, total_near)]
        else:
            drop = drop + lifted + total
            drop_near = [(d + a) + b for d, a, b in zip(drop_near, lifted_near, total_near)]
    drop = lax.all_to_all(drop, "layer", 0, 1, tiled=True)
    return (drop, ports)


def solution(mesh):
    placed = (
        P("layer", "row", "col"),
        P("layer", "row", "col"),
        P("layer", "row", "col"),
        P("layer", "row", "col"),
        P("row", "col"),
        P(),
        P(None, "col", None),
        P(None, "col", None),
    )
    return jax.shard_map(
        shards,
        mesh=mesh,
        in_specs=placed,
        out_specs=(P("layer", "row", "col"), P()),
        check_vma=False,
    )
```

```python
import jax
import jax.numpy as jnp
from jax import lax
from jax.sharding import PartitionSpec as P

TILE = 16
PANEL = 512
NPANEL = 4
DEG = 3
ITERS = 2


pad_gain = 8.0
bound_low = 0.1
bound_high = 1.9
restrict_scale = 0.25
prolong_scale = 0.5

highest = lax.Precision.HIGHEST
GRID_AXES = (("layer", 0), ("row", 1), ("col", 2))
ROW_AXES = ("layer", "row")


def axis_count(axis):
    names = axis if isinstance(axis, tuple) else (axis,)
    count = 1
    for name in names:
        count *= lax.axis_size(name)
    return count


def rims(field, axis, dim):
    size = field.shape[dim]
    head = lax.slice_in_dim(field, 0, 1, axis=dim)
    tail = lax.slice_in_dim(field, size - 1, size, axis=dim)
    if axis is None:
        return jnp.zeros_like(head), jnp.zeros_like(tail)
    count = axis_count(axis)
    place = list(range(count))
    if axis == ROW_AXES:
        layers, rows = lax.axis_size("layer"), lax.axis_size("row")
        place = [(b % layers) * rows + b // layers for b in range(count)]
    if count == 2:
        low = lax.axis_index(axis) == 0
        got = lax.ppermute(jnp.where(low, tail, head), axis, [(0, 1), (1, 0)])
        zero = jnp.zeros_like(got)
        return jnp.where(low, got, zero), jnp.where(low, zero, got)
    below = lax.ppermute(tail, axis, [(place[i], place[i + 1]) for i in range(count - 1)])
    above = lax.ppermute(head, axis, [(place[i + 1], place[i]) for i in range(count - 1)])
    return above, below


def neighbours(field, halo):
    out = []
    for (axis, dim), (above, below) in zip(GRID_AXES, halo):
        size = field.shape[dim]
        out.append(jnp.concatenate([lax.slice_in_dim(field, 1, size, axis=dim), above], axis=dim))
        out.append(jnp.concatenate([below, lax.slice_in_dim(field, 0, size - 1, axis=dim)], axis=dim))
    return out


def exchange(field):
    return [rims(field, axis, dim) for axis, dim in ((None, 0), (ROW_AXES, 1), ("col", 2))]


def apply_grid(field, near, weights, pad_term):
    result = pad_term * field
    for weight, other in zip(weights, near):
        result = result + weight * (field - other)
    return result


def smooth(resid, weights, pad_term, inverse):
    theta = (bound_high + bound_low) / 2.0
    delta = (bound_high - bound_low) / 2.0
    sigma = theta / delta
    rho = 1.0 / sigma
    change = inverse * resid / theta
    total = change
    for sweep in range(DEG - 1):
        remain = resid - apply_grid(total, neighbours(total, exchange(total)), weights, pad_term)
        rho_new = 1.0 / (2.0 * sigma - rho)
        change = rho_new * rho * change + 2.0 * rho_new / delta * inverse * remain
        total = total + change
        rho = rho_new
    return total


def all_sum(value):
    for axis, _ in GRID_AXES:
        count = lax.axis_size(axis)
        if count & (count - 1):
            value = lax.psum(value, axis)
            continue
        step = 1
        while step < count:
            value = value + lax.ppermute(value, axis, [(i, i ^ step) for i in range(count)])
            step *= 2
    return value


def share_tiles(tiles, own_rows, own_cols, flat_tiles):
    layers, rows, cols = (lax.axis_size(axis) for axis, _ in GRID_AXES)
    count = layers * rows * cols
    payload = jnp.broadcast_to(tiles.reshape(1, -1), (count, tiles.size))
    got = lax.all_to_all(payload, ("layer", "row", "col"), 0, 0, tiled=True)
    tile_cols = cols * own_cols
    tile_row, tile_col = flat_tiles // tile_cols, flat_tiles % tile_cols
    block = tile_row // own_rows
    device = ((block % layers) * rows + block // layers) * cols + tile_col // own_cols
    slot = (tile_row % own_rows) * own_cols + tile_col % own_cols
    pick_device = (device[:, None] == jnp.arange(count, dtype=jnp.int32)[None, :]).astype(jnp.float32)
    pick_slot = (slot[:, None] == jnp.arange(tiles.size, dtype=jnp.int32)[None, :]).astype(jnp.float32)
    return jnp.sum(jnp.dot(pick_device, got, precision=highest) * pick_slot, axis=1)


def swap_col(value):
    return lax.ppermute(value, "col", [(0, 1), (1, 0)])


def join_halves(mine, other, low):
    return jnp.where(low, jnp.concatenate([mine, other]), jnp.concatenate([other, mine]))


def coarse_pair(rhs, pivots, coupling):
    share = pivots.shape[1]
    low = lax.axis_index("col") == 0
    start = lax.axis_index("col") * share
    own = lambda vector: lax.dynamic_slice_in_dim(vector, start, share)
    other_half = lambda vector: lax.dynamic_slice_in_dim(vector, share - start, share)
    full = rhs[0]
    forward = [full]
    for section in range(1, NPANEL):
        piece = own(rhs[section]) - jnp.dot(coupling[section - 1], full, precision=highest)
        full = join_halves(piece, swap_col(piece), low)
        forward.append(full)
    scaled = [jnp.dot(pivots[section], forward[section], precision=highest) for section in range(NPANEL)]
    mine = scaled[NPANEL - 1]
    results = [None] * NPANEL
    for section in range(NPANEL - 2, 0, -1):
        partial = jnp.dot(mine, coupling[section], precision=highest)
        got = swap_col(jnp.concatenate([other_half(partial), mine]))
        results[section + 1] = join_halves(mine, got[share:], low)
        mine = scaled[section] - (own(partial) + got[:share])
    partial = jnp.dot(mine, coupling[0], precision=highest)
    got = swap_col(jnp.concatenate([partial, scaled[0], mine]))
    results[1] = join_halves(mine, got[PANEL + share:], low)
    first = join_halves(scaled[0], got[PANEL:PANEL + share], low)
    low_part = jnp.where(low, partial, got[:PANEL])
    high_part = jnp.where(low, got[:PANEL], partial)
    results[0] = first - (low_part + high_part)
    return jnp.stack(results)


def coarse_general(rhs, pivots, coupling):
    share = pivots.shape[1]
    start = lax.axis_index("col") * share
    full = rhs[0]
    forward = [full]
    for section in range(1, NPANEL):
        piece = lax.dynamic_slice_in_dim(rhs[section], start, share) - jnp.dot(
            coupling[section - 1], full, precision=highest
        )
        full = lax.all_gather(piece, "col", axis=0, tiled=True)
        forward.append(full)
    scaled = [jnp.dot(pivots[section], forward[section], precision=highest) for section in range(NPANEL)]
    results = [None] * NPANEL
    for section in range(NPANEL - 1, -1, -1):
        placed = lax.dynamic_update_slice_in_dim(jnp.zeros((PANEL,), jnp.float32), scaled[section], start, 0)
        if section < NPANEL - 1:
            later_rows = lax.dynamic_slice_in_dim(results[section + 1], start, share)
            placed = placed - jnp.dot(later_rows, coupling[section], precision=highest)
        results[section] = lax.psum(placed, "col")
    return jnp.stack(results)


def expand(values, edge):
    inner = values[1:-1] if edge else values
    body = jnp.repeat(inner, TILE, axis=0)
    if edge:
        body = jnp.concatenate([values[:1], body, values[-1:]], axis=0)
    return body


def shards(sources, conduct, via_cond, via_map, pad_map, port_tile, pivots, coupling):
    layer_count = lax.axis_size("layer")
    vertical = via_cond * via_map.astype(jnp.float32)
    packed = lax.all_to_all(jnp.stack((sources, conduct, vertical)), "layer", 2, 1, tiled=True)
    sources, conduct, vertical = packed[0], packed[1], packed[2]
    local_layers, grid_rows, grid_cols = sources.shape
    pad_rows = lax.dynamic_slice_in_dim(pad_map, lax.axis_index("layer") * grid_rows, grid_rows, 0)
    row_halo = rims(conduct, ROW_AXES, 1)
    col_halo = rims(conduct, "col", 2)
    layer_halo = rims(vertical, None, 0)
    near_vert = neighbours(vertical, [layer_halo, row_halo, col_halo])
    near_plane = neighbours(conduct, [layer_halo, row_halo, col_halo])
    weights = (
        jnp.sqrt(vertical * near_vert[0]),
        jnp.sqrt(vertical * near_vert[1]),
        jnp.sqrt(conduct * near_plane[2]),
        jnp.sqrt(conduct * near_plane[3]),
        jnp.sqrt(conduct * near_plane[4]),
        jnp.sqrt(conduct * near_plane[5]),
    )
    top_layer = pad_gain * pad_rows.astype(jnp.float32)
    pad_term = jnp.concatenate(
        (jnp.zeros((local_layers - 1, grid_rows, grid_cols), jnp.float32), top_layer[None]), 0
    )
    diagonal = pad_term
    for weight in weights:
        diagonal = diagonal + weight
    inverse = 1.0 / diagonal

    col_count = lax.axis_size("col")
    tile_cols = grid_cols * col_count // TILE
    tile_rows = grid_rows * axis_count(ROW_AXES) // TILE
    own_rows = grid_rows // TILE
    own_cols = grid_cols // TILE
    first_row = (lax.axis_index("row") * layer_count + lax.axis_index("layer")) * own_rows
    first_col = lax.axis_index("col") * own_cols
    flat_tiles = port_tile.reshape(-1)
    ring_rows = first_row - 1 + jnp.arange(own_rows + 2, dtype=jnp.int32)
    ring_cols = first_col - 1 + jnp.arange(own_cols + 2, dtype=jnp.int32)
    ring_ok = ((ring_rows >= 0) & (ring_rows < tile_rows))[:, None] & ((ring_cols >= 0) & (ring_cols < tile_cols))[None, :]
    ring_ids = jnp.where(ring_ok, ring_rows[:, None] * tile_cols + ring_cols[None, :], -1).reshape(-1)
    scatter_ring = (ring_ids[:, None] == flat_tiles[None, :]).astype(jnp.float32)
    coarse = coarse_pair if col_count == 2 else coarse_general

    drop = None
    drop_near = None
    for outer in range(ITERS):
        if drop is None:
            resid = sources
        else:
            resid = sources - apply_grid(drop, drop_near, weights, pad_term)
        plane = jnp.sum(resid, axis=0)
        tiles = plane.reshape(own_rows, TILE, own_cols, TILE).sum(axis=(1, 3)).reshape(-1)
        rhs = share_tiles(tiles, own_rows, own_cols, flat_tiles).reshape(NPANEL, PANEL) * (restrict_scale / TILE)
        ports = coarse(rhs, pivots, coupling)
        tile_values = jnp.dot(scatter_ring, ports.reshape(-1), precision=highest).reshape(own_rows + 2, own_cols + 2)
        ring = expand(expand(tile_values, True).T, True).T * prolong_scale
        centre = ring[1:-1, 1:-1]
        lifted = jnp.broadcast_to(centre[None], (local_layers, grid_rows, grid_cols))
        total = smooth(resid, weights, pad_term, inverse)
        if outer == ITERS - 1:
            drop = (lifted if drop is None else drop + lifted) + total
            break
        lifted_near = [lifted, lifted]
        for part in (ring[2:, 1:-1], ring[:-2, 1:-1], ring[1:-1, 2:], ring[1:-1, :-2]):
            lifted_near.append(jnp.broadcast_to(part[None], (local_layers, grid_rows, grid_cols)))
        total_near = neighbours(total, exchange(total))
        if drop is None:
            drop = lifted + total
            drop_near = [a + b for a, b in zip(lifted_near, total_near)]
        else:
            drop = drop + lifted + total
            drop_near = [(d + a) + b for d, a, b in zip(drop_near, lifted_near, total_near)]
    drop = lax.all_to_all(drop, "layer", 0, 1, tiled=True)
    return (drop, ports)


def solution(mesh):
    placed = (
        P("layer", "row", "col"),
        P("layer", "row", "col"),
        P("layer", "row", "col"),
        P("layer", "row", "col"),
        P("row", "col"),
        P(),
        P(None, "col", None),
        P(None, "col", None),
    )
    return jax.shard_map(
        shards,
        mesh=mesh,
        in_specs=placed,
        out_specs=(P("layer", "row", "col"), P()),
        check_vma=False,
    )
```

```python
import jax
import jax.numpy as jnp
from jax import lax
from jax.sharding import PartitionSpec as P

TILE = 16
PANEL = 512
NPANEL = 4
DEG = 3
ITERS = 2


pad_gain = 8.0
bound_low = 0.1
bound_high = 1.9
restrict_scale = 0.25
prolong_scale = 0.5

highest = lax.Precision.HIGHEST
GRID_AXES = (("layer", 0), ("row", 1), ("col", 2))
ROW_AXES = ("layer", "row")


def axis_count(axis):
    names = axis if isinstance(axis, tuple) else (axis,)
    count = 1
    for name in names:
        count *= lax.axis_size(name)
    return count


def rims(field, axis, dim):
    size = field.shape[dim]
    head = lax.slice_in_dim(field, 0, 1, axis=dim)
    tail = lax.slice_in_dim(field, size - 1, size, axis=dim)
    if axis is None:
        return jnp.zeros_like(head), jnp.zeros_like(tail)
    count = axis_count(axis)
    place = list(range(count))
    if axis == ROW_AXES:
        layers, rows = lax.axis_size("layer"), lax.axis_size("row")
        place = [(b % layers) * rows + b // layers for b in range(count)]
    if count == 2:
        low = lax.axis_index(axis) == 0
        got = lax.ppermute(jnp.where(low, tail, head), axis, [(0, 1), (1, 0)])
        zero = jnp.zeros_like(got)
        return jnp.where(low, got, zero), jnp.where(low, zero, got)
    below = lax.ppermute(tail, axis, [(place[i], place[i + 1]) for i in range(count - 1)])
    above = lax.ppermute(head, axis, [(place[i + 1], place[i]) for i in range(count - 1)])
    return above, below


def neighbours(field, halo):
    out = []
    for (axis, dim), (above, below) in zip(GRID_AXES, halo):
        size = field.shape[dim]
        out.append(jnp.concatenate([lax.slice_in_dim(field, 1, size, axis=dim), above], axis=dim))
        out.append(jnp.concatenate([below, lax.slice_in_dim(field, 0, size - 1, axis=dim)], axis=dim))
    return out


def exchange(field):
    return [rims(field, axis, dim) for axis, dim in ((None, 0), (ROW_AXES, 1), ("col", 2))]


def apply_grid(field, near, weights, pad_term):
    result = pad_term * field
    for weight, other in zip(weights, near):
        result = result + weight * (field - other)
    return result


def smooth(resid, weights, pad_term, inverse):
    theta = (bound_high + bound_low) / 2.0
    delta = (bound_high - bound_low) / 2.0
    sigma = theta / delta
    rho = 1.0 / sigma
    change = inverse * resid / theta
    total = change
    for sweep in range(DEG - 1):
        remain = resid - apply_grid(total, neighbours(total, exchange(total)), weights, pad_term)
        rho_new = 1.0 / (2.0 * sigma - rho)
        change = rho_new * rho * change + 2.0 * rho_new / delta * inverse * remain
        total = total + change
        rho = rho_new
    return total


def col_face(field):
    low = lax.axis_index("col") == 0
    return jnp.where(low, field[:, :, -1:], field[:, :, :1]).reshape(-1)


def col_halo(field, got):
    low = lax.axis_index("col") == 0
    got = got.reshape(field.shape[0], field.shape[1], 1)
    zero = jnp.zeros_like(got)
    return jnp.where(low, got, zero), jnp.where(low, zero, got)


def smooth_riding(resid, weights, pad_term, inverse, out, halo_after):
    theta = (bound_high + bound_low) / 2.0
    delta = (bound_high - bound_low) / 2.0
    sigma = theta / delta
    rho = 1.0 / sigma
    change = inverse * resid / theta
    total = change
    for sweep in range(DEG - 1):
        got = yield col_face(total)
        halo = [rims(total, None, 0), rims(total, ROW_AXES, 1), col_halo(total, got)]
        remain = resid - apply_grid(total, neighbours(total, halo), weights, pad_term)
        rho_new = 1.0 / (2.0 * sigma - rho)
        change = rho_new * rho * change + 2.0 * rho_new / delta * inverse * remain
        total = total + change
        rho = rho_new
    out["total"] = total
    if halo_after:
        got = yield col_face(total)
        halo = [rims(total, None, 0), rims(total, ROW_AXES, 1), col_halo(total, got)]
        out["near"] = neighbours(total, halo)


def all_sum(value):
    for axis, _ in GRID_AXES:
        count = lax.axis_size(axis)
        if count & (count - 1):
            value = lax.psum(value, axis)
            continue
        step = 1
        while step < count:
            value = value + lax.ppermute(value, axis, [(i, i ^ step) for i in range(count)])
            step *= 2
    return value


def share_tiles(tiles, own_rows, own_cols, flat_tiles):
    layers, rows, cols = (lax.axis_size(axis) for axis, _ in GRID_AXES)
    count = layers * rows * cols
    payload = jnp.broadcast_to(tiles.reshape(1, -1), (count, tiles.size))
    got = lax.all_to_all(payload, ("layer", "row", "col"), 0, 0, tiled=True)
    tile_cols = cols * own_cols
    tile_row, tile_col = flat_tiles // tile_cols, flat_tiles % tile_cols
    block = tile_row // own_rows
    device = ((block % layers) * rows + block // layers) * cols + tile_col // own_cols
    slot = (tile_row % own_rows) * own_cols + tile_col % own_cols
    pick_device = (device[:, None] == jnp.arange(count, dtype=jnp.int32)[None, :]).astype(jnp.float32)
    pick_slot = (slot[:, None] == jnp.arange(tiles.size, dtype=jnp.int32)[None, :]).astype(jnp.float32)
    return jnp.sum(jnp.dot(pick_device, got, precision=highest) * pick_slot, axis=1)


def swap_col(value):
    return lax.ppermute(value, "col", [(0, 1), (1, 0)])


def join_halves(mine, other, low):
    return jnp.where(low, jnp.concatenate([mine, other]), jnp.concatenate([other, mine]))


def coarse_pair(rhs, pivots, coupling, rider=None):
    carry = [rider.send(None) if rider is not None else None]

    def swap_col(value):
        extra = carry[0]
        if extra is None:
            return lax.ppermute(value, "col", [(0, 1), (1, 0)])
        got = lax.ppermute(jnp.concatenate([value, extra]), "col", [(0, 1), (1, 0)])
        try:
            carry[0] = rider.send(got[value.size:])
        except StopIteration:
            carry[0] = None
        return got[:value.size]

    share = pivots.shape[1]
    low = lax.axis_index("col") == 0
    start = lax.axis_index("col") * share
    own = lambda vector: lax.dynamic_slice_in_dim(vector, start, share)
    other_half = lambda vector: lax.dynamic_slice_in_dim(vector, share - start, share)
    full = rhs[0]
    forward = [full]
    for section in range(1, NPANEL):
        piece = own(rhs[section]) - jnp.dot(coupling[section - 1], full, precision=highest)
        full = join_halves(piece, swap_col(piece), low)
        forward.append(full)
    scaled = [jnp.dot(pivots[section], forward[section], precision=highest) for section in range(NPANEL)]
    mine = scaled[NPANEL - 1]
    results = [None] * NPANEL
    for section in range(NPANEL - 2, 0, -1):
        partial = jnp.dot(mine, coupling[section], precision=highest)
        got = swap_col(jnp.concatenate([other_half(partial), mine]))
        results[section + 1] = join_halves(mine, got[share:], low)
        mine = scaled[section] - (own(partial) + got[:share])
    partial = jnp.dot(mine, coupling[0], precision=highest)
    got = swap_col(jnp.concatenate([partial, scaled[0], mine]))
    results[1] = join_halves(mine, got[PANEL + share:], low)
    first = join_halves(scaled[0], got[PANEL:PANEL + share], low)
    low_part = jnp.where(low, partial, got[:PANEL])
    high_part = jnp.where(low, got[:PANEL], partial)
    results[0] = first - (low_part + high_part)
    return jnp.stack(results)


def coarse_general(rhs, pivots, coupling):
    share = pivots.shape[1]
    start = lax.axis_index("col") * share
    full = rhs[0]
    forward = [full]
    for section in range(1, NPANEL):
        piece = lax.dynamic_slice_in_dim(rhs[section], start, share) - jnp.dot(
            coupling[section - 1], full, precision=highest
        )
        full = lax.all_gather(piece, "col", axis=0, tiled=True)
        forward.append(full)
    scaled = [jnp.dot(pivots[section], forward[section], precision=highest) for section in range(NPANEL)]
    results = [None] * NPANEL
    for section in range(NPANEL - 1, -1, -1):
        placed = lax.dynamic_update_slice_in_dim(jnp.zeros((PANEL,), jnp.float32), scaled[section], start, 0)
        if section < NPANEL - 1:
            later_rows = lax.dynamic_slice_in_dim(results[section + 1], start, share)
            placed = placed - jnp.dot(later_rows, coupling[section], precision=highest)
        results[section] = lax.psum(placed, "col")
    return jnp.stack(results)


def expand(values, edge):
    inner = values[1:-1] if edge else values
    body = jnp.repeat(inner, TILE, axis=0)
    if edge:
        body = jnp.concatenate([values[:1], body, values[-1:]], axis=0)
    return body


def shards(sources, conduct, via_cond, via_map, pad_map, port_tile, pivots, coupling):
    layer_count = lax.axis_size("layer")
    vertical = via_cond * via_map.astype(jnp.float32)
    packed = lax.all_to_all(jnp.stack((sources, conduct, vertical)), "layer", 2, 1, tiled=True)
    sources, conduct, vertical = packed[0], packed[1], packed[2]
    local_layers, grid_rows, grid_cols = sources.shape
    pad_rows = lax.dynamic_slice_in_dim(pad_map, lax.axis_index("layer") * grid_rows, grid_rows, 0)
    row_halo = rims(conduct, ROW_AXES, 1)
    col_halo = rims(conduct, "col", 2)
    layer_halo = rims(vertical, None, 0)
    near_vert = neighbours(vertical, [layer_halo, row_halo, col_halo])
    near_plane = neighbours(conduct, [layer_halo, row_halo, col_halo])
    weights = (
        jnp.sqrt(vertical * near_vert[0]),
        jnp.sqrt(vertical * near_vert[1]),
        jnp.sqrt(conduct * near_plane[2]),
        jnp.sqrt(conduct * near_plane[3]),
        jnp.sqrt(conduct * near_plane[4]),
        jnp.sqrt(conduct * near_plane[5]),
    )
    top_layer = pad_gain * pad_rows.astype(jnp.float32)
    pad_term = jnp.concatenate(
        (jnp.zeros((local_layers - 1, grid_rows, grid_cols), jnp.float32), top_layer[None]), 0
    )
    diagonal = pad_term
    for weight in weights:
        diagonal = diagonal + weight
    inverse = 1.0 / diagonal

    col_count = lax.axis_size("col")
    tile_cols = grid_cols * col_count // TILE
    tile_rows = grid_rows * axis_count(ROW_AXES) // TILE
    own_rows = grid_rows // TILE
    own_cols = grid_cols // TILE
    first_row = (lax.axis_index("row") * layer_count + lax.axis_index("layer")) * own_rows
    first_col = lax.axis_index("col") * own_cols
    flat_tiles = port_tile.reshape(-1)
    ring_rows = first_row - 1 + jnp.arange(own_rows + 2, dtype=jnp.int32)
    ring_cols = first_col - 1 + jnp.arange(own_cols + 2, dtype=jnp.int32)
    ring_ok = ((ring_rows >= 0) & (ring_rows < tile_rows))[:, None] & ((ring_cols >= 0) & (ring_cols < tile_cols))[None, :]
    ring_ids = jnp.where(ring_ok, ring_rows[:, None] * tile_cols + ring_cols[None, :], -1).reshape(-1)
    scatter_ring = (ring_ids[:, None] == flat_tiles[None, :]).astype(jnp.float32)

    drop = None
    drop_near = None
    for outer in range(ITERS):
        if drop is None:
            resid = sources
        else:
            resid = sources - apply_grid(drop, drop_near, weights, pad_term)
        plane = jnp.sum(resid, axis=0)
        tiles = plane.reshape(own_rows, TILE, own_cols, TILE).sum(axis=(1, 3)).reshape(-1)
        rhs = share_tiles(tiles, own_rows, own_cols, flat_tiles).reshape(NPANEL, PANEL) * (restrict_scale / TILE)
        last = outer == ITERS - 1
        if col_count == 2:
            out = {}
            rider = smooth_riding(resid, weights, pad_term, inverse, out, not last)
            ports = coarse_pair(rhs, pivots, coupling, rider)
            total = out["total"]
        else:
            ports = coarse_general(rhs, pivots, coupling)
            total = smooth(resid, weights, pad_term, inverse)
        tile_values = jnp.dot(scatter_ring, ports.reshape(-1), precision=highest).reshape(own_rows + 2, own_cols + 2)
        ring = expand(expand(tile_values, True).T, True).T * prolong_scale
        centre = ring[1:-1, 1:-1]
        lifted = jnp.broadcast_to(centre[None], (local_layers, grid_rows, grid_cols))
        if last:
            drop = (lifted if drop is None else drop + lifted) + total
            break
        lifted_near = [lifted, lifted]
        for part in (ring[2:, 1:-1], ring[:-2, 1:-1], ring[1:-1, 2:], ring[1:-1, :-2]):
            lifted_near.append(jnp.broadcast_to(part[None], (local_layers, grid_rows, grid_cols)))
        total_near = out["near"] if col_count == 2 else neighbours(total, exchange(total))
        if drop is None:
            drop = lifted + total
            drop_near = [a + b for a, b in zip(lifted_near, total_near)]
        else:
            drop = drop + lifted + total
            drop_near = [(d + a) + b for d, a, b in zip(drop_near, lifted_near, total_near)]
    drop = lax.all_to_all(drop, "layer", 0, 1, tiled=True)
    return (drop, ports)


def solution(mesh):
    placed = (
        P("layer", "row", "col"),
        P("layer", "row", "col"),
        P("layer", "row", "col"),
        P("layer", "row", "col"),
        P("row", "col"),
        P(),
        P(None, "col", None),
        P(None, "col", None),
    )
    return jax.shard_map(
        shards,
        mesh=mesh,
        in_specs=placed,
        out_specs=(P("layer", "row", "col"), P()),
        check_vma=False,
    )
```

```python
import jax
import jax.numpy as jnp
from jax import lax
from jax.sharding import PartitionSpec as P

TILE = 16
PANEL = 512
NPANEL = 4
DEG = 3
ITERS = 2


pad_gain = 8.0
bound_low = 0.1
bound_high = 1.9
restrict_scale = 0.25
prolong_scale = 0.5

highest = lax.Precision.HIGHEST
GRID_AXES = (("layer", 0), ("row", 1), ("col", 2))
ROW_AXES = ("layer", "row")


def axis_count(axis):
    names = axis if isinstance(axis, tuple) else (axis,)
    count = 1
    for name in names:
        count *= lax.axis_size(name)
    return count


def rims(field, axis, dim):
    size = field.shape[dim]
    head = lax.slice_in_dim(field, 0, 1, axis=dim)
    tail = lax.slice_in_dim(field, size - 1, size, axis=dim)
    if axis is None:
        return jnp.zeros_like(head), jnp.zeros_like(tail)
    count = axis_count(axis)
    place = list(range(count))
    if axis == ROW_AXES:
        layers, rows = lax.axis_size("layer"), lax.axis_size("row")
        place = [(b % layers) * rows + b // layers for b in range(count)]
    if count == 2:
        low = lax.axis_index(axis) == 0
        got = lax.ppermute(jnp.where(low, tail, head), axis, [(0, 1), (1, 0)])
        zero = jnp.zeros_like(got)
        return jnp.where(low, got, zero), jnp.where(low, zero, got)
    below = lax.ppermute(tail, axis, [(place[i], place[i + 1]) for i in range(count - 1)])
    above = lax.ppermute(head, axis, [(place[i + 1], place[i]) for i in range(count - 1)])
    return above, below


def neighbours(field, halo):
    out = []
    for (axis, dim), (above, below) in zip(GRID_AXES, halo):
        size = field.shape[dim]
        out.append(jnp.concatenate([lax.slice_in_dim(field, 1, size, axis=dim), above], axis=dim))
        out.append(jnp.concatenate([below, lax.slice_in_dim(field, 0, size - 1, axis=dim)], axis=dim))
    return out


def exchange(field):
    return [rims(field, axis, dim) for axis, dim in ((None, 0), (ROW_AXES, 1), ("col", 2))]


def apply_grid(field, near, weights, pad_term):
    result = pad_term * field
    for weight, other in zip(weights, near):
        result = result + weight * (field - other)
    return result


def smooth(resid, weights, pad_term, inverse):
    theta = (bound_high + bound_low) / 2.0
    delta = (bound_high - bound_low) / 2.0
    sigma = theta / delta
    rho = 1.0 / sigma
    change = inverse * resid / theta
    total = change
    for sweep in range(DEG - 1):
        remain = resid - apply_grid(total, neighbours(total, exchange(total)), weights, pad_term)
        rho_new = 1.0 / (2.0 * sigma - rho)
        change = rho_new * rho * change + 2.0 * rho_new / delta * inverse * remain
        total = total + change
        rho = rho_new
    return total


def all_sum(value):
    for axis, _ in GRID_AXES:
        count = lax.axis_size(axis)
        if count & (count - 1):
            value = lax.psum(value, axis)
            continue
        step = 1
        while step < count:
            value = value + lax.ppermute(value, axis, [(i, i ^ step) for i in range(count)])
            step *= 2
    return value


def share_tiles(tiles, own_rows, own_cols, flat_tiles):
    layers, rows, cols = (lax.axis_size(axis) for axis, _ in GRID_AXES)
    count = layers * rows * cols
    payload = jnp.broadcast_to(tiles.reshape(1, -1), (count, tiles.size))
    got = lax.all_to_all(payload, ("layer", "row", "col"), 0, 0, tiled=True)
    tile_cols = cols * own_cols
    tile_row, tile_col = flat_tiles // tile_cols, flat_tiles % tile_cols
    block = tile_row // own_rows
    device = ((block % layers) * rows + block // layers) * cols + tile_col // own_cols
    slot = (tile_row % own_rows) * own_cols + tile_col % own_cols
    pick_device = (device[:, None] == jnp.arange(count, dtype=jnp.int32)[None, :]).astype(jnp.float32)
    pick_slot = (slot[:, None] == jnp.arange(tiles.size, dtype=jnp.int32)[None, :]).astype(jnp.float32)
    return jnp.sum(jnp.dot(pick_device, got, precision=highest) * pick_slot, axis=1)


def swap_col(value):
    return lax.ppermute(value, "col", [(0, 1), (1, 0)])


def join_halves(mine, other, low):
    return jnp.where(low, jnp.concatenate([mine, other]), jnp.concatenate([other, mine]))


def coarse_pair(rhs, pivots, coupling):
    share = pivots.shape[1]
    low = lax.axis_index("col") == 0
    start = lax.axis_index("col") * share
    own = lambda vector: lax.dynamic_slice_in_dim(vector, start, share)
    other_half = lambda vector: lax.dynamic_slice_in_dim(vector, share - start, share)
    full = rhs[0]
    forward = [full]
    for section in range(1, NPANEL):
        piece = own(rhs[section]) - jnp.dot(coupling[section - 1], full, precision=highest)
        full = join_halves(piece, swap_col(piece), low)
        forward.append(full)
    scaled = [jnp.dot(pivots[section], forward[section], precision=highest) for section in range(NPANEL)]
    mine = scaled[NPANEL - 1]
    results = [None] * NPANEL
    for section in range(NPANEL - 2, 0, -1):
        partial = jnp.dot(mine, coupling[section], precision=highest)
        got = swap_col(jnp.concatenate([other_half(partial), mine]))
        results[section + 1] = join_halves(mine, got[share:], low)
        mine = scaled[section] - (own(partial) + got[:share])
    partial = jnp.dot(mine, coupling[0], precision=highest)
    got = swap_col(jnp.concatenate([partial, scaled[0], mine]))
    results[1] = join_halves(mine, got[PANEL + share:], low)
    first = join_halves(scaled[0], got[PANEL:PANEL + share], low)
    low_part = jnp.where(low, partial, got[:PANEL])
    high_part = jnp.where(low, got[:PANEL], partial)
    results[0] = first - (low_part + high_part)
    return jnp.stack(results)


def coarse_general(rhs, pivots, coupling):
    share = pivots.shape[1]
    start = lax.axis_index("col") * share
    full = rhs[0]
    forward = [full]
    for section in range(1, NPANEL):
        piece = lax.dynamic_slice_in_dim(rhs[section], start, share) - jnp.dot(
            coupling[section - 1], full, precision=highest
        )
        full = lax.all_gather(piece, "col", axis=0, tiled=True)
        forward.append(full)
    scaled = [jnp.dot(pivots[section], forward[section], precision=highest) for section in range(NPANEL)]
    results = [None] * NPANEL
    for section in range(NPANEL - 1, -1, -1):
        placed = lax.dynamic_update_slice_in_dim(jnp.zeros((PANEL,), jnp.float32), scaled[section], start, 0)
        if section < NPANEL - 1:
            later_rows = lax.dynamic_slice_in_dim(results[section + 1], start, share)
            placed = placed - jnp.dot(later_rows, coupling[section], precision=highest)
        results[section] = lax.psum(placed, "col")
    return jnp.stack(results)


def expand(values, edge):
    inner = values[1:-1] if edge else values
    body = jnp.repeat(inner, TILE, axis=0)
    if edge:
        body = jnp.concatenate([values[:1], body, values[-1:]], axis=0)
    return body


def shards(sources, conduct, via_cond, via_map, pad_map, port_tile, pivots, coupling):
    layer_count = lax.axis_size("layer")
    vertical = via_cond * via_map.astype(jnp.float32)
    packed = lax.all_to_all(jnp.stack((conduct, vertical)), "layer", 2, 1, tiled=True)
    conduct, vertical = packed[0], packed[1]
    sources = lax.all_to_all(sources, "layer", 1, 0, tiled=True)
    local_layers, grid_rows, grid_cols = sources.shape
    pad_rows = lax.dynamic_slice_in_dim(pad_map, lax.axis_index("layer") * grid_rows, grid_rows, 0)
    row_halo = rims(conduct, ROW_AXES, 1)
    col_halo = rims(conduct, "col", 2)
    layer_halo = rims(vertical, None, 0)
    near_vert = neighbours(vertical, [layer_halo, row_halo, col_halo])
    near_plane = neighbours(conduct, [layer_halo, row_halo, col_halo])
    weights = (
        jnp.sqrt(vertical * near_vert[0]),
        jnp.sqrt(vertical * near_vert[1]),
        jnp.sqrt(conduct * near_plane[2]),
        jnp.sqrt(conduct * near_plane[3]),
        jnp.sqrt(conduct * near_plane[4]),
        jnp.sqrt(conduct * near_plane[5]),
    )
    top_layer = pad_gain * pad_rows.astype(jnp.float32)
    pad_term = jnp.concatenate(
        (jnp.zeros((local_layers - 1, grid_rows, grid_cols), jnp.float32), top_layer[None]), 0
    )
    diagonal = pad_term
    for weight in weights:
        diagonal = diagonal + weight
    inverse = 1.0 / diagonal

    col_count = lax.axis_size("col")
    tile_cols = grid_cols * col_count // TILE
    tile_rows = grid_rows * axis_count(ROW_AXES) // TILE
    own_rows = grid_rows // TILE
    own_cols = grid_cols // TILE
    first_row = (lax.axis_index("row") * layer_count + lax.axis_index("layer")) * own_rows
    first_col = lax.axis_index("col") * own_cols
    flat_tiles = port_tile.reshape(-1)
    ring_rows = first_row - 1 + jnp.arange(own_rows + 2, dtype=jnp.int32)
    ring_cols = first_col - 1 + jnp.arange(own_cols + 2, dtype=jnp.int32)
    ring_ok = ((ring_rows >= 0) & (ring_rows < tile_rows))[:, None] & ((ring_cols >= 0) & (ring_cols < tile_cols))[None, :]
    ring_ids = jnp.where(ring_ok, ring_rows[:, None] * tile_cols + ring_cols[None, :], -1).reshape(-1)
    scatter_ring = (ring_ids[:, None] == flat_tiles[None, :]).astype(jnp.float32)
    coarse = coarse_pair if col_count == 2 else coarse_general

    drop = None
    drop_near = None
    for outer in range(ITERS):
        if drop is None:
            resid = sources
        else:
            resid = sources - apply_grid(drop, drop_near, weights, pad_term)
        plane = jnp.sum(resid, axis=0)
        tiles = plane.reshape(own_rows, TILE, own_cols, TILE).sum(axis=(1, 3)).reshape(-1)
        rhs = share_tiles(tiles, own_rows, own_cols, flat_tiles).reshape(NPANEL, PANEL) * (restrict_scale / TILE)
        ports = coarse(rhs, pivots, coupling)
        tile_values = jnp.dot(scatter_ring, ports.reshape(-1), precision=highest).reshape(own_rows + 2, own_cols + 2)
        ring = expand(expand(tile_values, True).T, True).T * prolong_scale
        centre = ring[1:-1, 1:-1]
        lifted = jnp.broadcast_to(centre[None], (local_layers, grid_rows, grid_cols))
        total = smooth(resid, weights, pad_term, inverse)
        if outer == ITERS - 1:
            drop = (lifted if drop is None else drop + lifted) + total
            break
        lifted_near = [lifted, lifted]
        for part in (ring[2:, 1:-1], ring[:-2, 1:-1], ring[1:-1, 2:], ring[1:-1, :-2]):
            lifted_near.append(jnp.broadcast_to(part[None], (local_layers, grid_rows, grid_cols)))
        total_near = neighbours(total, exchange(total))
        if drop is None:
            drop = lifted + total
            drop_near = [a + b for a, b in zip(lifted_near, total_near)]
        else:
            drop = drop + lifted + total
            drop_near = [(d + a) + b for d, a, b in zip(drop_near, lifted_near, total_near)]
    drop = lax.all_to_all(drop, "layer", 0, 1, tiled=True)
    return (drop, ports)


def solution(mesh):
    placed = (
        P("layer", "row", "col"),
        P("layer", "row", "col"),
        P("layer", "row", "col"),
        P("layer", "row", "col"),
        P("row", "col"),
        P(),
        P(None, "col", None),
        P(None, "col", None),
    )
    return jax.shard_map(
        shards,
        mesh=mesh,
        in_specs=placed,
        out_specs=(P("layer", "row", "col"), P()),
        check_vma=False,
    )
```

```python
import jax
import jax.numpy as jnp
from jax import lax
from jax.sharding import PartitionSpec as P

TILE = 16
PANEL = 512
NPANEL = 4
DEG = 3
ITERS = 2


pad_gain = 8.0
bound_low = 0.1
bound_high = 1.9
restrict_scale = 0.25
prolong_scale = 0.5

highest = lax.Precision.HIGHEST
GRID_AXES = (("layer", 0), ("row", 1), ("col", 2))
ROW_AXES = ("layer", "row")


def axis_count(axis):
    names = axis if isinstance(axis, tuple) else (axis,)
    count = 1
    for name in names:
        count *= lax.axis_size(name)
    return count


def rims(field, axis, dim):
    size = field.shape[dim]
    head = lax.slice_in_dim(field, 0, 1, axis=dim)
    tail = lax.slice_in_dim(field, size - 1, size, axis=dim)
    if axis is None:
        return jnp.zeros_like(head), jnp.zeros_like(tail)
    count = axis_count(axis)
    place = list(range(count))
    if axis == ROW_AXES:
        layers, rows = lax.axis_size("layer"), lax.axis_size("row")
        place = [(b % layers) * rows + b // layers for b in range(count)]
    if count == 2:
        low = lax.axis_index(axis) == 0
        got = lax.ppermute(jnp.where(low, tail, head), axis, [(0, 1), (1, 0)])
        zero = jnp.zeros_like(got)
        return jnp.where(low, got, zero), jnp.where(low, zero, got)
    below = lax.ppermute(tail, axis, [(place[i], place[i + 1]) for i in range(count - 1)])
    above = lax.ppermute(head, axis, [(place[i + 1], place[i]) for i in range(count - 1)])
    return above, below


def neighbours(field, halo):
    out = []
    for (axis, dim), (above, below) in zip(GRID_AXES, halo):
        size = field.shape[dim]
        out.append(jnp.concatenate([lax.slice_in_dim(field, 1, size, axis=dim), above], axis=dim))
        out.append(jnp.concatenate([below, lax.slice_in_dim(field, 0, size - 1, axis=dim)], axis=dim))
    return out


def exchange(field):
    return [rims(field, axis, dim) for axis, dim in ((None, 0), (ROW_AXES, 1), ("col", 2))]


def apply_grid(field, near, weights, pad_term):
    result = pad_term * field
    for weight, other in zip(weights, near):
        result = result + weight * (field - other)
    return result


def smooth(resid, weights, pad_term, inverse):
    theta = (bound_high + bound_low) / 2.0
    delta = (bound_high - bound_low) / 2.0
    sigma = theta / delta
    rho = 1.0 / sigma
    change = inverse * resid / theta
    total = change
    for sweep in range(DEG - 1):
        remain = resid - apply_grid(total, neighbours(total, exchange(total)), weights, pad_term)
        rho_new = 1.0 / (2.0 * sigma - rho)
        change = rho_new * rho * change + 2.0 * rho_new / delta * inverse * remain
        total = total + change
        rho = rho_new
    return total


def all_sum(value):
    for axis, _ in GRID_AXES:
        count = lax.axis_size(axis)
        if count & (count - 1):
            value = lax.psum(value, axis)
            continue
        step = 1
        while step < count:
            value = value + lax.ppermute(value, axis, [(i, i ^ step) for i in range(count)])
            step *= 2
    return value


def share_tiles(tiles, own_rows, own_cols, flat_tiles):
    layers, rows, cols = (lax.axis_size(axis) for axis, _ in GRID_AXES)
    count = layers * rows * cols
    payload = jnp.broadcast_to(tiles.reshape(1, -1), (count, tiles.size))
    got = lax.all_to_all(payload, ("layer", "row", "col"), 0, 0, tiled=True)
    tile_cols = cols * own_cols
    tile_row, tile_col = flat_tiles // tile_cols, flat_tiles % tile_cols
    block = tile_row // own_rows
    device = ((block % layers) * rows + block // layers) * cols + tile_col // own_cols
    slot = (tile_row % own_rows) * own_cols + tile_col % own_cols
    pick_device = (device[:, None] == jnp.arange(count, dtype=jnp.int32)[None, :]).astype(jnp.float32)
    pick_slot = (slot[:, None] == jnp.arange(tiles.size, dtype=jnp.int32)[None, :]).astype(jnp.float32)
    return jnp.sum(jnp.dot(pick_device, got, precision=highest) * pick_slot, axis=1)


def swap_col(value):
    return lax.ppermute(value, "col", [(0, 1), (1, 0)])


def join_halves(mine, other, low):
    return jnp.where(low, jnp.concatenate([mine, other]), jnp.concatenate([other, mine]))


def coarse_pair(rhs, pivots, coupling):
    share = pivots.shape[1]
    low = lax.axis_index("col") == 0
    start = lax.axis_index("col") * share
    own = lambda vector: lax.dynamic_slice_in_dim(vector, start, share)
    other_half = lambda vector: lax.dynamic_slice_in_dim(vector, share - start, share)
    full = rhs[0]
    forward = [full]
    for section in range(1, NPANEL):
        piece = own(rhs[section]) - jnp.dot(coupling[section - 1], full, precision=highest)
        full = join_halves(piece, swap_col(piece), low)
        forward.append(full)
    scaled = [jnp.dot(pivots[section], forward[section], precision=highest) for section in range(NPANEL)]
    mine = scaled[NPANEL - 1]
    results = [None] * NPANEL
    for section in range(NPANEL - 2, 0, -1):
        partial = jnp.dot(mine, coupling[section], precision=highest)
        got = swap_col(jnp.concatenate([other_half(partial), mine]))
        results[section + 1] = join_halves(mine, got[share:], low)
        mine = scaled[section] - (own(partial) + got[:share])
    partial = jnp.dot(mine, coupling[0], precision=highest)
    got = swap_col(jnp.concatenate([partial, scaled[0], mine]))
    results[1] = join_halves(mine, got[PANEL + share:], low)
    first = join_halves(scaled[0], got[PANEL:PANEL + share], low)
    low_part = jnp.where(low, partial, got[:PANEL])
    high_part = jnp.where(low, got[:PANEL], partial)
    results[0] = first - (low_part + high_part)
    return jnp.stack(results)


def coarse_rows(rhs, pivots, coupling):
    share = pivots.shape[1]
    low = lax.axis_index("col") == 0
    start = lax.axis_index("col") * share
    own = lambda vector: lax.dynamic_slice_in_dim(vector, start, share)
    forward = [rhs[0]]
    for section in range(1, NPANEL):
        forward.append(rhs[section] - jnp.dot(coupling[section - 1], forward[-1], precision=highest))
    scaled = [jnp.dot(pivots[section], forward[section], precision=highest) for section in range(NPANEL)]
    results = [None] * NPANEL
    mine = scaled[NPANEL - 1]
    for section in range(NPANEL - 2, 0, -1):
        later = join_halves(mine, swap_col(mine), low)
        results[section + 1] = later
        mine = scaled[section] - own(jnp.dot(later, coupling[section], precision=highest))
    got = swap_col(jnp.concatenate([mine, scaled[0]]))
    results[1] = join_halves(mine, got[:share], low)
    first = join_halves(scaled[0], got[share:], low)
    results[0] = first - jnp.dot(results[1], coupling[0], precision=highest)
    return jnp.stack(results)


def whole_coupling(coupling):
    layers = lax.axis_size("layer")
    quarter = coupling.shape[1] // 2
    core = lax.axis_index("layer") % 2
    piece = lax.dynamic_slice_in_dim(coupling, core * quarter, quarter, 1)
    first = swap_col(piece)
    second = lax.ppermute(first, "layer", [(i, i ^ 1) for i in range(layers)])
    other = jnp.where(core == 0, jnp.concatenate([first, second], 1), jnp.concatenate([second, first], 1))
    low = lax.axis_index("col") == 0
    return jnp.where(low, jnp.concatenate([coupling, other], 1), jnp.concatenate([other, coupling], 1))


def coarse_general(rhs, pivots, coupling):
    share = pivots.shape[1]
    start = lax.axis_index("col") * share
    full = rhs[0]
    forward = [full]
    for section in range(1, NPANEL):
        piece = lax.dynamic_slice_in_dim(rhs[section], start, share) - jnp.dot(
            coupling[section - 1], full, precision=highest
        )
        full = lax.all_gather(piece, "col", axis=0, tiled=True)
        forward.append(full)
    scaled = [jnp.dot(pivots[section], forward[section], precision=highest) for section in range(NPANEL)]
    results = [None] * NPANEL
    for section in range(NPANEL - 1, -1, -1):
        placed = lax.dynamic_update_slice_in_dim(jnp.zeros((PANEL,), jnp.float32), scaled[section], start, 0)
        if section < NPANEL - 1:
            later_rows = lax.dynamic_slice_in_dim(results[section + 1], start, share)
            placed = placed - jnp.dot(later_rows, coupling[section], precision=highest)
        results[section] = lax.psum(placed, "col")
    return jnp.stack(results)


def expand(values, edge):
    inner = values[1:-1] if edge else values
    body = jnp.repeat(inner, TILE, axis=0)
    if edge:
        body = jnp.concatenate([values[:1], body, values[-1:]], axis=0)
    return body


def shards(sources, conduct, via_cond, via_map, pad_map, port_tile, pivots, coupling):
    layer_count = lax.axis_size("layer")
    vertical = via_cond * via_map.astype(jnp.float32)
    split_coupling = lax.axis_size("col") == 2 and layer_count % 2 == 0 and coupling.shape[1] % 2 == 0
    if split_coupling:
        full_coupling = whole_coupling(coupling)
    packed = lax.all_to_all(jnp.stack((conduct, vertical)), "layer", 2, 1, tiled=True)
    conduct, vertical = packed[0], packed[1]
    sources = lax.all_to_all(sources, "layer", 1, 0, tiled=True)
    local_layers, grid_rows, grid_cols = sources.shape
    pad_rows = lax.dynamic_slice_in_dim(pad_map, lax.axis_index("layer") * grid_rows, grid_rows, 0)
    row_halo = rims(conduct, ROW_AXES, 1)
    col_halo = rims(conduct, "col", 2)
    layer_halo = rims(vertical, None, 0)
    near_vert = neighbours(vertical, [layer_halo, row_halo, col_halo])
    near_plane = neighbours(conduct, [layer_halo, row_halo, col_halo])
    weights = (
        jnp.sqrt(vertical * near_vert[0]),
        jnp.sqrt(vertical * near_vert[1]),
        jnp.sqrt(conduct * near_plane[2]),
        jnp.sqrt(conduct * near_plane[3]),
        jnp.sqrt(conduct * near_plane[4]),
        jnp.sqrt(conduct * near_plane[5]),
    )
    top_layer = pad_gain * pad_rows.astype(jnp.float32)
    pad_term = jnp.concatenate(
        (jnp.zeros((local_layers - 1, grid_rows, grid_cols), jnp.float32), top_layer[None]), 0
    )
    diagonal = pad_term
    for weight in weights:
        diagonal = diagonal + weight
    inverse = 1.0 / diagonal

    col_count = lax.axis_size("col")
    tile_cols = grid_cols * col_count // TILE
    tile_rows = grid_rows * axis_count(ROW_AXES) // TILE
    own_rows = grid_rows // TILE
    own_cols = grid_cols // TILE
    first_row = (lax.axis_index("row") * layer_count + lax.axis_index("layer")) * own_rows
    first_col = lax.axis_index("col") * own_cols
    flat_tiles = port_tile.reshape(-1)
    ring_rows = first_row - 1 + jnp.arange(own_rows + 2, dtype=jnp.int32)
    ring_cols = first_col - 1 + jnp.arange(own_cols + 2, dtype=jnp.int32)
    ring_ok = ((ring_rows >= 0) & (ring_rows < tile_rows))[:, None] & ((ring_cols >= 0) & (ring_cols < tile_cols))[None, :]
    ring_ids = jnp.where(ring_ok, ring_rows[:, None] * tile_cols + ring_cols[None, :], -1).reshape(-1)
    scatter_ring = (ring_ids[:, None] == flat_tiles[None, :]).astype(jnp.float32)
    coarse = coarse_pair if col_count == 2 else coarse_general

    drop = None
    drop_near = None
    for outer in range(ITERS):
        if drop is None:
            resid = sources
        else:
            resid = sources - apply_grid(drop, drop_near, weights, pad_term)
        plane = jnp.sum(resid, axis=0)
        tiles = plane.reshape(own_rows, TILE, own_cols, TILE).sum(axis=(1, 3)).reshape(-1)
        rhs = share_tiles(tiles, own_rows, own_cols, flat_tiles).reshape(NPANEL, PANEL) * (restrict_scale / TILE)
        if split_coupling:
            ports = coarse_rows(rhs, pivots, full_coupling)
        else:
            ports = coarse(rhs, pivots, coupling)
        tile_values = jnp.dot(scatter_ring, ports.reshape(-1), precision=highest).reshape(own_rows + 2, own_cols + 2)
        ring = expand(expand(tile_values, True).T, True).T * prolong_scale
        centre = ring[1:-1, 1:-1]
        lifted = jnp.broadcast_to(centre[None], (local_layers, grid_rows, grid_cols))
        total = smooth(resid, weights, pad_term, inverse)
        if outer == ITERS - 1:
            drop = (lifted if drop is None else drop + lifted) + total
            break
        lifted_near = [lifted, lifted]
        for part in (ring[2:, 1:-1], ring[:-2, 1:-1], ring[1:-1, 2:], ring[1:-1, :-2]):
            lifted_near.append(jnp.broadcast_to(part[None], (local_layers, grid_rows, grid_cols)))
        total_near = neighbours(total, exchange(total))
        if drop is None:
            drop = lifted + total
            drop_near = [a + b for a, b in zip(lifted_near, total_near)]
        else:
            drop = drop + lifted + total
            drop_near = [(d + a) + b for d, a, b in zip(drop_near, lifted_near, total_near)]
    drop = lax.all_to_all(drop, "layer", 0, 1, tiled=True)
    return (drop, ports)


def solution(mesh):
    placed = (
        P("layer", "row", "col"),
        P("layer", "row", "col"),
        P("layer", "row", "col"),
        P("layer", "row", "col"),
        P("row", "col"),
        P(),
        P(None, "col", None),
        P(None, "col", None),
    )
    return jax.shard_map(
        shards,
        mesh=mesh,
        in_specs=placed,
        out_specs=(P("layer", "row", "col"), P()),
        check_vma=False,
    )
```

```python
import jax
import jax.numpy as jnp
from jax import lax
from jax.sharding import PartitionSpec as P

TILE = 16
PANEL = 512
NPANEL = 4
DEG = 3
ITERS = 2


pad_gain = 8.0
bound_low = 0.1
bound_high = 1.9
restrict_scale = 0.25
prolong_scale = 0.5

highest = lax.Precision.HIGHEST
GRID_AXES = (("layer", 0), ("row", 1), ("col", 2))
ROW_AXES = ("layer", "row")


def axis_count(axis):
    names = axis if isinstance(axis, tuple) else (axis,)
    count = 1
    for name in names:
        count *= lax.axis_size(name)
    return count


def rims(field, axis, dim):
    size = field.shape[dim]
    head = lax.slice_in_dim(field, 0, 1, axis=dim)
    tail = lax.slice_in_dim(field, size - 1, size, axis=dim)
    if axis is None:
        return jnp.zeros_like(head), jnp.zeros_like(tail)
    count = axis_count(axis)
    place = list(range(count))
    if axis == ROW_AXES:
        layers, rows = lax.axis_size("layer"), lax.axis_size("row")
        place = [(b % layers) * rows + b // layers for b in range(count)]
    if count == 2:
        low = lax.axis_index(axis) == 0
        got = lax.ppermute(jnp.where(low, tail, head), axis, [(0, 1), (1, 0)])
        zero = jnp.zeros_like(got)
        return jnp.where(low, got, zero), jnp.where(low, zero, got)
    below = lax.ppermute(tail, axis, [(place[i], place[i + 1]) for i in range(count - 1)])
    above = lax.ppermute(head, axis, [(place[i + 1], place[i]) for i in range(count - 1)])
    return above, below


def neighbours(field, halo):
    out = []
    for (axis, dim), (above, below) in zip(GRID_AXES, halo):
        size = field.shape[dim]
        out.append(jnp.concatenate([lax.slice_in_dim(field, 1, size, axis=dim), above], axis=dim))
        out.append(jnp.concatenate([below, lax.slice_in_dim(field, 0, size - 1, axis=dim)], axis=dim))
    return out


def exchange(field):
    return [rims(field, axis, dim) for axis, dim in ((None, 0), (ROW_AXES, 1), ("col", 2))]


def apply_grid(field, near, weights, pad_term):
    result = pad_term * field
    for weight, other in zip(weights, near):
        result = result + weight * (field - other)
    return result


def smooth(resid, weights, pad_term, inverse):
    theta = (bound_high + bound_low) / 2.0
    delta = (bound_high - bound_low) / 2.0
    sigma = theta / delta
    rho = 1.0 / sigma
    change = inverse * resid / theta
    total = change
    for sweep in range(DEG - 1):
        remain = resid - apply_grid(total, neighbours(total, exchange(total)), weights, pad_term)
        rho_new = 1.0 / (2.0 * sigma - rho)
        change = rho_new * rho * change + 2.0 * rho_new / delta * inverse * remain
        total = total + change
        rho = rho_new
    return total


def all_sum(value):
    for axis, _ in GRID_AXES:
        count = lax.axis_size(axis)
        if count & (count - 1):
            value = lax.psum(value, axis)
            continue
        step = 1
        while step < count:
            value = value + lax.ppermute(value, axis, [(i, i ^ step) for i in range(count)])
            step *= 2
    return value


def share_tiles(tiles, own_rows, own_cols, flat_tiles):
    layers, rows, cols = (lax.axis_size(axis) for axis, _ in GRID_AXES)
    count = layers * rows * cols
    payload = jnp.broadcast_to(tiles.reshape(1, -1), (count, tiles.size))
    got = lax.all_to_all(payload, ("layer", "row", "col"), 0, 0, tiled=True)
    tile_cols = cols * own_cols
    tile_row, tile_col = flat_tiles // tile_cols, flat_tiles % tile_cols
    block = tile_row // own_rows
    device = ((block % layers) * rows + block // layers) * cols + tile_col // own_cols
    slot = (tile_row % own_rows) * own_cols + tile_col % own_cols
    pick_device = (device[:, None] == jnp.arange(count, dtype=jnp.int32)[None, :]).astype(jnp.float32)
    pick_slot = (slot[:, None] == jnp.arange(tiles.size, dtype=jnp.int32)[None, :]).astype(jnp.float32)
    return jnp.sum(jnp.dot(pick_device, got, precision=highest) * pick_slot, axis=1)


def swap_col(value):
    return lax.ppermute(value, "col", [(0, 1), (1, 0)])


def join_halves(mine, other, low):
    return jnp.where(low, jnp.concatenate([mine, other]), jnp.concatenate([other, mine]))


def coarse_pair(rhs, pivots, coupling):
    share = pivots.shape[1]
    low = lax.axis_index("col") == 0
    start = lax.axis_index("col") * share
    own = lambda vector: lax.dynamic_slice_in_dim(vector, start, share)
    other_half = lambda vector: lax.dynamic_slice_in_dim(vector, share - start, share)
    full = rhs[0]
    forward = [full]
    for section in range(1, NPANEL):
        piece = own(rhs[section]) - jnp.dot(coupling[section - 1], full, precision=highest)
        full = join_halves(piece, swap_col(piece), low)
        forward.append(full)
    scaled = [jnp.dot(pivots[section], forward[section], precision=highest) for section in range(NPANEL)]
    mine = scaled[NPANEL - 1]
    results = [None] * NPANEL
    for section in range(NPANEL - 2, 0, -1):
        partial = jnp.dot(mine, coupling[section], precision=highest)
        got = swap_col(jnp.concatenate([other_half(partial), mine]))
        results[section + 1] = join_halves(mine, got[share:], low)
        mine = scaled[section] - (own(partial) + got[:share])
    partial = jnp.dot(mine, coupling[0], precision=highest)
    got = swap_col(jnp.concatenate([partial, scaled[0], mine]))
    results[1] = join_halves(mine, got[PANEL + share:], low)
    first = join_halves(scaled[0], got[PANEL:PANEL + share], low)
    low_part = jnp.where(low, partial, got[:PANEL])
    high_part = jnp.where(low, got[:PANEL], partial)
    results[0] = first - (low_part + high_part)
    return jnp.stack(results)


def coarse_general(rhs, pivots, coupling):
    share = pivots.shape[1]
    start = lax.axis_index("col") * share
    full = rhs[0]
    forward = [full]
    for section in range(1, NPANEL):
        piece = lax.dynamic_slice_in_dim(rhs[section], start, share) - jnp.dot(
            coupling[section - 1], full, precision=highest
        )
        full = lax.all_gather(piece, "col", axis=0, tiled=True)
        forward.append(full)
    scaled = [jnp.dot(pivots[section], forward[section], precision=highest) for section in range(NPANEL)]
    results = [None] * NPANEL
    for section in range(NPANEL - 1, -1, -1):
        placed = lax.dynamic_update_slice_in_dim(jnp.zeros((PANEL,), jnp.float32), scaled[section], start, 0)
        if section < NPANEL - 1:
            later_rows = lax.dynamic_slice_in_dim(results[section + 1], start, share)
            placed = placed - jnp.dot(later_rows, coupling[section], precision=highest)
        results[section] = lax.psum(placed, "col")
    return jnp.stack(results)


def expand(values, edge):
    inner = values[1:-1] if edge else values
    body = jnp.repeat(inner, TILE, axis=0)
    if edge:
        body = jnp.concatenate([values[:1], body, values[-1:]], axis=0)
    return body


def shards_blocks(sources, conduct, via_cond, via_map, pad_map, port_tile, pivots, coupling):
    layer_count = lax.axis_size("layer")
    vertical = via_cond * via_map.astype(jnp.float32)
    packed = lax.all_to_all(jnp.stack((sources, conduct, vertical)), "layer", 2, 1, tiled=True)
    sources, conduct, vertical = packed[0], packed[1], packed[2]
    local_layers, grid_rows, grid_cols = sources.shape
    pad_rows = lax.dynamic_slice_in_dim(pad_map, lax.axis_index("layer") * grid_rows, grid_rows, 0)
    row_halo = rims(conduct, ROW_AXES, 1)
    col_halo = rims(conduct, "col", 2)
    layer_halo = rims(vertical, None, 0)
    near_vert = neighbours(vertical, [layer_halo, row_halo, col_halo])
    near_plane = neighbours(conduct, [layer_halo, row_halo, col_halo])
    weights = (
        jnp.sqrt(vertical * near_vert[0]),
        jnp.sqrt(vertical * near_vert[1]),
        jnp.sqrt(conduct * near_plane[2]),
        jnp.sqrt(conduct * near_plane[3]),
        jnp.sqrt(conduct * near_plane[4]),
        jnp.sqrt(conduct * near_plane[5]),
    )
    top_layer = pad_gain * pad_rows.astype(jnp.float32)
    pad_term = jnp.concatenate(
        (jnp.zeros((local_layers - 1, grid_rows, grid_cols), jnp.float32), top_layer[None]), 0
    )
    diagonal = pad_term
    for weight in weights:
        diagonal = diagonal + weight
    inverse = 1.0 / diagonal

    col_count = lax.axis_size("col")
    tile_cols = grid_cols * col_count // TILE
    tile_rows = grid_rows * axis_count(ROW_AXES) // TILE
    own_rows = grid_rows // TILE
    own_cols = grid_cols // TILE
    first_row = (lax.axis_index("row") * layer_count + lax.axis_index("layer")) * own_rows
    first_col = lax.axis_index("col") * own_cols
    flat_tiles = port_tile.reshape(-1)
    ring_rows = first_row - 1 + jnp.arange(own_rows + 2, dtype=jnp.int32)
    ring_cols = first_col - 1 + jnp.arange(own_cols + 2, dtype=jnp.int32)
    ring_ok = ((ring_rows >= 0) & (ring_rows < tile_rows))[:, None] & ((ring_cols >= 0) & (ring_cols < tile_cols))[None, :]
    ring_ids = jnp.where(ring_ok, ring_rows[:, None] * tile_cols + ring_cols[None, :], -1).reshape(-1)
    scatter_ring = (ring_ids[:, None] == flat_tiles[None, :]).astype(jnp.float32)
    coarse = coarse_pair if col_count == 2 else coarse_general

    drop = None
    drop_near = None
    for outer in range(ITERS):
        if drop is None:
            resid = sources
        else:
            resid = sources - apply_grid(drop, drop_near, weights, pad_term)
        plane = jnp.sum(resid, axis=0)
        tiles = plane.reshape(own_rows, TILE, own_cols, TILE).sum(axis=(1, 3)).reshape(-1)
        rhs = share_tiles(tiles, own_rows, own_cols, flat_tiles).reshape(NPANEL, PANEL) * (restrict_scale / TILE)
        ports = coarse(rhs, pivots, coupling)
        tile_values = jnp.dot(scatter_ring, ports.reshape(-1), precision=highest).reshape(own_rows + 2, own_cols + 2)
        ring = expand(expand(tile_values, True).T, True).T * prolong_scale
        centre = ring[1:-1, 1:-1]
        lifted = jnp.broadcast_to(centre[None], (local_layers, grid_rows, grid_cols))
        total = smooth(resid, weights, pad_term, inverse)
        if outer == ITERS - 1:
            drop = (lifted if drop is None else drop + lifted) + total
            break
        lifted_near = [lifted, lifted]
        for part in (ring[2:, 1:-1], ring[:-2, 1:-1], ring[1:-1, 2:], ring[1:-1, :-2]):
            lifted_near.append(jnp.broadcast_to(part[None], (local_layers, grid_rows, grid_cols)))
        total_near = neighbours(total, exchange(total))
        if drop is None:
            drop = lifted + total
            drop_near = [a + b for a, b in zip(lifted_near, total_near)]
        else:
            drop = drop + lifted + total
            drop_near = [(d + a) + b for d, a, b in zip(drop_near, lifted_near, total_near)]
    drop = lax.all_to_all(drop, "layer", 0, 1, tiled=True)
    return (drop, ports)


def shards_rows(sources, conduct, via_cond, via_map, pad_map, port_tile, pivots, coupling):
    layer_count, row_count, col_count = (lax.axis_size(axis) for axis, _ in GRID_AXES)
    vertical = via_cond * via_map.astype(jnp.float32)
    local_layers, block_rows, block_cols = sources.shape
    group = layer_count * col_count
    rows = block_rows // group
    pad_plane = jnp.broadcast_to(pad_map.astype(jnp.float32)[None], sources.shape)
    packed = jnp.stack((sources, conduct, vertical, pad_plane)).reshape(4, local_layers, group, rows, block_cols)
    packed = lax.all_to_all(packed, ("layer", "col"), 2, 2, tiled=True)
    packed = packed.reshape(4, local_layers, layer_count, col_count, rows, block_cols)
    packed = packed.transpose(0, 2, 1, 4, 3, 5).reshape(4, layer_count * local_layers, rows, col_count * block_cols)
    sources, conduct, vertical = packed[0], packed[1], packed[2]
    pad_rows = packed[3][-1]
    layers, _, grid_cols = sources.shape
    blocks = row_count * group
    place = []
    for block in range(blocks):
        r, rest = divmod(block, group)
        l, c = divmod(rest, col_count)
        place.append((l * row_count + r) * col_count + c)
    block = lax.axis_index("row") * group + lax.axis_index("layer") * col_count + lax.axis_index("col")

    def row_rims(field):
        head, tail = field[:, :1], field[:, -1:]
        below = lax.ppermute(tail, ("layer", "row", "col"), [(place[i], place[i + 1]) for i in range(blocks - 1)])
        above = lax.ppermute(head, ("layer", "row", "col"), [(place[i + 1], place[i]) for i in range(blocks - 1)])
        return above, below

    def halo_of(field, row_halo):
        return [rims(field, None, 0), row_halo, rims(field, None, 2)]

    def grid_apply(field, row_halo):
        return apply_grid(field, neighbours(field, halo_of(field, row_halo)), weights, pad_term)

    near_vert = neighbours(vertical, halo_of(vertical, row_rims(vertical)))
    near_plane = neighbours(conduct, halo_of(conduct, row_rims(conduct)))
    weights = (
        jnp.sqrt(vertical * near_vert[0]),
        jnp.sqrt(vertical * near_vert[1]),
        jnp.sqrt(conduct * near_plane[2]),
        jnp.sqrt(conduct * near_plane[3]),
        jnp.sqrt(conduct * near_plane[4]),
        jnp.sqrt(conduct * near_plane[5]),
    )
    pad_term = jnp.concatenate((jnp.zeros((layers - 1, rows, grid_cols), jnp.float32), (pad_gain * pad_rows)[None]), 0)
    diagonal = pad_term
    for weight in weights:
        diagonal = diagonal + weight
    inverse = 1.0 / diagonal

    theta = (bound_high + bound_low) / 2.0
    delta = (bound_high - bound_low) / 2.0
    sigma = theta / delta

    def smooth_rows(resid):
        rho = 1.0 / sigma
        change = inverse * resid / theta
        total = change
        for sweep in range(DEG - 1):
            remain = resid - grid_apply(total, row_rims(total))
            rho_new = 1.0 / (2.0 * sigma - rho)
            change = rho_new * rho * change + 2.0 * rho_new / delta * inverse * remain
            total = total + change
            rho = rho_new
        return total

    tile_cols = grid_cols // TILE
    tile_rows = rows * blocks // TILE
    flat_tiles = port_tile.reshape(-1)
    port_row, port_col = flat_tiles // tile_cols, flat_tiles % tile_cols
    devices = jnp.arange(layer_count * row_count * col_count, dtype=jnp.int32)
    device_block = (devices // (row_count * col_count)) * col_count + (devices // col_count) % row_count * group + devices % col_count
    pick_device = ((device_block * rows) // TILE == port_row[:, None]).astype(jnp.float32)
    pick_slot = (port_col[:, None] == jnp.arange(tile_cols, dtype=jnp.int32)[None, :]).astype(jnp.float32)
    first_ring = (block * rows - 1) // TILE
    ring_count = rows // TILE + 2
    ring_rows = first_ring + jnp.arange(ring_count, dtype=jnp.int32)
    ring_ids = jnp.where(((ring_rows >= 0) & (ring_rows < tile_rows))[:, None], ring_rows[:, None] * tile_cols + jnp.arange(tile_cols, dtype=jnp.int32)[None, :], -1).reshape(-1)
    scatter_ring = (ring_ids[:, None] == flat_tiles[None, :]).astype(jnp.float32)
    node_rows = block * rows - 1 + jnp.arange(rows + 2, dtype=jnp.int32)
    pick_ring = ((node_rows // TILE - first_ring)[:, None] == jnp.arange(ring_count, dtype=jnp.int32)[None, :]).astype(jnp.float32)

    drop = None
    for outer in range(ITERS):
        if drop is None:
            resid = sources
        else:
            resid = sources - grid_apply(drop, drop_halo)
        plane = jnp.sum(resid, axis=0)
        tiles = plane.reshape(rows, tile_cols, TILE).sum(axis=(0, 2))
        count = layer_count * row_count * col_count
        got = lax.all_to_all(jnp.broadcast_to(tiles[None], (count, tile_cols)), ("layer", "row", "col"), 0, 0, tiled=True)
        rhs = jnp.sum(jnp.dot(pick_device, got, precision=highest) * pick_slot, axis=1)
        rhs = rhs.reshape(NPANEL, PANEL) * (restrict_scale / TILE)
        ports = coarse_pair(rhs, pivots, coupling) if col_count == 2 else coarse_general(rhs, pivots, coupling)
        tile_values = jnp.dot(scatter_ring, ports.reshape(-1), precision=highest).reshape(ring_count, tile_cols)
        ring = jnp.repeat(jnp.dot(pick_ring, tile_values, precision=highest), TILE, axis=1) * prolong_scale
        lifted = jnp.broadcast_to(ring[None, 1:-1], (layers, rows, grid_cols))
        total = smooth_rows(resid)
        if outer == ITERS - 1:
            drop = (lifted if drop is None else drop + lifted) + total
            break
        above, below = row_rims(total)
        lifted_above = jnp.broadcast_to(ring[None, -1:], above.shape)
        lifted_below = jnp.broadcast_to(ring[None, :1], below.shape)
        if drop is None:
            drop = lifted + total
            drop_halo = (lifted_above + above, lifted_below + below)
        else:
            drop = drop + lifted + total
            drop_halo = ((drop_halo[0] + lifted_above) + above, (drop_halo[1] + lifted_below) + below)
    back = drop.reshape(layer_count, local_layers, rows, col_count, block_cols).transpose(0, 3, 1, 2, 4)
    back = lax.all_to_all(back.reshape(group, local_layers, rows, block_cols), ("layer", "col"), 0, 0, tiled=True)
    drop = back.transpose(1, 0, 2, 3).reshape(local_layers, block_rows, block_cols)
    return (drop, ports)


def shards(*args):
    group = lax.axis_size("layer") * lax.axis_size("col")
    block_rows = args[0].shape[1]
    if block_rows % group == 0 and TILE % (block_rows // group) == 0:
        return shards_rows(*args)
    return shards_blocks(*args)


def solution(mesh):
    placed = (
        P("layer", "row", "col"),
        P("layer", "row", "col"),
        P("layer", "row", "col"),
        P("layer", "row", "col"),
        P("row", "col"),
        P(),
        P(None, "col", None),
        P(None, "col", None),
    )
    return jax.shard_map(
        shards,
        mesh=mesh,
        in_specs=placed,
        out_specs=(P("layer", "row", "col"), P()),
        check_vma=False,
    )
```

```python
import jax
import jax.numpy as jnp
from jax import lax
from jax.sharding import PartitionSpec as P

TILE = 16
PANEL = 512
NPANEL = 4
DEG = 3
ITERS = 2


pad_gain = 8.0
bound_low = 0.1
bound_high = 1.9
restrict_scale = 0.25
prolong_scale = 0.5

highest = lax.Precision.HIGHEST
solve_precision = lax.Precision.HIGH
GRID_AXES = (("layer", 0), ("row", 1), ("col", 2))
ROW_AXES = ("layer", "row")


def axis_count(axis):
    names = axis if isinstance(axis, tuple) else (axis,)
    count = 1
    for name in names:
        count *= lax.axis_size(name)
    return count


def rims(field, axis, dim):
    size = field.shape[dim]
    head = lax.slice_in_dim(field, 0, 1, axis=dim)
    tail = lax.slice_in_dim(field, size - 1, size, axis=dim)
    if axis is None:
        return jnp.zeros_like(head), jnp.zeros_like(tail)
    count = axis_count(axis)
    place = list(range(count))
    if axis == ROW_AXES:
        layers, rows = lax.axis_size("layer"), lax.axis_size("row")
        place = [(b % layers) * rows + b // layers for b in range(count)]
    if count == 2:
        low = lax.axis_index(axis) == 0
        got = lax.ppermute(jnp.where(low, tail, head), axis, [(0, 1), (1, 0)])
        zero = jnp.zeros_like(got)
        return jnp.where(low, got, zero), jnp.where(low, zero, got)
    below = lax.ppermute(tail, axis, [(place[i], place[i + 1]) for i in range(count - 1)])
    above = lax.ppermute(head, axis, [(place[i + 1], place[i]) for i in range(count - 1)])
    return above, below


def neighbours(field, halo):
    out = []
    for (axis, dim), (above, below) in zip(GRID_AXES, halo):
        size = field.shape[dim]
        out.append(jnp.concatenate([lax.slice_in_dim(field, 1, size, axis=dim), above], axis=dim))
        out.append(jnp.concatenate([below, lax.slice_in_dim(field, 0, size - 1, axis=dim)], axis=dim))
    return out


def exchange(field):
    return [rims(field, axis, dim) for axis, dim in ((None, 0), (ROW_AXES, 1), ("col", 2))]


def apply_grid(field, near, weights, pad_term):
    result = pad_term * field
    for weight, other in zip(weights, near):
        result = result + weight * (field - other)
    return result


def smooth(resid, weights, pad_term, inverse):
    theta = (bound_high + bound_low) / 2.0
    delta = (bound_high - bound_low) / 2.0
    sigma = theta / delta
    rho = 1.0 / sigma
    change = inverse * resid / theta
    total = change
    for sweep in range(DEG - 1):
        remain = resid - apply_grid(total, neighbours(total, exchange(total)), weights, pad_term)
        rho_new = 1.0 / (2.0 * sigma - rho)
        change = rho_new * rho * change + 2.0 * rho_new / delta * inverse * remain
        total = total + change
        rho = rho_new
    return total


def all_sum(value):
    for axis, _ in GRID_AXES:
        count = lax.axis_size(axis)
        if count & (count - 1):
            value = lax.psum(value, axis)
            continue
        step = 1
        while step < count:
            value = value + lax.ppermute(value, axis, [(i, i ^ step) for i in range(count)])
            step *= 2
    return value


def share_tiles(tiles, own_rows, own_cols, flat_tiles):
    layers, rows, cols = (lax.axis_size(axis) for axis, _ in GRID_AXES)
    count = layers * rows * cols
    payload = jnp.broadcast_to(tiles.reshape(1, -1), (count, tiles.size))
    got = lax.all_to_all(payload, ("layer", "row", "col"), 0, 0, tiled=True)
    tile_cols = cols * own_cols
    tile_row, tile_col = flat_tiles // tile_cols, flat_tiles % tile_cols
    block = tile_row // own_rows
    device = ((block % layers) * rows + block // layers) * cols + tile_col // own_cols
    slot = (tile_row % own_rows) * own_cols + tile_col % own_cols
    pick_device = (device[:, None] == jnp.arange(count, dtype=jnp.int32)[None, :]).astype(jnp.float32)
    pick_slot = (slot[:, None] == jnp.arange(tiles.size, dtype=jnp.int32)[None, :]).astype(jnp.float32)
    return jnp.sum(jnp.dot(pick_device, got, precision=highest) * pick_slot, axis=1)


def swap_col(value):
    return lax.ppermute(value, "col", [(0, 1), (1, 0)])


def join_halves(mine, other, low):
    return jnp.where(low, jnp.concatenate([mine, other]), jnp.concatenate([other, mine]))


def coarse_pair(rhs, pivots, coupling):
    share = pivots.shape[1]
    low = lax.axis_index("col") == 0
    start = lax.axis_index("col") * share
    own = lambda vector: lax.dynamic_slice_in_dim(vector, start, share)
    other_half = lambda vector: lax.dynamic_slice_in_dim(vector, share - start, share)
    full = rhs[0]
    forward = [full]
    for section in range(1, NPANEL):
        piece = own(rhs[section]) - jnp.dot(coupling[section - 1], full, precision=solve_precision)
        full = join_halves(piece, swap_col(piece), low)
        forward.append(full)
    scaled = [jnp.dot(pivots[section], forward[section], precision=solve_precision) for section in range(NPANEL)]
    mine = scaled[NPANEL - 1]
    results = [None] * NPANEL
    for section in range(NPANEL - 2, 0, -1):
        partial = jnp.dot(mine, coupling[section], precision=solve_precision)
        got = swap_col(jnp.concatenate([other_half(partial), mine]))
        results[section + 1] = join_halves(mine, got[share:], low)
        mine = scaled[section] - (own(partial) + got[:share])
    partial = jnp.dot(mine, coupling[0], precision=solve_precision)
    got = swap_col(jnp.concatenate([partial, scaled[0], mine]))
    results[1] = join_halves(mine, got[PANEL + share:], low)
    first = join_halves(scaled[0], got[PANEL:PANEL + share], low)
    low_part = jnp.where(low, partial, got[:PANEL])
    high_part = jnp.where(low, got[:PANEL], partial)
    results[0] = first - (low_part + high_part)
    return jnp.stack(results)


def coarse_general(rhs, pivots, coupling):
    share = pivots.shape[1]
    start = lax.axis_index("col") * share
    full = rhs[0]
    forward = [full]
    for section in range(1, NPANEL):
        piece = lax.dynamic_slice_in_dim(rhs[section], start, share) - jnp.dot(
            coupling[section - 1], full, precision=solve_precision
        )
        full = lax.all_gather(piece, "col", axis=0, tiled=True)
        forward.append(full)
    scaled = [jnp.dot(pivots[section], forward[section], precision=solve_precision) for section in range(NPANEL)]
    results = [None] * NPANEL
    for section in range(NPANEL - 1, -1, -1):
        placed = lax.dynamic_update_slice_in_dim(jnp.zeros((PANEL,), jnp.float32), scaled[section], start, 0)
        if section < NPANEL - 1:
            later_rows = lax.dynamic_slice_in_dim(results[section + 1], start, share)
            placed = placed - jnp.dot(later_rows, coupling[section], precision=solve_precision)
        results[section] = lax.psum(placed, "col")
    return jnp.stack(results)


def expand(values, edge):
    inner = values[1:-1] if edge else values
    body = jnp.repeat(inner, TILE, axis=0)
    if edge:
        body = jnp.concatenate([values[:1], body, values[-1:]], axis=0)
    return body


def shards(sources, conduct, via_cond, via_map, pad_map, port_tile, pivots, coupling):
    layer_count = lax.axis_size("layer")
    vertical = via_cond * via_map.astype(jnp.float32)
    packed = lax.all_to_all(jnp.stack((conduct, vertical)), "layer", 2, 1, tiled=True)
    conduct, vertical = packed[0], packed[1]
    sources = lax.all_to_all(sources, "layer", 1, 0, tiled=True)
    local_layers, grid_rows, grid_cols = sources.shape
    pad_rows = lax.dynamic_slice_in_dim(pad_map, lax.axis_index("layer") * grid_rows, grid_rows, 0)
    row_halo = rims(conduct, ROW_AXES, 1)
    col_halo = rims(conduct, "col", 2)
    layer_halo = rims(vertical, None, 0)
    near_vert = neighbours(vertical, [layer_halo, row_halo, col_halo])
    near_plane = neighbours(conduct, [layer_halo, row_halo, col_halo])
    weights = (
        jnp.sqrt(vertical * near_vert[0]),
        jnp.sqrt(vertical * near_vert[1]),
        jnp.sqrt(conduct * near_plane[2]),
        jnp.sqrt(conduct * near_plane[3]),
        jnp.sqrt(conduct * near_plane[4]),
        jnp.sqrt(conduct * near_plane[5]),
    )
    top_layer = pad_gain * pad_rows.astype(jnp.float32)
    pad_term = jnp.concatenate(
        (jnp.zeros((local_layers - 1, grid_rows, grid_cols), jnp.float32), top_layer[None]), 0
    )
    diagonal = pad_term
    for weight in weights:
        diagonal = diagonal + weight
    inverse = 1.0 / diagonal

    col_count = lax.axis_size("col")
    tile_cols = grid_cols * col_count // TILE
    tile_rows = grid_rows * axis_count(ROW_AXES) // TILE
    own_rows = grid_rows // TILE
    own_cols = grid_cols // TILE
    first_row = (lax.axis_index("row") * layer_count + lax.axis_index("layer")) * own_rows
    first_col = lax.axis_index("col") * own_cols
    flat_tiles = port_tile.reshape(-1)
    ring_rows = first_row - 1 + jnp.arange(own_rows + 2, dtype=jnp.int32)
    ring_cols = first_col - 1 + jnp.arange(own_cols + 2, dtype=jnp.int32)
    ring_ok = ((ring_rows >= 0) & (ring_rows < tile_rows))[:, None] & ((ring_cols >= 0) & (ring_cols < tile_cols))[None, :]
    ring_ids = jnp.where(ring_ok, ring_rows[:, None] * tile_cols + ring_cols[None, :], -1).reshape(-1)
    scatter_ring = (ring_ids[:, None] == flat_tiles[None, :]).astype(jnp.float32)
    coarse = coarse_pair if col_count == 2 else coarse_general

    drop = None
    drop_near = None
    for outer in range(ITERS):
        if drop is None:
            resid = sources
        else:
            resid = sources - apply_grid(drop, drop_near, weights, pad_term)
        plane = jnp.sum(resid, axis=0)
        tiles = plane.reshape(own_rows, TILE, own_cols, TILE).sum(axis=(1, 3)).reshape(-1)
        rhs = share_tiles(tiles, own_rows, own_cols, flat_tiles).reshape(NPANEL, PANEL) * (restrict_scale / TILE)
        ports = coarse(rhs, pivots, coupling)
        tile_values = jnp.dot(scatter_ring, ports.reshape(-1), precision=highest).reshape(own_rows + 2, own_cols + 2)
        ring = expand(expand(tile_values, True).T, True).T * prolong_scale
        centre = ring[1:-1, 1:-1]
        lifted = jnp.broadcast_to(centre[None], (local_layers, grid_rows, grid_cols))
        total = smooth(resid, weights, pad_term, inverse)
        if outer == ITERS - 1:
            drop = (lifted if drop is None else drop + lifted) + total
            break
        lifted_near = [lifted, lifted]
        for part in (ring[2:, 1:-1], ring[:-2, 1:-1], ring[1:-1, 2:], ring[1:-1, :-2]):
            lifted_near.append(jnp.broadcast_to(part[None], (local_layers, grid_rows, grid_cols)))
        total_near = neighbours(total, exchange(total))
        if drop is None:
            drop = lifted + total
            drop_near = [a + b for a, b in zip(lifted_near, total_near)]
        else:
            drop = drop + lifted + total
            drop_near = [(d + a) + b for d, a, b in zip(drop_near, lifted_near, total_near)]
    drop = lax.all_to_all(drop, "layer", 0, 1, tiled=True)
    return (drop, ports)


def solution(mesh):
    placed = (
        P("layer", "row", "col"),
        P("layer", "row", "col"),
        P("layer", "row", "col"),
        P("layer", "row", "col"),
        P("row", "col"),
        P(),
        P(None, "col", None),
        P(None, "col", None),
    )
    return jax.shard_map(
        shards,
        mesh=mesh,
        in_specs=placed,
        out_specs=(P("layer", "row", "col"), P()),
        check_vma=False,
    )
```

```python
import jax
import jax.numpy as jnp
from jax import lax
from jax.sharding import PartitionSpec as P

TILE = 16
PANEL = 512
NPANEL = 4
DEG = 3
ITERS = 2


pad_gain = 8.0
bound_low = 0.1
bound_high = 1.9
restrict_scale = 0.25
prolong_scale = 0.5

highest = lax.Precision.HIGHEST
solve_precision = lax.Precision.HIGH
GRID_AXES = (("layer", 0), ("row", 1), ("col", 2))
ROW_AXES = ("layer", "row")


def axis_count(axis):
    names = axis if isinstance(axis, tuple) else (axis,)
    count = 1
    for name in names:
        count *= lax.axis_size(name)
    return count


def rims(field, axis, dim):
    size = field.shape[dim]
    head = lax.slice_in_dim(field, 0, 1, axis=dim)
    tail = lax.slice_in_dim(field, size - 1, size, axis=dim)
    if axis is None:
        return jnp.zeros_like(head), jnp.zeros_like(tail)
    count = axis_count(axis)
    place = list(range(count))
    if axis == ROW_AXES:
        layers, rows = lax.axis_size("layer"), lax.axis_size("row")
        place = [(b % layers) * rows + b // layers for b in range(count)]
    if count == 2:
        low = lax.axis_index(axis) == 0
        got = lax.ppermute(jnp.where(low, tail, head), axis, [(0, 1), (1, 0)])
        zero = jnp.zeros_like(got)
        return jnp.where(low, got, zero), jnp.where(low, zero, got)
    below = lax.ppermute(tail, axis, [(place[i], place[i + 1]) for i in range(count - 1)])
    above = lax.ppermute(head, axis, [(place[i + 1], place[i]) for i in range(count - 1)])
    return above, below


def neighbours(field, halo):
    out = []
    for (axis, dim), (above, below) in zip(GRID_AXES, halo):
        size = field.shape[dim]
        out.append(jnp.concatenate([lax.slice_in_dim(field, 1, size, axis=dim), above], axis=dim))
        out.append(jnp.concatenate([below, lax.slice_in_dim(field, 0, size - 1, axis=dim)], axis=dim))
    return out


def exchange(field):
    return [rims(field, axis, dim) for axis, dim in ((None, 0), (ROW_AXES, 1), ("col", 2))]


def apply_grid(field, near, weights, pad_term):
    result = pad_term * field
    for weight, other in zip(weights, near):
        result = result + weight * (field - other)
    return result


def smooth(resid, weights, pad_term, inverse):
    theta = (bound_high + bound_low) / 2.0
    delta = (bound_high - bound_low) / 2.0
    sigma = theta / delta
    rho = 1.0 / sigma
    change = inverse * resid / theta
    total = change
    for sweep in range(DEG - 1):
        remain = resid - apply_grid(total, neighbours(total, exchange(total)), weights, pad_term)
        rho_new = 1.0 / (2.0 * sigma - rho)
        change = rho_new * rho * change + 2.0 * rho_new / delta * inverse * remain
        total = total + change
        rho = rho_new
    return total


def all_sum(value):
    for axis, _ in GRID_AXES:
        count = lax.axis_size(axis)
        if count & (count - 1):
            value = lax.psum(value, axis)
            continue
        step = 1
        while step < count:
            value = value + lax.ppermute(value, axis, [(i, i ^ step) for i in range(count)])
            step *= 2
    return value


def share_tiles(tiles, own_rows, own_cols, flat_tiles):
    layers, rows, cols = (lax.axis_size(axis) for axis, _ in GRID_AXES)
    count = layers * rows * cols
    payload = jnp.broadcast_to(tiles.reshape(1, -1), (count, tiles.size))
    got = lax.all_to_all(payload, ("layer", "row", "col"), 0, 0, tiled=True)
    tile_cols = cols * own_cols
    tile_row, tile_col = flat_tiles // tile_cols, flat_tiles % tile_cols
    block = tile_row // own_rows
    device = ((block % layers) * rows + block // layers) * cols + tile_col // own_cols
    slot = (tile_row % own_rows) * own_cols + tile_col % own_cols
    pick_device = (device[:, None] == jnp.arange(count, dtype=jnp.int32)[None, :]).astype(jnp.float32)
    pick_slot = (slot[:, None] == jnp.arange(tiles.size, dtype=jnp.int32)[None, :]).astype(jnp.float32)
    return jnp.sum(jnp.dot(pick_device, got, precision=highest) * pick_slot, axis=1)


def swap_col(value):
    return lax.ppermute(value, "col", [(0, 1), (1, 0)])


def join_halves(mine, other, low):
    return jnp.where(low, jnp.concatenate([mine, other]), jnp.concatenate([other, mine]))


def coarse_pair(rhs, pivots, coupling, tie=None):
    share = pivots.shape[1]
    low = lax.axis_index("col") == 0
    start = lax.axis_index("col") * share
    own = lambda vector: lax.dynamic_slice_in_dim(vector, start, share)
    other_half = lambda vector: lax.dynamic_slice_in_dim(vector, share - start, share)
    full = rhs[0]
    forward = [full]
    for section in range(1, NPANEL):
        piece = own(rhs[section]) - jnp.dot(coupling[section - 1], full, precision=solve_precision)
        full = join_halves(piece, swap_col(piece), low)
        forward.append(full)
    scaled = [jnp.dot(pivots[section], forward[section], precision=solve_precision) for section in range(NPANEL)]
    mine = scaled[NPANEL - 1]
    results = [None] * NPANEL
    if tie is not None:
        mine, _ = lax.optimization_barrier((mine, tie))
    for section in range(NPANEL - 2, 0, -1):
        partial = jnp.dot(mine, coupling[section], precision=solve_precision)
        got = swap_col(jnp.concatenate([other_half(partial), mine]))
        results[section + 1] = join_halves(mine, got[share:], low)
        mine = scaled[section] - (own(partial) + got[:share])
    partial = jnp.dot(mine, coupling[0], precision=solve_precision)
    got = swap_col(jnp.concatenate([partial, scaled[0], mine]))
    results[1] = join_halves(mine, got[PANEL + share:], low)
    first = join_halves(scaled[0], got[PANEL:PANEL + share], low)
    low_part = jnp.where(low, partial, got[:PANEL])
    high_part = jnp.where(low, got[:PANEL], partial)
    results[0] = first - (low_part + high_part)
    return jnp.stack(results)


def coarse_general(rhs, pivots, coupling):
    share = pivots.shape[1]
    start = lax.axis_index("col") * share
    full = rhs[0]
    forward = [full]
    for section in range(1, NPANEL):
        piece = lax.dynamic_slice_in_dim(rhs[section], start, share) - jnp.dot(
            coupling[section - 1], full, precision=solve_precision
        )
        full = lax.all_gather(piece, "col", axis=0, tiled=True)
        forward.append(full)
    scaled = [jnp.dot(pivots[section], forward[section], precision=solve_precision) for section in range(NPANEL)]
    results = [None] * NPANEL
    for section in range(NPANEL - 1, -1, -1):
        placed = lax.dynamic_update_slice_in_dim(jnp.zeros((PANEL,), jnp.float32), scaled[section], start, 0)
        if section < NPANEL - 1:
            later_rows = lax.dynamic_slice_in_dim(results[section + 1], start, share)
            placed = placed - jnp.dot(later_rows, coupling[section], precision=solve_precision)
        results[section] = lax.psum(placed, "col")
    return jnp.stack(results)


def expand(values, edge):
    inner = values[1:-1] if edge else values
    body = jnp.repeat(inner, TILE, axis=0)
    if edge:
        body = jnp.concatenate([values[:1], body, values[-1:]], axis=0)
    return body


def shards(sources, conduct, via_cond, via_map, pad_map, port_tile, pivots, coupling):
    layer_count = lax.axis_size("layer")
    vertical = via_cond * via_map.astype(jnp.float32)
    given_rows = sources.shape[1] // TILE
    given_cols = sources.shape[2] // TILE
    given_tile_cols = given_cols * lax.axis_size("col")
    given_ids = (
        (lax.axis_index("row") * given_rows + jnp.arange(given_rows, dtype=jnp.int32))[:, None] * given_tile_cols
        + (lax.axis_index("col") * given_cols + jnp.arange(given_cols, dtype=jnp.int32))[None, :]
    ).reshape(-1)
    given_pick = (given_ids[:, None] == port_tile.reshape(-1)[None, :]).astype(jnp.float32)
    packed = lax.all_to_all(jnp.stack((conduct, vertical)), "layer", 2, 1, tiled=True)
    conduct, vertical = packed[0], packed[1]
    sources = lax.all_to_all(sources, "layer", 1, 0, tiled=True)
    local_layers, grid_rows, grid_cols = sources.shape
    pad_rows = lax.dynamic_slice_in_dim(pad_map, lax.axis_index("layer") * grid_rows, grid_rows, 0)
    row_halo = rims(conduct, ROW_AXES, 1)
    col_halo = rims(conduct, "col", 2)
    layer_halo = rims(vertical, None, 0)
    near_vert = neighbours(vertical, [layer_halo, row_halo, col_halo])
    near_plane = neighbours(conduct, [layer_halo, row_halo, col_halo])
    weights = (
        jnp.sqrt(vertical * near_vert[0]),
        jnp.sqrt(vertical * near_vert[1]),
        jnp.sqrt(conduct * near_plane[2]),
        jnp.sqrt(conduct * near_plane[3]),
        jnp.sqrt(conduct * near_plane[4]),
        jnp.sqrt(conduct * near_plane[5]),
    )
    top_layer = pad_gain * pad_rows.astype(jnp.float32)
    pad_term = jnp.concatenate(
        (jnp.zeros((local_layers - 1, grid_rows, grid_cols), jnp.float32), top_layer[None]), 0
    )
    diagonal = pad_term
    for weight in weights:
        diagonal = diagonal + weight
    inverse = 1.0 / diagonal

    col_count = lax.axis_size("col")
    tile_cols = grid_cols * col_count // TILE
    tile_rows = grid_rows * axis_count(ROW_AXES) // TILE
    own_rows = grid_rows // TILE
    own_cols = grid_cols // TILE
    first_row = (lax.axis_index("row") * layer_count + lax.axis_index("layer")) * own_rows
    first_col = lax.axis_index("col") * own_cols
    flat_tiles = port_tile.reshape(-1)
    ring_rows = first_row - 1 + jnp.arange(own_rows + 2, dtype=jnp.int32)
    ring_cols = first_col - 1 + jnp.arange(own_cols + 2, dtype=jnp.int32)
    ring_ok = ((ring_rows >= 0) & (ring_rows < tile_rows))[:, None] & ((ring_cols >= 0) & (ring_cols < tile_cols))[None, :]
    ring_ids = jnp.where(ring_ok, ring_rows[:, None] * tile_cols + ring_cols[None, :], -1).reshape(-1)
    scatter_ring = (ring_ids[:, None] == flat_tiles[None, :]).astype(jnp.float32)
    coarse = coarse_pair if col_count == 2 else coarse_general

    drop = None
    drop_near = None
    for outer in range(ITERS):
        if drop is None:
            resid = sources
        else:
            resid = sources - apply_grid(drop, drop_near, weights, pad_term)
        plane = jnp.sum(resid, axis=0)
        tiles = plane.reshape(own_rows, TILE, own_cols, TILE).sum(axis=(1, 3)).reshape(-1)
        rhs = share_tiles(tiles, own_rows, own_cols, flat_tiles).reshape(NPANEL, PANEL) * (restrict_scale / TILE)
        total = smooth(resid, weights, pad_term, inverse)
        if col_count == 2 and outer == ITERS - 1 and drop is not None:
            ports = coarse_pair(rhs, pivots, coupling, total)
        else:
            ports = coarse(rhs, pivots, coupling)
        tile_values = jnp.dot(scatter_ring, ports.reshape(-1), precision=highest).reshape(own_rows + 2, own_cols + 2)
        ring = expand(expand(tile_values, True).T, True).T * prolong_scale
        centre = ring[1:-1, 1:-1]
        lifted = jnp.broadcast_to(centre[None], (local_layers, grid_rows, grid_cols))
        if outer == ITERS - 1 and drop is not None:
            both = lax.all_to_all(jnp.stack((drop, total)), "layer", 1, 2, tiled=True)
            given_values = jnp.dot(given_pick, ports.reshape(-1), precision=highest).reshape(given_rows, given_cols)
            given_field = jnp.repeat(jnp.repeat(given_values, TILE, axis=0), TILE, axis=1) * prolong_scale
            given_lifted = jnp.broadcast_to(given_field[None], both.shape[1:])
            return ((both[0] + given_lifted) + both[1], ports)
        if outer == ITERS - 1:
            drop = (lifted if drop is None else drop + lifted) + total
            break
        lifted_near = [lifted, lifted]
        for part in (ring[2:, 1:-1], ring[:-2, 1:-1], ring[1:-1, 2:], ring[1:-1, :-2]):
            lifted_near.append(jnp.broadcast_to(part[None], (local_layers, grid_rows, grid_cols)))
        total_near = neighbours(total, exchange(total))
        if drop is None:
            drop = lifted + total
            drop_near = [a + b for a, b in zip(lifted_near, total_near)]
        else:
            drop = drop + lifted + total
            drop_near = [(d + a) + b for d, a, b in zip(drop_near, lifted_near, total_near)]
    drop = lax.all_to_all(drop, "layer", 0, 1, tiled=True)
    return (drop, ports)


def solution(mesh):
    placed = (
        P("layer", "row", "col"),
        P("layer", "row", "col"),
        P("layer", "row", "col"),
        P("layer", "row", "col"),
        P("row", "col"),
        P(),
        P(None, "col", None),
        P(None, "col", None),
    )
    return jax.shard_map(
        shards,
        mesh=mesh,
        in_specs=placed,
        out_specs=(P("layer", "row", "col"), P()),
        check_vma=False,
    )
```

```python
import jax
import jax.numpy as jnp
from jax import lax
from jax.sharding import PartitionSpec as P

TILE = 16
PANEL = 512
NPANEL = 4
DEG = 3
ITERS = 2


pad_gain = 8.0
bound_low = 0.1
bound_high = 1.9
restrict_scale = 0.25
prolong_scale = 0.5

highest = lax.Precision.HIGHEST
solve_precision = lax.Precision.HIGH
GRID_AXES = (("layer", 0), ("row", 1), ("col", 2))
ROW_AXES = ("layer", "row")


def axis_count(axis):
    names = axis if isinstance(axis, tuple) else (axis,)
    count = 1
    for name in names:
        count *= lax.axis_size(name)
    return count


def rims(field, axis, dim):
    size = field.shape[dim]
    head = lax.slice_in_dim(field, 0, 1, axis=dim)
    tail = lax.slice_in_dim(field, size - 1, size, axis=dim)
    if axis is None:
        return jnp.zeros_like(head), jnp.zeros_like(tail)
    count = axis_count(axis)
    place = list(range(count))
    if axis == ROW_AXES:
        layers, rows = lax.axis_size("layer"), lax.axis_size("row")
        place = [(b % layers) * rows + b // layers for b in range(count)]
    if count == 2:
        low = lax.axis_index(axis) == 0
        got = lax.ppermute(jnp.where(low, tail, head), axis, [(0, 1), (1, 0)])
        zero = jnp.zeros_like(got)
        return jnp.where(low, got, zero), jnp.where(low, zero, got)
    below = lax.ppermute(tail, axis, [(place[i], place[i + 1]) for i in range(count - 1)])
    above = lax.ppermute(head, axis, [(place[i + 1], place[i]) for i in range(count - 1)])
    return above, below


def neighbours(field, halo):
    out = []
    for (axis, dim), (above, below) in zip(GRID_AXES, halo):
        size = field.shape[dim]
        out.append(jnp.concatenate([lax.slice_in_dim(field, 1, size, axis=dim), above], axis=dim))
        out.append(jnp.concatenate([below, lax.slice_in_dim(field, 0, size - 1, axis=dim)], axis=dim))
    return out


def exchange(field):
    return [rims(field, axis, dim) for axis, dim in ((None, 0), (ROW_AXES, 1), ("col", 2))]


def apply_grid(field, near, weights, pad_term):
    result = pad_term * field
    for weight, other in zip(weights, near):
        result = result + weight * (field - other)
    return result


def smooth(resid, weights, pad_term, inverse):
    theta = (bound_high + bound_low) / 2.0
    delta = (bound_high - bound_low) / 2.0
    sigma = theta / delta
    rho = 1.0 / sigma
    change = inverse * resid / theta
    total = change
    for sweep in range(DEG - 1):
        remain = resid - apply_grid(total, neighbours(total, exchange(total)), weights, pad_term)
        rho_new = 1.0 / (2.0 * sigma - rho)
        change = rho_new * rho * change + 2.0 * rho_new / delta * inverse * remain
        total = total + change
        rho = rho_new
    return total


def all_sum(value):
    for axis, _ in GRID_AXES:
        count = lax.axis_size(axis)
        if count & (count - 1):
            value = lax.psum(value, axis)
            continue
        step = 1
        while step < count:
            value = value + lax.ppermute(value, axis, [(i, i ^ step) for i in range(count)])
            step *= 2
    return value


def share_tiles(tiles, own_rows, own_cols, flat_tiles):
    layers, rows, cols = (lax.axis_size(axis) for axis, _ in GRID_AXES)
    count = layers * rows * cols
    payload = jnp.broadcast_to(tiles.reshape(1, -1), (count, tiles.size))
    got = lax.all_to_all(payload, ("layer", "row", "col"), 0, 0, tiled=True)
    tile_cols = cols * own_cols
    tile_row, tile_col = flat_tiles // tile_cols, flat_tiles % tile_cols
    block = tile_row // own_rows
    device = ((block % layers) * rows + block // layers) * cols + tile_col // own_cols
    slot = (tile_row % own_rows) * own_cols + tile_col % own_cols
    pick_device = (device[:, None] == jnp.arange(count, dtype=jnp.int32)[None, :]).astype(jnp.float32)
    pick_slot = (slot[:, None] == jnp.arange(tiles.size, dtype=jnp.int32)[None, :]).astype(jnp.float32)
    return jnp.sum(jnp.dot(pick_device, got, precision=highest) * pick_slot, axis=1)


def swap_col(value):
    return lax.ppermute(value, "col", [(0, 1), (1, 0)])


def join_halves(mine, other, low):
    return jnp.where(low, jnp.concatenate([mine, other]), jnp.concatenate([other, mine]))


def coarse_pair(rhs, pivots, coupling, tie=None):
    share = pivots.shape[1]
    low = lax.axis_index("col") == 0
    start = lax.axis_index("col") * share
    own = lambda vector: lax.dynamic_slice_in_dim(vector, start, share)
    other_half = lambda vector: lax.dynamic_slice_in_dim(vector, share - start, share)
    full = rhs[0]
    forward = [full]
    for section in range(1, NPANEL):
        piece = own(rhs[section]) - jnp.dot(coupling[section - 1], full, precision=solve_precision)
        full = join_halves(piece, swap_col(piece), low)
        forward.append(full)
    scaled = [jnp.dot(pivots[section], forward[section], precision=solve_precision) for section in range(NPANEL)]
    mine = scaled[NPANEL - 1]
    results = [None] * NPANEL
    if tie is not None:
        mine, _ = lax.optimization_barrier((mine, tie))
    for section in range(NPANEL - 2, 0, -1):
        partial = jnp.dot(mine, coupling[section], precision=solve_precision)
        got = swap_col(jnp.concatenate([other_half(partial), mine]))
        results[section + 1] = join_halves(mine, got[share:], low)
        mine = scaled[section] - (own(partial) + got[:share])
    partial = jnp.dot(mine, coupling[0], precision=solve_precision)
    got = swap_col(jnp.concatenate([partial, scaled[0], mine]))
    results[1] = join_halves(mine, got[PANEL + share:], low)
    first = join_halves(scaled[0], got[PANEL:PANEL + share], low)
    low_part = jnp.where(low, partial, got[:PANEL])
    high_part = jnp.where(low, got[:PANEL], partial)
    results[0] = first - (low_part + high_part)
    return jnp.stack(results)


def coarse_general(rhs, pivots, coupling):
    share = pivots.shape[1]
    start = lax.axis_index("col") * share
    full = rhs[0]
    forward = [full]
    for section in range(1, NPANEL):
        piece = lax.dynamic_slice_in_dim(rhs[section], start, share) - jnp.dot(
            coupling[section - 1], full, precision=solve_precision
        )
        full = lax.all_gather(piece, "col", axis=0, tiled=True)
        forward.append(full)
    scaled = [jnp.dot(pivots[section], forward[section], precision=solve_precision) for section in range(NPANEL)]
    results = [None] * NPANEL
    for section in range(NPANEL - 1, -1, -1):
        placed = lax.dynamic_update_slice_in_dim(jnp.zeros((PANEL,), jnp.float32), scaled[section], start, 0)
        if section < NPANEL - 1:
            later_rows = lax.dynamic_slice_in_dim(results[section + 1], start, share)
            placed = placed - jnp.dot(later_rows, coupling[section], precision=solve_precision)
        results[section] = lax.psum(placed, "col")
    return jnp.stack(results)


def expand(values, edge):
    inner = values[1:-1] if edge else values
    body = jnp.repeat(inner, TILE, axis=0)
    if edge:
        body = jnp.concatenate([values[:1], body, values[-1:]], axis=0)
    return body


def shards(sources, conduct, via_cond, via_map, pad_map, port_tile, pivots, coupling):
    layer_count = lax.axis_size("layer")
    vertical = via_cond * via_map.astype(jnp.float32)
    given_rows = sources.shape[1] // TILE
    given_cols = sources.shape[2] // TILE
    given_tile_cols = given_cols * lax.axis_size("col")
    given_ids = (
        (lax.axis_index("row") * given_rows + jnp.arange(given_rows, dtype=jnp.int32))[:, None] * given_tile_cols
        + (lax.axis_index("col") * given_cols + jnp.arange(given_cols, dtype=jnp.int32))[None, :]
    ).reshape(-1)
    given_pick = (given_ids[:, None] == port_tile.reshape(-1)[None, :]).astype(jnp.float32)
    packed = lax.all_to_all(jnp.stack((conduct, vertical)), "layer", 2, 1, tiled=True)
    conduct, vertical = packed[0], packed[1]
    sources = lax.all_to_all(sources, "layer", 1, 0, tiled=True)
    local_layers, grid_rows, grid_cols = sources.shape
    pad_rows = lax.dynamic_slice_in_dim(pad_map, lax.axis_index("layer") * grid_rows, grid_rows, 0)
    row_halo = rims(conduct, ROW_AXES, 1)
    col_halo = rims(conduct, "col", 2)
    layer_halo = rims(vertical, None, 0)
    near_vert = neighbours(vertical, [layer_halo, row_halo, col_halo])
    near_plane = neighbours(conduct, [layer_halo, row_halo, col_halo])
    weights = (
        jnp.sqrt(vertical * near_vert[0]),
        jnp.sqrt(vertical * near_vert[1]),
        jnp.sqrt(conduct * near_plane[2]),
        jnp.sqrt(conduct * near_plane[3]),
        jnp.sqrt(conduct * near_plane[4]),
        jnp.sqrt(conduct * near_plane[5]),
    )
    top_layer = pad_gain * pad_rows.astype(jnp.float32)
    pad_term = jnp.concatenate(
        (jnp.zeros((local_layers - 1, grid_rows, grid_cols), jnp.float32), top_layer[None]), 0
    )
    diagonal = pad_term
    for weight in weights:
        diagonal = diagonal + weight
    inverse = 1.0 / diagonal

    col_count = lax.axis_size("col")
    tile_cols = grid_cols * col_count // TILE
    tile_rows = grid_rows * axis_count(ROW_AXES) // TILE
    own_rows = grid_rows // TILE
    own_cols = grid_cols // TILE
    first_row = (lax.axis_index("row") * layer_count + lax.axis_index("layer")) * own_rows
    first_col = lax.axis_index("col") * own_cols
    flat_tiles = port_tile.reshape(-1)
    ring_rows = first_row - 1 + jnp.arange(own_rows + 2, dtype=jnp.int32)
    ring_cols = first_col - 1 + jnp.arange(own_cols + 2, dtype=jnp.int32)
    ring_ok = ((ring_rows >= 0) & (ring_rows < tile_rows))[:, None] & ((ring_cols >= 0) & (ring_cols < tile_cols))[None, :]
    ring_ids = jnp.where(ring_ok, ring_rows[:, None] * tile_cols + ring_cols[None, :], -1).reshape(-1)
    scatter_ring = (ring_ids[:, None] == flat_tiles[None, :]).astype(jnp.float32)
    coarse = coarse_pair if col_count == 2 else coarse_general

    drop = None
    drop_near = None
    for outer in range(ITERS):
        if drop is None:
            resid = sources
        else:
            resid = sources - apply_grid(drop, drop_near, weights, pad_term)
        plane = jnp.sum(resid, axis=0)
        tiles = plane.reshape(own_rows, TILE, own_cols, TILE).sum(axis=(1, 3)).reshape(-1)
        rhs = share_tiles(tiles, own_rows, own_cols, flat_tiles).reshape(NPANEL, PANEL) * (restrict_scale / TILE)
        total = smooth(resid, weights, pad_term, inverse)
        if col_count == 2:
            ports = coarse_pair(rhs, pivots, coupling, total)
        else:
            ports = coarse(rhs, pivots, coupling)
        tile_values = jnp.dot(scatter_ring, ports.reshape(-1), precision=highest).reshape(own_rows + 2, own_cols + 2)
        ring = expand(expand(tile_values, True).T, True).T * prolong_scale
        centre = ring[1:-1, 1:-1]
        lifted = jnp.broadcast_to(centre[None], (local_layers, grid_rows, grid_cols))
        if outer == ITERS - 1 and drop is not None:
            both = lax.all_to_all(jnp.stack((drop, total)), "layer", 1, 2, tiled=True)
            given_values = jnp.dot(given_pick, ports.reshape(-1), precision=highest).reshape(given_rows, given_cols)
            given_field = jnp.repeat(jnp.repeat(given_values, TILE, axis=0), TILE, axis=1) * prolong_scale
            given_lifted = jnp.broadcast_to(given_field[None], both.shape[1:])
            return ((both[0] + given_lifted) + both[1], ports)
        if outer == ITERS - 1:
            drop = (lifted if drop is None else drop + lifted) + total
            break
        lifted_near = [lifted, lifted]
        for part in (ring[2:, 1:-1], ring[:-2, 1:-1], ring[1:-1, 2:], ring[1:-1, :-2]):
            lifted_near.append(jnp.broadcast_to(part[None], (local_layers, grid_rows, grid_cols)))
        total_near = neighbours(total, exchange(total))
        if drop is None:
            drop = lifted + total
            drop_near = [a + b for a, b in zip(lifted_near, total_near)]
        else:
            drop = drop + lifted + total
            drop_near = [(d + a) + b for d, a, b in zip(drop_near, lifted_near, total_near)]
    drop = lax.all_to_all(drop, "layer", 0, 1, tiled=True)
    return (drop, ports)


def solution(mesh):
    placed = (
        P("layer", "row", "col"),
        P("layer", "row", "col"),
        P("layer", "row", "col"),
        P("layer", "row", "col"),
        P("row", "col"),
        P(),
        P(None, "col", None),
        P(None, "col", None),
    )
    return jax.shard_map(
        shards,
        mesh=mesh,
        in_specs=placed,
        out_specs=(P("layer", "row", "col"), P()),
        check_vma=False,
    )
```

```python
import jax
import jax.numpy as jnp
from jax import lax
from jax.sharding import PartitionSpec as P

TILE = 16
PANEL = 512
NPANEL = 4
DEG = 3
ITERS = 2


pad_gain = 8.0
bound_low = 0.1
bound_high = 1.9
restrict_scale = 0.25
prolong_scale = 0.5

highest = lax.Precision.HIGHEST
solve_precision = lax.Precision.HIGH
GRID_AXES = (("layer", 0), ("row", 1), ("col", 2))
ROW_AXES = ("layer", "row")


def axis_count(axis):
    names = axis if isinstance(axis, tuple) else (axis,)
    count = 1
    for name in names:
        count *= lax.axis_size(name)
    return count


def rims(field, axis, dim):
    size = field.shape[dim]
    head = lax.slice_in_dim(field, 0, 1, axis=dim)
    tail = lax.slice_in_dim(field, size - 1, size, axis=dim)
    if axis is None:
        return jnp.zeros_like(head), jnp.zeros_like(tail)
    count = axis_count(axis)
    place = list(range(count))
    if axis == ROW_AXES:
        layers, rows = lax.axis_size("layer"), lax.axis_size("row")
        place = [(b % layers) * rows + b // layers for b in range(count)]
    if count == 2:
        low = lax.axis_index(axis) == 0
        got = lax.ppermute(jnp.where(low, tail, head), axis, [(0, 1), (1, 0)])
        zero = jnp.zeros_like(got)
        return jnp.where(low, got, zero), jnp.where(low, zero, got)
    below = lax.ppermute(tail, axis, [(place[i], place[i + 1]) for i in range(count - 1)])
    above = lax.ppermute(head, axis, [(place[i + 1], place[i]) for i in range(count - 1)])
    return above, below


def neighbours(field, halo):
    out = []
    for (axis, dim), (above, below) in zip(GRID_AXES, halo):
        size = field.shape[dim]
        out.append(jnp.concatenate([lax.slice_in_dim(field, 1, size, axis=dim), above], axis=dim))
        out.append(jnp.concatenate([below, lax.slice_in_dim(field, 0, size - 1, axis=dim)], axis=dim))
    return out


def exchange(field):
    return [rims(field, axis, dim) for axis, dim in ((None, 0), (ROW_AXES, 1), ("col", 2))]


def apply_grid(field, near, weights, pad_term):
    result = pad_term * field
    for weight, other in zip(weights, near):
        result = result + weight * (field - other)
    return result


def smooth(resid, weights, pad_term, inverse):
    theta = (bound_high + bound_low) / 2.0
    delta = (bound_high - bound_low) / 2.0
    sigma = theta / delta
    rho = 1.0 / sigma
    change = inverse * resid / theta
    total = change
    for sweep in range(DEG - 1):
        remain = resid - apply_grid(total, neighbours(total, exchange(total)), weights, pad_term)
        rho_new = 1.0 / (2.0 * sigma - rho)
        change = rho_new * rho * change + 2.0 * rho_new / delta * inverse * remain
        total = total + change
        rho = rho_new
    return total


def all_sum(value):
    for axis, _ in GRID_AXES:
        count = lax.axis_size(axis)
        if count & (count - 1):
            value = lax.psum(value, axis)
            continue
        step = 1
        while step < count:
            value = value + lax.ppermute(value, axis, [(i, i ^ step) for i in range(count)])
            step *= 2
    return value


def share_tiles(tiles, own_rows, own_cols, flat_tiles):
    layers, rows, cols = (lax.axis_size(axis) for axis, _ in GRID_AXES)
    count = layers * rows * cols
    payload = jnp.broadcast_to(tiles.reshape(1, -1), (count, tiles.size))
    got = lax.all_to_all(payload, ("layer", "row", "col"), 0, 0, tiled=True)
    tile_cols = cols * own_cols
    tile_row, tile_col = flat_tiles // tile_cols, flat_tiles % tile_cols
    block = tile_row // own_rows
    device = ((block % layers) * rows + block // layers) * cols + tile_col // own_cols
    slot = (tile_row % own_rows) * own_cols + tile_col % own_cols
    pick_device = (device[:, None] == jnp.arange(count, dtype=jnp.int32)[None, :]).astype(jnp.float32)
    pick_slot = (slot[:, None] == jnp.arange(tiles.size, dtype=jnp.int32)[None, :]).astype(jnp.float32)
    return jnp.sum(jnp.dot(pick_device, got, precision=highest) * pick_slot, axis=1)


def swap_col(value):
    return lax.ppermute(value, "col", [(0, 1), (1, 0)])


def join_halves(mine, other, low):
    return jnp.where(low, jnp.concatenate([mine, other]), jnp.concatenate([other, mine]))


def coarse_pair(rhs, pivots, coupling, tie=None):
    share = pivots.shape[1]
    low = lax.axis_index("col") == 0
    start = lax.axis_index("col") * share
    own = lambda vector: lax.dynamic_slice_in_dim(vector, start, share)
    other_half = lambda vector: lax.dynamic_slice_in_dim(vector, share - start, share)
    full = rhs[0]
    forward = [full]
    for section in range(1, NPANEL):
        piece = own(rhs[section]) - jnp.dot(coupling[section - 1], full, precision=solve_precision)
        full = join_halves(piece, swap_col(piece), low)
        forward.append(full)
    scaled = [jnp.dot(pivots[section], forward[section], precision=solve_precision) for section in range(NPANEL)]
    mine = scaled[NPANEL - 1]
    results = [None] * NPANEL
    if tie is not None:
        mine, _ = lax.optimization_barrier((mine, tie))
    for section in range(NPANEL - 2, 0, -1):
        partial = jnp.dot(mine, coupling[section], precision=solve_precision)
        got = swap_col(jnp.concatenate([other_half(partial), mine]))
        results[section + 1] = join_halves(mine, got[share:], low)
        mine = scaled[section] - (own(partial) + got[:share])
    partial = jnp.dot(mine, coupling[0], precision=solve_precision)
    got = swap_col(jnp.concatenate([partial, scaled[0], mine]))
    results[1] = join_halves(mine, got[PANEL + share:], low)
    first = join_halves(scaled[0], got[PANEL:PANEL + share], low)
    low_part = jnp.where(low, partial, got[:PANEL])
    high_part = jnp.where(low, got[:PANEL], partial)
    results[0] = first - (low_part + high_part)
    return jnp.stack(results)


def coarse_general(rhs, pivots, coupling):
    share = pivots.shape[1]
    start = lax.axis_index("col") * share
    full = rhs[0]
    forward = [full]
    for section in range(1, NPANEL):
        piece = lax.dynamic_slice_in_dim(rhs[section], start, share) - jnp.dot(
            coupling[section - 1], full, precision=solve_precision
        )
        full = lax.all_gather(piece, "col", axis=0, tiled=True)
        forward.append(full)
    scaled = [jnp.dot(pivots[section], forward[section], precision=solve_precision) for section in range(NPANEL)]
    results = [None] * NPANEL
    for section in range(NPANEL - 1, -1, -1):
        placed = lax.dynamic_update_slice_in_dim(jnp.zeros((PANEL,), jnp.float32), scaled[section], start, 0)
        if section < NPANEL - 1:
            later_rows = lax.dynamic_slice_in_dim(results[section + 1], start, share)
            placed = placed - jnp.dot(later_rows, coupling[section], precision=solve_precision)
        results[section] = lax.psum(placed, "col")
    return jnp.stack(results)


def expand(values, edge):
    inner = values[1:-1] if edge else values
    body = jnp.repeat(inner, TILE, axis=0)
    if edge:
        body = jnp.concatenate([values[:1], body, values[-1:]], axis=0)
    return body


def shards(sources, conduct, via_cond, via_map, pad_map, port_tile, pivots, coupling):
    layer_count = lax.axis_size("layer")
    vertical = via_cond * via_map.astype(jnp.float32)
    given_rows = sources.shape[1] // TILE
    given_cols = sources.shape[2] // TILE
    given_tile_cols = given_cols * lax.axis_size("col")
    given_ids = (
        (lax.axis_index("row") * given_rows + jnp.arange(given_rows, dtype=jnp.int32))[:, None] * given_tile_cols
        + (lax.axis_index("col") * given_cols + jnp.arange(given_cols, dtype=jnp.int32))[None, :]
    ).reshape(-1)
    given_pick = (given_ids[:, None] == port_tile.reshape(-1)[None, :]).astype(jnp.float32)
    start_rhs = None
    pair_cols = lax.axis_size("col")
    if pair_cols == 2:
        layer_n, row_n = layer_count, lax.axis_size("row")
        start_plane = jnp.sum(sources, axis=0)
        start_tiles = start_plane.reshape(given_rows, TILE, given_cols, TILE).sum(axis=(1, 3)).reshape(-1)
        count = layer_n * row_n * pair_cols
        got = lax.all_to_all(jnp.broadcast_to(start_tiles[None], (count, start_tiles.size)), ("layer", "row", "col"), 0, 0, tiled=True)
        flat = port_tile.reshape(-1)
        tr, tc = flat // given_tile_cols, flat % given_tile_cols
        devices = jnp.arange(count, dtype=jnp.int32)
        same = ((devices // pair_cols) % row_n == (tr // given_rows)[:, None]) & (devices % pair_cols == (tc // given_cols)[:, None])
        slot = (tr % given_rows) * given_cols + tc % given_cols
        pick_slot = (slot[:, None] == jnp.arange(start_tiles.size, dtype=jnp.int32)[None, :]).astype(jnp.float32)
        start_rhs = jnp.sum(jnp.dot(same.astype(jnp.float32), got, precision=highest) * pick_slot, axis=1)
    packed = lax.all_to_all(jnp.stack((conduct, vertical)), "layer", 2, 1, tiled=True)
    conduct, vertical = packed[0], packed[1]
    sources = lax.all_to_all(sources, "layer", 1, 0, tiled=True)
    local_layers, grid_rows, grid_cols = sources.shape
    pad_rows = lax.dynamic_slice_in_dim(pad_map, lax.axis_index("layer") * grid_rows, grid_rows, 0)
    row_halo = rims(conduct, ROW_AXES, 1)
    col_halo = rims(conduct, "col", 2)
    layer_halo = rims(vertical, None, 0)
    near_vert = neighbours(vertical, [layer_halo, row_halo, col_halo])
    near_plane = neighbours(conduct, [layer_halo, row_halo, col_halo])
    weights = (
        jnp.sqrt(vertical * near_vert[0]),
        jnp.sqrt(vertical * near_vert[1]),
        jnp.sqrt(conduct * near_plane[2]),
        jnp.sqrt(conduct * near_plane[3]),
        jnp.sqrt(conduct * near_plane[4]),
        jnp.sqrt(conduct * near_plane[5]),
    )
    top_layer = pad_gain * pad_rows.astype(jnp.float32)
    pad_term = jnp.concatenate(
        (jnp.zeros((local_layers - 1, grid_rows, grid_cols), jnp.float32), top_layer[None]), 0
    )
    diagonal = pad_term
    for weight in weights:
        diagonal = diagonal + weight
    inverse = 1.0 / diagonal

    col_count = lax.axis_size("col")
    tile_cols = grid_cols * col_count // TILE
    tile_rows = grid_rows * axis_count(ROW_AXES) // TILE
    own_rows = grid_rows // TILE
    own_cols = grid_cols // TILE
    first_row = (lax.axis_index("row") * layer_count + lax.axis_index("layer")) * own_rows
    first_col = lax.axis_index("col") * own_cols
    flat_tiles = port_tile.reshape(-1)
    ring_rows = first_row - 1 + jnp.arange(own_rows + 2, dtype=jnp.int32)
    ring_cols = first_col - 1 + jnp.arange(own_cols + 2, dtype=jnp.int32)
    ring_ok = ((ring_rows >= 0) & (ring_rows < tile_rows))[:, None] & ((ring_cols >= 0) & (ring_cols < tile_cols))[None, :]
    ring_ids = jnp.where(ring_ok, ring_rows[:, None] * tile_cols + ring_cols[None, :], -1).reshape(-1)
    scatter_ring = (ring_ids[:, None] == flat_tiles[None, :]).astype(jnp.float32)
    coarse = coarse_pair if col_count == 2 else coarse_general

    drop = None
    drop_near = None
    for outer in range(ITERS):
        if drop is None:
            resid = sources
        else:
            resid = sources - apply_grid(drop, drop_near, weights, pad_term)
        plane = jnp.sum(resid, axis=0)
        tiles = plane.reshape(own_rows, TILE, own_cols, TILE).sum(axis=(1, 3)).reshape(-1)
        if drop is None and start_rhs is not None:
            rhs = start_rhs.reshape(NPANEL, PANEL) * (restrict_scale / TILE)
        else:
            rhs = share_tiles(tiles, own_rows, own_cols, flat_tiles).reshape(NPANEL, PANEL) * (restrict_scale / TILE)
        total = smooth(resid, weights, pad_term, inverse)
        if col_count == 2 and outer == ITERS - 1 and drop is not None:
            ports = coarse_pair(rhs, pivots, coupling, total)
        else:
            ports = coarse(rhs, pivots, coupling)
        tile_values = jnp.dot(scatter_ring, ports.reshape(-1), precision=highest).reshape(own_rows + 2, own_cols + 2)
        ring = expand(expand(tile_values, True).T, True).T * prolong_scale
        centre = ring[1:-1, 1:-1]
        lifted = jnp.broadcast_to(centre[None], (local_layers, grid_rows, grid_cols))
        if outer == ITERS - 1 and drop is not None:
            both = lax.all_to_all(jnp.stack((drop, total)), "layer", 1, 2, tiled=True)
            given_values = jnp.dot(given_pick, ports.reshape(-1), precision=highest).reshape(given_rows, given_cols)
            given_field = jnp.repeat(jnp.repeat(given_values, TILE, axis=0), TILE, axis=1) * prolong_scale
            given_lifted = jnp.broadcast_to(given_field[None], both.shape[1:])
            return ((both[0] + given_lifted) + both[1], ports)
        if outer == ITERS - 1:
            drop = (lifted if drop is None else drop + lifted) + total
            break
        lifted_near = [lifted, lifted]
        for part in (ring[2:, 1:-1], ring[:-2, 1:-1], ring[1:-1, 2:], ring[1:-1, :-2]):
            lifted_near.append(jnp.broadcast_to(part[None], (local_layers, grid_rows, grid_cols)))
        total_near = neighbours(total, exchange(total))
        if drop is None:
            drop = lifted + total
            drop_near = [a + b for a, b in zip(lifted_near, total_near)]
        else:
            drop = drop + lifted + total
            drop_near = [(d + a) + b for d, a, b in zip(drop_near, lifted_near, total_near)]
    drop = lax.all_to_all(drop, "layer", 0, 1, tiled=True)
    return (drop, ports)


def solution(mesh):
    placed = (
        P("layer", "row", "col"),
        P("layer", "row", "col"),
        P("layer", "row", "col"),
        P("layer", "row", "col"),
        P("row", "col"),
        P(),
        P(None, "col", None),
        P(None, "col", None),
    )
    return jax.shard_map(
        shards,
        mesh=mesh,
        in_specs=placed,
        out_specs=(P("layer", "row", "col"), P()),
        check_vma=False,
    )
```

```python
import jax
import jax.numpy as jnp
from jax import lax
from jax.sharding import PartitionSpec as P

TILE = 16
PANEL = 512
NPANEL = 4
DEG = 3
ITERS = 2


pad_gain = 8.0
bound_low = 0.1
bound_high = 1.9
restrict_scale = 0.25
prolong_scale = 0.5

highest = lax.Precision.HIGHEST
solve_precision = lax.Precision.HIGH
GRID_AXES = (("layer", 0), ("row", 1), ("col", 2))
ROW_AXES = ("layer", "row")


def axis_count(axis):
    names = axis if isinstance(axis, tuple) else (axis,)
    count = 1
    for name in names:
        count *= lax.axis_size(name)
    return count


def rims(field, axis, dim):
    size = field.shape[dim]
    head = lax.slice_in_dim(field, 0, 1, axis=dim)
    tail = lax.slice_in_dim(field, size - 1, size, axis=dim)
    if axis is None:
        return jnp.zeros_like(head), jnp.zeros_like(tail)
    count = axis_count(axis)
    place = list(range(count))
    if axis == ROW_AXES:
        layers, rows = lax.axis_size("layer"), lax.axis_size("row")
        place = [(b % layers) * rows + b // layers for b in range(count)]
    if count == 2:
        low = lax.axis_index(axis) == 0
        got = lax.ppermute(jnp.where(low, tail, head), axis, [(0, 1), (1, 0)])
        zero = jnp.zeros_like(got)
        return jnp.where(low, got, zero), jnp.where(low, zero, got)
    below = lax.ppermute(tail, axis, [(place[i], place[i + 1]) for i in range(count - 1)])
    above = lax.ppermute(head, axis, [(place[i + 1], place[i]) for i in range(count - 1)])
    return above, below


def neighbours(field, halo):
    out = []
    for (axis, dim), (above, below) in zip(GRID_AXES, halo):
        size = field.shape[dim]
        out.append(jnp.concatenate([lax.slice_in_dim(field, 1, size, axis=dim), above], axis=dim))
        out.append(jnp.concatenate([below, lax.slice_in_dim(field, 0, size - 1, axis=dim)], axis=dim))
    return out


def exchange(field):
    return [rims(field, axis, dim) for axis, dim in ((None, 0), (ROW_AXES, 1), ("col", 2))]


def apply_grid(field, near, weights, pad_term):
    result = pad_term * field
    for weight, other in zip(weights, near):
        result = result + weight * (field - other)
    return result


def smooth(resid, weights, pad_term, inverse):
    theta = (bound_high + bound_low) / 2.0
    delta = (bound_high - bound_low) / 2.0
    sigma = theta / delta
    rho = 1.0 / sigma
    change = inverse * resid / theta
    total = change
    for sweep in range(DEG - 1):
        remain = resid - apply_grid(total, neighbours(total, exchange(total)), weights, pad_term)
        rho_new = 1.0 / (2.0 * sigma - rho)
        change = rho_new * rho * change + 2.0 * rho_new / delta * inverse * remain
        total = total + change
        rho = rho_new
    return total


def all_sum(value):
    for axis, _ in GRID_AXES:
        count = lax.axis_size(axis)
        if count & (count - 1):
            value = lax.psum(value, axis)
            continue
        step = 1
        while step < count:
            value = value + lax.ppermute(value, axis, [(i, i ^ step) for i in range(count)])
            step *= 2
    return value


def share_tiles(tiles, own_rows, own_cols, flat_tiles):
    layers, rows, cols = (lax.axis_size(axis) for axis, _ in GRID_AXES)
    count = layers * rows * cols
    payload = jnp.broadcast_to(tiles.reshape(1, -1), (count, tiles.size))
    got = lax.all_to_all(payload, ("layer", "row", "col"), 0, 0, tiled=True)
    tile_cols = cols * own_cols
    tile_row, tile_col = flat_tiles // tile_cols, flat_tiles % tile_cols
    block = tile_row // own_rows
    device = ((block % layers) * rows + block // layers) * cols + tile_col // own_cols
    slot = (tile_row % own_rows) * own_cols + tile_col % own_cols
    pick_device = (device[:, None] == jnp.arange(count, dtype=jnp.int32)[None, :]).astype(jnp.float32)
    pick_slot = (slot[:, None] == jnp.arange(tiles.size, dtype=jnp.int32)[None, :]).astype(jnp.float32)
    return jnp.sum(jnp.dot(pick_device, got, precision=highest) * pick_slot, axis=1)


def swap_col(value):
    return lax.ppermute(value, "col", [(0, 1), (1, 0)])


def join_halves(mine, other, low):
    return jnp.where(low, jnp.concatenate([mine, other]), jnp.concatenate([other, mine]))


def coarse_pair(rhs, pivots, coupling, tie=None):
    share = pivots.shape[1]
    low = lax.axis_index("col") == 0
    start = lax.axis_index("col") * share
    own = lambda vector: lax.dynamic_slice_in_dim(vector, start, share)
    other_half = lambda vector: lax.dynamic_slice_in_dim(vector, share - start, share)
    full = rhs[0]
    forward = [full]
    for section in range(1, NPANEL):
        piece = own(rhs[section]) - jnp.dot(coupling[section - 1], full, precision=solve_precision)
        full = join_halves(piece, swap_col(piece), low)
        forward.append(full)
    scaled = [jnp.dot(pivots[section], forward[section], precision=solve_precision) for section in range(NPANEL)]
    mine = scaled[NPANEL - 1]
    results = [None] * NPANEL
    if tie is not None:
        mine, _ = lax.optimization_barrier((mine, tie))
    for section in range(NPANEL - 2, 0, -1):
        partial = jnp.dot(mine, coupling[section], precision=solve_precision)
        got = swap_col(jnp.concatenate([other_half(partial), mine]))
        results[section + 1] = join_halves(mine, got[share:], low)
        mine = scaled[section] - (own(partial) + got[:share])
    partial = jnp.dot(mine, coupling[0], precision=solve_precision)
    got = swap_col(jnp.concatenate([partial, scaled[0], mine]))
    results[1] = join_halves(mine, got[PANEL + share:], low)
    first = join_halves(scaled[0], got[PANEL:PANEL + share], low)
    low_part = jnp.where(low, partial, got[:PANEL])
    high_part = jnp.where(low, got[:PANEL], partial)
    results[0] = first - (low_part + high_part)
    return jnp.stack(results)


def coarse_rows(rhs, pivots, coupling, tie=None):
    share = pivots.shape[1]
    low = lax.axis_index("col") == 0
    start = lax.axis_index("col") * share
    own = lambda vector: lax.dynamic_slice_in_dim(vector, start, share)
    forward = [rhs[0]]
    for section in range(1, NPANEL):
        forward.append(rhs[section] - jnp.dot(coupling[section - 1], forward[-1], precision=solve_precision))
    scaled = [jnp.dot(pivots[section], forward[section], precision=solve_precision) for section in range(NPANEL)]
    results = [None] * NPANEL
    mine = scaled[NPANEL - 1]
    if tie is not None:
        mine, _ = lax.optimization_barrier((mine, tie))
    for section in range(NPANEL - 2, 0, -1):
        later = join_halves(mine, swap_col(mine), low)
        results[section + 1] = later
        mine = scaled[section] - own(jnp.dot(later, coupling[section], precision=solve_precision))
    got = swap_col(jnp.concatenate([mine, scaled[0]]))
    results[1] = join_halves(mine, got[:share], low)
    first = join_halves(scaled[0], got[share:], low)
    results[0] = first - jnp.dot(results[1], coupling[0], precision=solve_precision)
    return jnp.stack(results)


def whole_coupling(coupling):
    layers = lax.axis_size("layer")
    quarter = coupling.shape[1] // 2
    core = lax.axis_index("layer") % 2
    piece = lax.dynamic_slice_in_dim(coupling, core * quarter, quarter, 1)
    first = swap_col(piece)
    second = lax.ppermute(first, "layer", [(i, i ^ 1) for i in range(layers)])
    other = jnp.where(core == 0, jnp.concatenate([first, second], 1), jnp.concatenate([second, first], 1))
    low = lax.axis_index("col") == 0
    return jnp.where(low, jnp.concatenate([coupling, other], 1), jnp.concatenate([other, coupling], 1))


def coarse_general(rhs, pivots, coupling):
    share = pivots.shape[1]
    start = lax.axis_index("col") * share
    full = rhs[0]
    forward = [full]
    for section in range(1, NPANEL):
        piece = lax.dynamic_slice_in_dim(rhs[section], start, share) - jnp.dot(
            coupling[section - 1], full, precision=solve_precision
        )
        full = lax.all_gather(piece, "col", axis=0, tiled=True)
        forward.append(full)
    scaled = [jnp.dot(pivots[section], forward[section], precision=solve_precision) for section in range(NPANEL)]
    results = [None] * NPANEL
    for section in range(NPANEL - 1, -1, -1):
        placed = lax.dynamic_update_slice_in_dim(jnp.zeros((PANEL,), jnp.float32), scaled[section], start, 0)
        if section < NPANEL - 1:
            later_rows = lax.dynamic_slice_in_dim(results[section + 1], start, share)
            placed = placed - jnp.dot(later_rows, coupling[section], precision=solve_precision)
        results[section] = lax.psum(placed, "col")
    return jnp.stack(results)


def expand(values, edge):
    inner = values[1:-1] if edge else values
    body = jnp.repeat(inner, TILE, axis=0)
    if edge:
        body = jnp.concatenate([values[:1], body, values[-1:]], axis=0)
    return body


def shards(sources, conduct, via_cond, via_map, pad_map, port_tile, pivots, coupling):
    layer_count = lax.axis_size("layer")
    vertical = via_cond * via_map.astype(jnp.float32)
    given_rows = sources.shape[1] // TILE
    given_cols = sources.shape[2] // TILE
    given_tile_cols = given_cols * lax.axis_size("col")
    given_ids = (
        (lax.axis_index("row") * given_rows + jnp.arange(given_rows, dtype=jnp.int32))[:, None] * given_tile_cols
        + (lax.axis_index("col") * given_cols + jnp.arange(given_cols, dtype=jnp.int32))[None, :]
    ).reshape(-1)
    given_pick = (given_ids[:, None] == port_tile.reshape(-1)[None, :]).astype(jnp.float32)
    split_coupling = lax.axis_size("col") == 2 and layer_count % 2 == 0 and coupling.shape[1] % 2 == 0
    if split_coupling:
        full_coupling = whole_coupling(coupling)
    packed = lax.all_to_all(jnp.stack((conduct, vertical)), "layer", 2, 1, tiled=True)
    conduct, vertical = packed[0], packed[1]
    sources = lax.all_to_all(sources, "layer", 1, 0, tiled=True)
    local_layers, grid_rows, grid_cols = sources.shape
    pad_rows = lax.dynamic_slice_in_dim(pad_map, lax.axis_index("layer") * grid_rows, grid_rows, 0)
    row_halo = rims(conduct, ROW_AXES, 1)
    col_halo = rims(conduct, "col", 2)
    layer_halo = rims(vertical, None, 0)
    near_vert = neighbours(vertical, [layer_halo, row_halo, col_halo])
    near_plane = neighbours(conduct, [layer_halo, row_halo, col_halo])
    weights = (
        jnp.sqrt(vertical * near_vert[0]),
        jnp.sqrt(vertical * near_vert[1]),
        jnp.sqrt(conduct * near_plane[2]),
        jnp.sqrt(conduct * near_plane[3]),
        jnp.sqrt(conduct * near_plane[4]),
        jnp.sqrt(conduct * near_plane[5]),
    )
    top_layer = pad_gain * pad_rows.astype(jnp.float32)
    pad_term = jnp.concatenate(
        (jnp.zeros((local_layers - 1, grid_rows, grid_cols), jnp.float32), top_layer[None]), 0
    )
    diagonal = pad_term
    for weight in weights:
        diagonal = diagonal + weight
    inverse = 1.0 / diagonal

    col_count = lax.axis_size("col")
    tile_cols = grid_cols * col_count // TILE
    tile_rows = grid_rows * axis_count(ROW_AXES) // TILE
    own_rows = grid_rows // TILE
    own_cols = grid_cols // TILE
    first_row = (lax.axis_index("row") * layer_count + lax.axis_index("layer")) * own_rows
    first_col = lax.axis_index("col") * own_cols
    flat_tiles = port_tile.reshape(-1)
    ring_rows = first_row - 1 + jnp.arange(own_rows + 2, dtype=jnp.int32)
    ring_cols = first_col - 1 + jnp.arange(own_cols + 2, dtype=jnp.int32)
    ring_ok = ((ring_rows >= 0) & (ring_rows < tile_rows))[:, None] & ((ring_cols >= 0) & (ring_cols < tile_cols))[None, :]
    ring_ids = jnp.where(ring_ok, ring_rows[:, None] * tile_cols + ring_cols[None, :], -1).reshape(-1)
    scatter_ring = (ring_ids[:, None] == flat_tiles[None, :]).astype(jnp.float32)
    coarse = coarse_pair if col_count == 2 else coarse_general

    drop = None
    drop_near = None
    for outer in range(ITERS):
        if drop is None:
            resid = sources
        else:
            resid = sources - apply_grid(drop, drop_near, weights, pad_term)
        plane = jnp.sum(resid, axis=0)
        tiles = plane.reshape(own_rows, TILE, own_cols, TILE).sum(axis=(1, 3)).reshape(-1)
        rhs = share_tiles(tiles, own_rows, own_cols, flat_tiles).reshape(NPANEL, PANEL) * (restrict_scale / TILE)
        total = smooth(resid, weights, pad_term, inverse)
        if split_coupling:
            ports = coarse_rows(rhs, pivots, full_coupling, total if outer == ITERS - 1 and drop is not None else None)
        elif col_count == 2 and outer == ITERS - 1 and drop is not None:
            ports = coarse_pair(rhs, pivots, coupling, total)
        else:
            ports = coarse(rhs, pivots, coupling)
        tile_values = jnp.dot(scatter_ring, ports.reshape(-1), precision=highest).reshape(own_rows + 2, own_cols + 2)
        ring = expand(expand(tile_values, True).T, True).T * prolong_scale
        centre = ring[1:-1, 1:-1]
        lifted = jnp.broadcast_to(centre[None], (local_layers, grid_rows, grid_cols))
        if outer == ITERS - 1 and drop is not None:
            both = lax.all_to_all(jnp.stack((drop, total)), "layer", 1, 2, tiled=True)
            given_values = jnp.dot(given_pick, ports.reshape(-1), precision=highest).reshape(given_rows, given_cols)
            given_field = jnp.repeat(jnp.repeat(given_values, TILE, axis=0), TILE, axis=1) * prolong_scale
            given_lifted = jnp.broadcast_to(given_field[None], both.shape[1:])
            return ((both[0] + given_lifted) + both[1], ports)
        if outer == ITERS - 1:
            drop = (lifted if drop is None else drop + lifted) + total
            break
        lifted_near = [lifted, lifted]
        for part in (ring[2:, 1:-1], ring[:-2, 1:-1], ring[1:-1, 2:], ring[1:-1, :-2]):
            lifted_near.append(jnp.broadcast_to(part[None], (local_layers, grid_rows, grid_cols)))
        total_near = neighbours(total, exchange(total))
        if drop is None:
            drop = lifted + total
            drop_near = [a + b for a, b in zip(lifted_near, total_near)]
        else:
            drop = drop + lifted + total
            drop_near = [(d + a) + b for d, a, b in zip(drop_near, lifted_near, total_near)]
    drop = lax.all_to_all(drop, "layer", 0, 1, tiled=True)
    return (drop, ports)


def solution(mesh):
    placed = (
        P("layer", "row", "col"),
        P("layer", "row", "col"),
        P("layer", "row", "col"),
        P("layer", "row", "col"),
        P("row", "col"),
        P(),
        P(None, "col", None),
        P(None, "col", None),
    )
    return jax.shard_map(
        shards,
        mesh=mesh,
        in_specs=placed,
        out_specs=(P("layer", "row", "col"), P()),
        check_vma=False,
    )
```

```python
import jax
import jax.numpy as jnp
from jax import lax
from jax.sharding import PartitionSpec as P

TILE = 16
PANEL = 512
NPANEL = 4
DEG = 3
ITERS = 2


pad_gain = 8.0
bound_low = 0.1
bound_high = 1.9
restrict_scale = 0.25
prolong_scale = 0.5

highest = lax.Precision.HIGHEST
solve_precision = lax.Precision.HIGH
GRID_AXES = (("layer", 0), ("row", 1), ("col", 2))
ROW_AXES = ("layer", "row")


def axis_count(axis):
    names = axis if isinstance(axis, tuple) else (axis,)
    count = 1
    for name in names:
        count *= lax.axis_size(name)
    return count


def rims(field, axis, dim):
    size = field.shape[dim]
    head = lax.slice_in_dim(field, 0, 1, axis=dim)
    tail = lax.slice_in_dim(field, size - 1, size, axis=dim)
    if axis is None:
        return jnp.zeros_like(head), jnp.zeros_like(tail)
    count = axis_count(axis)
    place = list(range(count))
    if axis == ROW_AXES:
        layers, rows = lax.axis_size("layer"), lax.axis_size("row")
        place = [(b % layers) * rows + b // layers for b in range(count)]
    if count == 2:
        low = lax.axis_index(axis) == 0
        got = lax.ppermute(jnp.where(low, tail, head), axis, [(0, 1), (1, 0)])
        zero = jnp.zeros_like(got)
        return jnp.where(low, got, zero), jnp.where(low, zero, got)
    below = lax.ppermute(tail, axis, [(place[i], place[i + 1]) for i in range(count - 1)])
    above = lax.ppermute(head, axis, [(place[i + 1], place[i]) for i in range(count - 1)])
    return above, below


def neighbours(field, halo):
    out = []
    for (axis, dim), (above, below) in zip(GRID_AXES, halo):
        size = field.shape[dim]
        out.append(jnp.concatenate([lax.slice_in_dim(field, 1, size, axis=dim), above], axis=dim))
        out.append(jnp.concatenate([below, lax.slice_in_dim(field, 0, size - 1, axis=dim)], axis=dim))
    return out


def exchange(field):
    return [rims(field, axis, dim) for axis, dim in ((None, 0), (ROW_AXES, 1), ("col", 2))]


def apply_grid(field, near, weights, pad_term):
    result = pad_term * field
    for weight, other in zip(weights, near):
        result = result + weight * (field - other)
    return result


def smooth(resid, weights, pad_term, inverse):
    theta = (bound_high + bound_low) / 2.0
    delta = (bound_high - bound_low) / 2.0
    sigma = theta / delta
    rho = 1.0 / sigma
    change = inverse * resid / theta
    total = change
    for sweep in range(DEG - 1):
        remain = resid - apply_grid(total, neighbours(total, exchange(total)), weights, pad_term)
        rho_new = 1.0 / (2.0 * sigma - rho)
        change = rho_new * rho * change + 2.0 * rho_new / delta * inverse * remain
        total = total + change
        rho = rho_new
    return total


def all_sum(value):
    for axis, _ in GRID_AXES:
        count = lax.axis_size(axis)
        if count & (count - 1):
            value = lax.psum(value, axis)
            continue
        step = 1
        while step < count:
            value = value + lax.ppermute(value, axis, [(i, i ^ step) for i in range(count)])
            step *= 2
    return value


def share_tiles(tiles, own_rows, own_cols, flat_tiles):
    layers, rows, cols = (lax.axis_size(axis) for axis, _ in GRID_AXES)
    count = layers * rows * cols
    payload = jnp.broadcast_to(tiles.reshape(1, -1), (count, tiles.size))
    got = lax.all_to_all(payload, ("layer", "row", "col"), 0, 0, tiled=True)
    tile_cols = cols * own_cols
    tile_row, tile_col = flat_tiles // tile_cols, flat_tiles % tile_cols
    block = tile_row // own_rows
    device = ((block % layers) * rows + block // layers) * cols + tile_col // own_cols
    slot = (tile_row % own_rows) * own_cols + tile_col % own_cols
    pick_device = (device[:, None] == jnp.arange(count, dtype=jnp.int32)[None, :]).astype(jnp.float32)
    pick_slot = (slot[:, None] == jnp.arange(tiles.size, dtype=jnp.int32)[None, :]).astype(jnp.float32)
    return jnp.sum(jnp.dot(pick_device, got, precision=highest) * pick_slot, axis=1)


def swap_col(value):
    return lax.ppermute(value, "col", [(0, 1), (1, 0)])


def join_halves(mine, other, low):
    return jnp.where(low, jnp.concatenate([mine, other]), jnp.concatenate([other, mine]))


def coarse_pair(rhs, pivots, coupling, tie=None):
    share = pivots.shape[1]
    low = lax.axis_index("col") == 0
    start = lax.axis_index("col") * share
    own = lambda vector: lax.dynamic_slice_in_dim(vector, start, share)
    other_half = lambda vector: lax.dynamic_slice_in_dim(vector, share - start, share)
    full = rhs[0]
    forward = [full]
    for section in range(1, NPANEL):
        piece = own(rhs[section]) - jnp.dot(coupling[section - 1], full, precision=solve_precision)
        full = join_halves(piece, swap_col(piece), low)
        forward.append(full)
    scaled = [jnp.dot(pivots[section], forward[section], precision=solve_precision) for section in range(NPANEL)]
    mine = scaled[NPANEL - 1]
    results = [None] * NPANEL
    if tie is not None:
        mine, _ = lax.optimization_barrier((mine, tie))
    for section in range(NPANEL - 2, 0, -1):
        partial = jnp.dot(mine, coupling[section], precision=solve_precision)
        got = swap_col(jnp.concatenate([other_half(partial), mine]))
        results[section + 1] = join_halves(mine, got[share:], low)
        mine = scaled[section] - (own(partial) + got[:share])
    partial = jnp.dot(mine, coupling[0], precision=solve_precision)
    got = swap_col(jnp.concatenate([partial, scaled[0], mine]))
    results[1] = join_halves(mine, got[PANEL + share:], low)
    first = join_halves(scaled[0], got[PANEL:PANEL + share], low)
    low_part = jnp.where(low, partial, got[:PANEL])
    high_part = jnp.where(low, got[:PANEL], partial)
    results[0] = first - (low_part + high_part)
    return jnp.stack(results)


def coarse_general(rhs, pivots, coupling):
    share = pivots.shape[1]
    start = lax.axis_index("col") * share
    full = rhs[0]
    forward = [full]
    for section in range(1, NPANEL):
        piece = lax.dynamic_slice_in_dim(rhs[section], start, share) - jnp.dot(
            coupling[section - 1], full, precision=solve_precision
        )
        full = lax.all_gather(piece, "col", axis=0, tiled=True)
        forward.append(full)
    scaled = [jnp.dot(pivots[section], forward[section], precision=solve_precision) for section in range(NPANEL)]
    results = [None] * NPANEL
    for section in range(NPANEL - 1, -1, -1):
        placed = lax.dynamic_update_slice_in_dim(jnp.zeros((PANEL,), jnp.float32), scaled[section], start, 0)
        if section < NPANEL - 1:
            later_rows = lax.dynamic_slice_in_dim(results[section + 1], start, share)
            placed = placed - jnp.dot(later_rows, coupling[section], precision=solve_precision)
        results[section] = lax.psum(placed, "col")
    return jnp.stack(results)


def expand(values, edge):
    inner = values[1:-1] if edge else values
    body = jnp.repeat(inner, TILE, axis=0)
    if edge:
        body = jnp.concatenate([values[:1], body, values[-1:]], axis=0)
    return body


def shards(sources, conduct, via_cond, via_map, pad_map, port_tile, pivots, coupling):
    layer_count = lax.axis_size("layer")
    vertical = via_cond * via_map.astype(jnp.float32)
    given_rows = sources.shape[1] // TILE
    given_cols = sources.shape[2] // TILE
    given_tile_cols = given_cols * lax.axis_size("col")
    given_ids = (
        (lax.axis_index("row") * given_rows + jnp.arange(given_rows, dtype=jnp.int32))[:, None] * given_tile_cols
        + (lax.axis_index("col") * given_cols + jnp.arange(given_cols, dtype=jnp.int32))[None, :]
    ).reshape(-1)
    given_pick = (given_ids[:, None] == port_tile.reshape(-1)[None, :]).astype(jnp.float32)
    packed = lax.all_to_all(jnp.stack((conduct, vertical)), "layer", 2, 1, tiled=True)
    sources, packed = lax.optimization_barrier((sources, packed))
    conduct, vertical = packed[0], packed[1]
    sources = lax.all_to_all(sources, "layer", 1, 0, tiled=True)
    local_layers, grid_rows, grid_cols = sources.shape
    pad_rows = lax.dynamic_slice_in_dim(pad_map, lax.axis_index("layer") * grid_rows, grid_rows, 0)
    row_halo = rims(conduct, ROW_AXES, 1)
    col_halo = rims(conduct, "col", 2)
    layer_halo = rims(vertical, None, 0)
    near_vert = neighbours(vertical, [layer_halo, row_halo, col_halo])
    near_plane = neighbours(conduct, [layer_halo, row_halo, col_halo])
    weights = (
        jnp.sqrt(vertical * near_vert[0]),
        jnp.sqrt(vertical * near_vert[1]),
        jnp.sqrt(conduct * near_plane[2]),
        jnp.sqrt(conduct * near_plane[3]),
        jnp.sqrt(conduct * near_plane[4]),
        jnp.sqrt(conduct * near_plane[5]),
    )
    top_layer = pad_gain * pad_rows.astype(jnp.float32)
    pad_term = jnp.concatenate(
        (jnp.zeros((local_layers - 1, grid_rows, grid_cols), jnp.float32), top_layer[None]), 0
    )
    diagonal = pad_term
    for weight in weights:
        diagonal = diagonal + weight
    inverse = 1.0 / diagonal

    col_count = lax.axis_size("col")
    tile_cols = grid_cols * col_count // TILE
    tile_rows = grid_rows * axis_count(ROW_AXES) // TILE
    own_rows = grid_rows // TILE
    own_cols = grid_cols // TILE
    first_row = (lax.axis_index("row") * layer_count + lax.axis_index("layer")) * own_rows
    first_col = lax.axis_index("col") * own_cols
    flat_tiles = port_tile.reshape(-1)
    ring_rows = first_row - 1 + jnp.arange(own_rows + 2, dtype=jnp.int32)
    ring_cols = first_col - 1 + jnp.arange(own_cols + 2, dtype=jnp.int32)
    ring_ok = ((ring_rows >= 0) & (ring_rows < tile_rows))[:, None] & ((ring_cols >= 0) & (ring_cols < tile_cols))[None, :]
    ring_ids = jnp.where(ring_ok, ring_rows[:, None] * tile_cols + ring_cols[None, :], -1).reshape(-1)
    scatter_ring = (ring_ids[:, None] == flat_tiles[None, :]).astype(jnp.float32)
    coarse = coarse_pair if col_count == 2 else coarse_general

    drop = None
    drop_near = None
    for outer in range(ITERS):
        if drop is None:
            resid = sources
        else:
            resid = sources - apply_grid(drop, drop_near, weights, pad_term)
        plane = jnp.sum(resid, axis=0)
        tiles = plane.reshape(own_rows, TILE, own_cols, TILE).sum(axis=(1, 3)).reshape(-1)
        rhs = share_tiles(tiles, own_rows, own_cols, flat_tiles).reshape(NPANEL, PANEL) * (restrict_scale / TILE)
        total = smooth(resid, weights, pad_term, inverse)
        if col_count == 2 and outer == ITERS - 1 and drop is not None:
            ports = coarse_pair(rhs, pivots, coupling, total)
        else:
            ports = coarse(rhs, pivots, coupling)
        tile_values = jnp.dot(scatter_ring, ports.reshape(-1), precision=highest).reshape(own_rows + 2, own_cols + 2)
        ring = expand(expand(tile_values, True).T, True).T * prolong_scale
        centre = ring[1:-1, 1:-1]
        lifted = jnp.broadcast_to(centre[None], (local_layers, grid_rows, grid_cols))
        if outer == ITERS - 1 and drop is not None:
            both = lax.all_to_all(jnp.stack((drop, total)), "layer", 1, 2, tiled=True)
            given_values = jnp.dot(given_pick, ports.reshape(-1), precision=highest).reshape(given_rows, given_cols)
            given_field = jnp.repeat(jnp.repeat(given_values, TILE, axis=0), TILE, axis=1) * prolong_scale
            given_lifted = jnp.broadcast_to(given_field[None], both.shape[1:])
            return ((both[0] + given_lifted) + both[1], ports)
        if outer == ITERS - 1:
            drop = (lifted if drop is None else drop + lifted) + total
            break
        lifted_near = [lifted, lifted]
        for part in (ring[2:, 1:-1], ring[:-2, 1:-1], ring[1:-1, 2:], ring[1:-1, :-2]):
            lifted_near.append(jnp.broadcast_to(part[None], (local_layers, grid_rows, grid_cols)))
        total_near = neighbours(total, exchange(total))
        if drop is None:
            drop = lifted + total
            drop_near = [a + b for a, b in zip(lifted_near, total_near)]
        else:
            drop = drop + lifted + total
            drop_near = [(d + a) + b for d, a, b in zip(drop_near, lifted_near, total_near)]
    drop = lax.all_to_all(drop, "layer", 0, 1, tiled=True)
    return (drop, ports)


def solution(mesh):
    placed = (
        P("layer", "row", "col"),
        P("layer", "row", "col"),
        P("layer", "row", "col"),
        P("layer", "row", "col"),
        P("row", "col"),
        P(),
        P(None, "col", None),
        P(None, "col", None),
    )
    return jax.shard_map(
        shards,
        mesh=mesh,
        in_specs=placed,
        out_specs=(P("layer", "row", "col"), P()),
        check_vma=False,
    )
```

```python
import jax
import jax.numpy as jnp
from jax import lax
from jax.sharding import PartitionSpec as P

TILE = 16
PANEL = 512
NPANEL = 4
DEG = 3
ITERS = 2


pad_gain = 8.0
bound_low = 0.1
bound_high = 1.9
restrict_scale = 0.25
prolong_scale = 0.5

highest = lax.Precision.HIGHEST
solve_precision = lax.Precision.HIGH
GRID_AXES = (("layer", 0), ("row", 1), ("col", 2))
ROW_AXES = ("layer", "row")


def axis_count(axis):
    names = axis if isinstance(axis, tuple) else (axis,)
    count = 1
    for name in names:
        count *= lax.axis_size(name)
    return count


def rims(field, axis, dim):
    size = field.shape[dim]
    head = lax.slice_in_dim(field, 0, 1, axis=dim)
    tail = lax.slice_in_dim(field, size - 1, size, axis=dim)
    if axis is None:
        return jnp.zeros_like(head), jnp.zeros_like(tail)
    count = axis_count(axis)
    place = list(range(count))
    if axis == ROW_AXES:
        layers, rows = lax.axis_size("layer"), lax.axis_size("row")
        place = [(b % layers) * rows + b // layers for b in range(count)]
    if count == 2:
        low = lax.axis_index(axis) == 0
        got = lax.ppermute(jnp.where(low, tail, head), axis, [(0, 1), (1, 0)])
        zero = jnp.zeros_like(got)
        return jnp.where(low, got, zero), jnp.where(low, zero, got)
    below = lax.ppermute(tail, axis, [(place[i], place[i + 1]) for i in range(count - 1)])
    above = lax.ppermute(head, axis, [(place[i + 1], place[i]) for i in range(count - 1)])
    return above, below


def neighbours(field, halo):
    out = []
    for (axis, dim), (above, below) in zip(GRID_AXES, halo):
        size = field.shape[dim]
        out.append(jnp.concatenate([lax.slice_in_dim(field, 1, size, axis=dim), above], axis=dim))
        out.append(jnp.concatenate([below, lax.slice_in_dim(field, 0, size - 1, axis=dim)], axis=dim))
    return out


def exchange(field):
    return [rims(field, axis, dim) for axis, dim in ((None, 0), (ROW_AXES, 1), ("col", 2))]


def apply_grid(field, near, weights, pad_term):
    result = pad_term * field
    for weight, other in zip(weights, near):
        result = result + weight * (field - other)
    return result


def smooth(resid, weights, pad_term, inverse):
    theta = (bound_high + bound_low) / 2.0
    delta = (bound_high - bound_low) / 2.0
    sigma = theta / delta
    rho = 1.0 / sigma
    change = inverse * resid / theta
    total = change
    for sweep in range(DEG - 1):
        remain = resid - apply_grid(total, neighbours(total, exchange(total)), weights, pad_term)
        rho_new = 1.0 / (2.0 * sigma - rho)
        change = rho_new * rho * change + 2.0 * rho_new / delta * inverse * remain
        total = total + change
        rho = rho_new
    return total


def all_sum(value):
    for axis, _ in GRID_AXES:
        count = lax.axis_size(axis)
        if count & (count - 1):
            value = lax.psum(value, axis)
            continue
        step = 1
        while step < count:
            value = value + lax.ppermute(value, axis, [(i, i ^ step) for i in range(count)])
            step *= 2
    return value


def share_tiles(tiles, own_rows, own_cols, flat_tiles):
    layers, rows, cols = (lax.axis_size(axis) for axis, _ in GRID_AXES)
    count = layers * rows * cols
    payload = jnp.broadcast_to(tiles.reshape(1, -1), (count, tiles.size))
    got = lax.all_to_all(payload, ("layer", "row", "col"), 0, 0, tiled=True)
    tile_cols = cols * own_cols
    tile_row, tile_col = flat_tiles // tile_cols, flat_tiles % tile_cols
    block = tile_row // own_rows
    device = ((block % layers) * rows + block // layers) * cols + tile_col // own_cols
    slot = (tile_row % own_rows) * own_cols + tile_col % own_cols
    pick_device = (device[:, None] == jnp.arange(count, dtype=jnp.int32)[None, :]).astype(jnp.float32)
    pick_slot = (slot[:, None] == jnp.arange(tiles.size, dtype=jnp.int32)[None, :]).astype(jnp.float32)
    return jnp.sum(jnp.dot(pick_device, got, precision=highest) * pick_slot, axis=1)


def swap_col(value):
    return lax.ppermute(value, "col", [(0, 1), (1, 0)])


def join_halves(mine, other, low):
    return jnp.where(low, jnp.concatenate([mine, other]), jnp.concatenate([other, mine]))


def coarse_pair(rhs, pivots, coupling, tie=None):
    share = pivots.shape[1]
    low = lax.axis_index("col") == 0
    start = lax.axis_index("col") * share
    own = lambda vector: lax.dynamic_slice_in_dim(vector, start, share)
    other_half = lambda vector: lax.dynamic_slice_in_dim(vector, share - start, share)
    full = rhs[0]
    forward = [full]
    for section in range(1, NPANEL):
        piece = own(rhs[section]) - jnp.dot(coupling[section - 1], full, precision=solve_precision)
        full = join_halves(piece, swap_col(piece), low)
        forward.append(full)
    scaled = [jnp.dot(pivots[section], forward[section], precision=solve_precision) for section in range(NPANEL)]
    mine = scaled[NPANEL - 1]
    results = [None] * NPANEL
    if tie is not None:
        mine, _ = lax.optimization_barrier((mine, tie))
    for section in range(NPANEL - 2, 0, -1):
        partial = jnp.dot(mine, coupling[section], precision=solve_precision)
        got = swap_col(jnp.concatenate([other_half(partial), mine]))
        results[section + 1] = join_halves(mine, got[share:], low)
        mine = scaled[section] - (own(partial) + got[:share])
    partial = jnp.dot(mine, coupling[0], precision=solve_precision)
    got = swap_col(jnp.concatenate([partial, scaled[0], mine]))
    results[1] = join_halves(mine, got[PANEL + share:], low)
    first = join_halves(scaled[0], got[PANEL:PANEL + share], low)
    low_part = jnp.where(low, partial, got[:PANEL])
    high_part = jnp.where(low, got[:PANEL], partial)
    results[0] = first - (low_part + high_part)
    return jnp.stack(results)


def coarse_general(rhs, pivots, coupling):
    share = pivots.shape[1]
    start = lax.axis_index("col") * share
    full = rhs[0]
    forward = [full]
    for section in range(1, NPANEL):
        piece = lax.dynamic_slice_in_dim(rhs[section], start, share) - jnp.dot(
            coupling[section - 1], full, precision=solve_precision
        )
        full = lax.all_gather(piece, "col", axis=0, tiled=True)
        forward.append(full)
    scaled = [jnp.dot(pivots[section], forward[section], precision=solve_precision) for section in range(NPANEL)]
    results = [None] * NPANEL
    for section in range(NPANEL - 1, -1, -1):
        placed = lax.dynamic_update_slice_in_dim(jnp.zeros((PANEL,), jnp.float32), scaled[section], start, 0)
        if section < NPANEL - 1:
            later_rows = lax.dynamic_slice_in_dim(results[section + 1], start, share)
            placed = placed - jnp.dot(later_rows, coupling[section], precision=solve_precision)
        results[section] = lax.psum(placed, "col")
    return jnp.stack(results)


def expand(values, edge):
    inner = values[1:-1] if edge else values
    body = jnp.repeat(inner, TILE, axis=0)
    if edge:
        body = jnp.concatenate([values[:1], body, values[-1:]], axis=0)
    return body


def shards(sources, conduct, via_cond, via_map, pad_map, port_tile, pivots, coupling):
    layer_count = lax.axis_size("layer")
    vertical = via_cond * via_map.astype(jnp.float32)
    given_rows = sources.shape[1] // TILE
    given_cols = sources.shape[2] // TILE
    given_tile_cols = given_cols * lax.axis_size("col")
    given_ids = (
        (lax.axis_index("row") * given_rows + jnp.arange(given_rows, dtype=jnp.int32))[:, None] * given_tile_cols
        + (lax.axis_index("col") * given_cols + jnp.arange(given_cols, dtype=jnp.int32))[None, :]
    ).reshape(-1)
    given_pick = (given_ids[:, None] == port_tile.reshape(-1)[None, :]).astype(jnp.float32)
    packed = lax.all_to_all(jnp.stack((sources, conduct, vertical)), "layer", 2, 1, tiled=True)
    sources, conduct, vertical = packed[0], packed[1], packed[2]
    local_layers, grid_rows, grid_cols = sources.shape
    pad_rows = lax.dynamic_slice_in_dim(pad_map, lax.axis_index("layer") * grid_rows, grid_rows, 0)
    row_halo = rims(conduct, ROW_AXES, 1)
    col_halo = rims(conduct, "col", 2)
    layer_halo = rims(vertical, None, 0)
    near_vert = neighbours(vertical, [layer_halo, row_halo, col_halo])
    near_plane = neighbours(conduct, [layer_halo, row_halo, col_halo])
    weights = (
        jnp.sqrt(vertical * near_vert[0]),
        jnp.sqrt(vertical * near_vert[1]),
        jnp.sqrt(conduct * near_plane[2]),
        jnp.sqrt(conduct * near_plane[3]),
        jnp.sqrt(conduct * near_plane[4]),
        jnp.sqrt(conduct * near_plane[5]),
    )
    top_layer = pad_gain * pad_rows.astype(jnp.float32)
    pad_term = jnp.concatenate(
        (jnp.zeros((local_layers - 1, grid_rows, grid_cols), jnp.float32), top_layer[None]), 0
    )
    diagonal = pad_term
    for weight in weights:
        diagonal = diagonal + weight
    inverse = 1.0 / diagonal

    col_count = lax.axis_size("col")
    tile_cols = grid_cols * col_count // TILE
    tile_rows = grid_rows * axis_count(ROW_AXES) // TILE
    own_rows = grid_rows // TILE
    own_cols = grid_cols // TILE
    first_row = (lax.axis_index("row") * layer_count + lax.axis_index("layer")) * own_rows
    first_col = lax.axis_index("col") * own_cols
    flat_tiles = port_tile.reshape(-1)
    ring_rows = first_row - 1 + jnp.arange(own_rows + 2, dtype=jnp.int32)
    ring_cols = first_col - 1 + jnp.arange(own_cols + 2, dtype=jnp.int32)
    ring_ok = ((ring_rows >= 0) & (ring_rows < tile_rows))[:, None] & ((ring_cols >= 0) & (ring_cols < tile_cols))[None, :]
    ring_ids = jnp.where(ring_ok, ring_rows[:, None] * tile_cols + ring_cols[None, :], -1).reshape(-1)
    scatter_ring = (ring_ids[:, None] == flat_tiles[None, :]).astype(jnp.float32)
    coarse = coarse_pair if col_count == 2 else coarse_general

    drop = None
    drop_near = None
    for outer in range(ITERS):
        if drop is None:
            resid = sources
        else:
            resid = sources - apply_grid(drop, drop_near, weights, pad_term)
        plane = jnp.sum(resid, axis=0)
        tiles = plane.reshape(own_rows, TILE, own_cols, TILE).sum(axis=(1, 3)).reshape(-1)
        rhs = share_tiles(tiles, own_rows, own_cols, flat_tiles).reshape(NPANEL, PANEL) * (restrict_scale / TILE)
        total = smooth(resid, weights, pad_term, inverse)
        if col_count == 2 and outer == ITERS - 1 and drop is not None:
            ports = coarse_pair(rhs, pivots, coupling, total)
        else:
            ports = coarse(rhs, pivots, coupling)
        tile_values = jnp.dot(scatter_ring, ports.reshape(-1), precision=highest).reshape(own_rows + 2, own_cols + 2)
        ring = expand(expand(tile_values, True).T, True).T * prolong_scale
        centre = ring[1:-1, 1:-1]
        lifted = jnp.broadcast_to(centre[None], (local_layers, grid_rows, grid_cols))
        if outer == ITERS - 1 and drop is not None:
            both = lax.all_to_all(jnp.stack((drop, total)), "layer", 1, 2, tiled=True)
            given_values = jnp.dot(given_pick, ports.reshape(-1), precision=highest).reshape(given_rows, given_cols)
            given_field = jnp.repeat(jnp.repeat(given_values, TILE, axis=0), TILE, axis=1) * prolong_scale
            given_lifted = jnp.broadcast_to(given_field[None], both.shape[1:])
            return ((both[0] + given_lifted) + both[1], ports)
        if outer == ITERS - 1:
            drop = (lifted if drop is None else drop + lifted) + total
            break
        lifted_near = [lifted, lifted]
        for part in (ring[2:, 1:-1], ring[:-2, 1:-1], ring[1:-1, 2:], ring[1:-1, :-2]):
            lifted_near.append(jnp.broadcast_to(part[None], (local_layers, grid_rows, grid_cols)))
        total_near = neighbours(total, exchange(total))
        if drop is None:
            drop = lifted + total
            drop_near = [a + b for a, b in zip(lifted_near, total_near)]
        else:
            drop = drop + lifted + total
            drop_near = [(d + a) + b for d, a, b in zip(drop_near, lifted_near, total_near)]
    drop = lax.all_to_all(drop, "layer", 0, 1, tiled=True)
    return (drop, ports)


def solution(mesh):
    placed = (
        P("layer", "row", "col"),
        P("layer", "row", "col"),
        P("layer", "row", "col"),
        P("layer", "row", "col"),
        P("row", "col"),
        P(),
        P(None, "col", None),
        P(None, "col", None),
    )
    return jax.shard_map(
        shards,
        mesh=mesh,
        in_specs=placed,
        out_specs=(P("layer", "row", "col"), P()),
        check_vma=False,
    )
```

```python
import jax
import jax.numpy as jnp
from jax import lax
from jax.sharding import PartitionSpec as P

TILE = 16
PANEL = 512
NPANEL = 4
DEG = 3
ITERS = 2


pad_gain = 8.0
bound_low = 0.1
bound_high = 1.9
restrict_scale = 0.25
prolong_scale = 0.5

highest = lax.Precision.HIGHEST
solve_precision = lax.Precision.HIGH
GRID_AXES = (("layer", 0), ("row", 1), ("col", 2))
ROW_AXES = ("layer", "row")


def axis_count(axis):
    names = axis if isinstance(axis, tuple) else (axis,)
    count = 1
    for name in names:
        count *= lax.axis_size(name)
    return count


def rims(field, axis, dim):
    size = field.shape[dim]
    head = lax.slice_in_dim(field, 0, 1, axis=dim)
    tail = lax.slice_in_dim(field, size - 1, size, axis=dim)
    if axis is None:
        return jnp.zeros_like(head), jnp.zeros_like(tail)
    count = axis_count(axis)
    place = list(range(count))
    if axis == ROW_AXES:
        layers, rows = lax.axis_size("layer"), lax.axis_size("row")
        place = [(b % layers) * rows + b // layers for b in range(count)]
    if count == 2:
        low = lax.axis_index(axis) == 0
        got = lax.ppermute(jnp.where(low, tail, head), axis, [(0, 1), (1, 0)])
        zero = jnp.zeros_like(got)
        return jnp.where(low, got, zero), jnp.where(low, zero, got)
    below = lax.ppermute(tail, axis, [(place[i], place[i + 1]) for i in range(count - 1)])
    above = lax.ppermute(head, axis, [(place[i + 1], place[i]) for i in range(count - 1)])
    return above, below


def neighbours(field, halo):
    out = []
    for (axis, dim), (above, below) in zip(GRID_AXES, halo):
        size = field.shape[dim]
        out.append(jnp.concatenate([lax.slice_in_dim(field, 1, size, axis=dim), above], axis=dim))
        out.append(jnp.concatenate([below, lax.slice_in_dim(field, 0, size - 1, axis=dim)], axis=dim))
    return out


def exchange(field):
    return [rims(field, axis, dim) for axis, dim in ((None, 0), (ROW_AXES, 1), ("col", 2))]


def apply_grid(field, near, weights, pad_term):
    result = pad_term * field
    for weight, other in zip(weights, near):
        result = result + weight * (field - other)
    return result


def smooth(resid, weights, pad_term, inverse):
    theta = (bound_high + bound_low) / 2.0
    delta = (bound_high - bound_low) / 2.0
    sigma = theta / delta
    rho = 1.0 / sigma
    change = inverse * resid / theta
    total = change
    for sweep in range(DEG - 1):
        remain = resid - apply_grid(total, neighbours(total, exchange(total)), weights, pad_term)
        rho_new = 1.0 / (2.0 * sigma - rho)
        change = rho_new * rho * change + 2.0 * rho_new / delta * inverse * remain
        total = total + change
        rho = rho_new
    return total


def all_sum(value):
    for axis, _ in GRID_AXES:
        count = lax.axis_size(axis)
        if count & (count - 1):
            value = lax.psum(value, axis)
            continue
        step = 1
        while step < count:
            value = value + lax.ppermute(value, axis, [(i, i ^ step) for i in range(count)])
            step *= 2
    return value


def share_tiles(tiles, own_rows, own_cols, flat_tiles):
    layers, rows, cols = (lax.axis_size(axis) for axis, _ in GRID_AXES)
    count = layers * rows * cols
    payload = jnp.broadcast_to(tiles.reshape(1, -1), (count, tiles.size))
    got = lax.all_to_all(payload, ("layer", "row", "col"), 0, 0, tiled=True)
    tile_cols = cols * own_cols
    tile_row, tile_col = flat_tiles // tile_cols, flat_tiles % tile_cols
    block = tile_row // own_rows
    device = ((block % layers) * rows + block // layers) * cols + tile_col // own_cols
    slot = (tile_row % own_rows) * own_cols + tile_col % own_cols
    pick_device = (device[:, None] == jnp.arange(count, dtype=jnp.int32)[None, :]).astype(jnp.float32)
    pick_slot = (slot[:, None] == jnp.arange(tiles.size, dtype=jnp.int32)[None, :]).astype(jnp.float32)
    return jnp.sum(jnp.dot(pick_device, got, precision=solve_precision) * pick_slot, axis=1)


def swap_col(value):
    return lax.ppermute(value, "col", [(0, 1), (1, 0)])


def join_halves(mine, other, low):
    return jnp.where(low, jnp.concatenate([mine, other]), jnp.concatenate([other, mine]))


def coarse_pair(rhs, pivots, coupling, tie=None):
    share = pivots.shape[1]
    low = lax.axis_index("col") == 0
    start = lax.axis_index("col") * share
    own = lambda vector: lax.dynamic_slice_in_dim(vector, start, share)
    other_half = lambda vector: lax.dynamic_slice_in_dim(vector, share - start, share)
    full = rhs[0]
    forward = [full]
    for section in range(1, NPANEL):
        piece = own(rhs[section]) - jnp.dot(coupling[section - 1], full, precision=solve_precision)
        full = join_halves(piece, swap_col(piece), low)
        forward.append(full)
    scaled = [jnp.dot(pivots[section], forward[section], precision=solve_precision) for section in range(NPANEL)]
    mine = scaled[NPANEL - 1]
    results = [None] * NPANEL
    if tie is not None:
        mine, _ = lax.optimization_barrier((mine, tie))
    for section in range(NPANEL - 2, 0, -1):
        partial = jnp.dot(mine, coupling[section], precision=solve_precision)
        got = swap_col(jnp.concatenate([other_half(partial), mine]))
        results[section + 1] = join_halves(mine, got[share:], low)
        mine = scaled[section] - (own(partial) + got[:share])
    partial = jnp.dot(mine, coupling[0], precision=solve_precision)
    got = swap_col(jnp.concatenate([partial, scaled[0], mine]))
    results[1] = join_halves(mine, got[PANEL + share:], low)
    first = join_halves(scaled[0], got[PANEL:PANEL + share], low)
    low_part = jnp.where(low, partial, got[:PANEL])
    high_part = jnp.where(low, got[:PANEL], partial)
    results[0] = first - (low_part + high_part)
    return jnp.stack(results)


def coarse_general(rhs, pivots, coupling):
    share = pivots.shape[1]
    start = lax.axis_index("col") * share
    full = rhs[0]
    forward = [full]
    for section in range(1, NPANEL):
        piece = lax.dynamic_slice_in_dim(rhs[section], start, share) - jnp.dot(
            coupling[section - 1], full, precision=solve_precision
        )
        full = lax.all_gather(piece, "col", axis=0, tiled=True)
        forward.append(full)
    scaled = [jnp.dot(pivots[section], forward[section], precision=solve_precision) for section in range(NPANEL)]
    results = [None] * NPANEL
    for section in range(NPANEL - 1, -1, -1):
        placed = lax.dynamic_update_slice_in_dim(jnp.zeros((PANEL,), jnp.float32), scaled[section], start, 0)
        if section < NPANEL - 1:
            later_rows = lax.dynamic_slice_in_dim(results[section + 1], start, share)
            placed = placed - jnp.dot(later_rows, coupling[section], precision=solve_precision)
        results[section] = lax.psum(placed, "col")
    return jnp.stack(results)


def expand(values, edge):
    inner = values[1:-1] if edge else values
    body = jnp.repeat(inner, TILE, axis=0)
    if edge:
        body = jnp.concatenate([values[:1], body, values[-1:]], axis=0)
    return body


def shards(sources, conduct, via_cond, via_map, pad_map, port_tile, pivots, coupling):
    layer_count = lax.axis_size("layer")
    vertical = via_cond * via_map.astype(jnp.float32)
    given_rows = sources.shape[1] // TILE
    given_cols = sources.shape[2] // TILE
    given_tile_cols = given_cols * lax.axis_size("col")
    given_ids = (
        (lax.axis_index("row") * given_rows + jnp.arange(given_rows, dtype=jnp.int32))[:, None] * given_tile_cols
        + (lax.axis_index("col") * given_cols + jnp.arange(given_cols, dtype=jnp.int32))[None, :]
    ).reshape(-1)
    given_pick = (given_ids[:, None] == port_tile.reshape(-1)[None, :]).astype(jnp.float32)
    packed = lax.all_to_all(jnp.stack((conduct, vertical)), "layer", 2, 1, tiled=True)
    conduct, vertical = packed[0], packed[1]
    sources = lax.all_to_all(sources, "layer", 1, 0, tiled=True)
    local_layers, grid_rows, grid_cols = sources.shape
    pad_rows = lax.dynamic_slice_in_dim(pad_map, lax.axis_index("layer") * grid_rows, grid_rows, 0)
    row_halo = rims(conduct, ROW_AXES, 1)
    col_halo = rims(conduct, "col", 2)
    layer_halo = rims(vertical, None, 0)
    near_vert = neighbours(vertical, [layer_halo, row_halo, col_halo])
    near_plane = neighbours(conduct, [layer_halo, row_halo, col_halo])
    weights = (
        jnp.sqrt(vertical * near_vert[0]),
        jnp.sqrt(vertical * near_vert[1]),
        jnp.sqrt(conduct * near_plane[2]),
        jnp.sqrt(conduct * near_plane[3]),
        jnp.sqrt(conduct * near_plane[4]),
        jnp.sqrt(conduct * near_plane[5]),
    )
    top_layer = pad_gain * pad_rows.astype(jnp.float32)
    pad_term = jnp.concatenate(
        (jnp.zeros((local_layers - 1, grid_rows, grid_cols), jnp.float32), top_layer[None]), 0
    )
    diagonal = pad_term
    for weight in weights:
        diagonal = diagonal + weight
    inverse = 1.0 / diagonal

    col_count = lax.axis_size("col")
    tile_cols = grid_cols * col_count // TILE
    tile_rows = grid_rows * axis_count(ROW_AXES) // TILE
    own_rows = grid_rows // TILE
    own_cols = grid_cols // TILE
    first_row = (lax.axis_index("row") * layer_count + lax.axis_index("layer")) * own_rows
    first_col = lax.axis_index("col") * own_cols
    flat_tiles = port_tile.reshape(-1)
    ring_rows = first_row - 1 + jnp.arange(own_rows + 2, dtype=jnp.int32)
    ring_cols = first_col - 1 + jnp.arange(own_cols + 2, dtype=jnp.int32)
    ring_ok = ((ring_rows >= 0) & (ring_rows < tile_rows))[:, None] & ((ring_cols >= 0) & (ring_cols < tile_cols))[None, :]
    ring_ids = jnp.where(ring_ok, ring_rows[:, None] * tile_cols + ring_cols[None, :], -1).reshape(-1)
    scatter_ring = (ring_ids[:, None] == flat_tiles[None, :]).astype(jnp.float32)
    coarse = coarse_pair if col_count == 2 else coarse_general

    drop = None
    drop_near = None
    for outer in range(ITERS):
        if drop is None:
            resid = sources
        else:
            resid = sources - apply_grid(drop, drop_near, weights, pad_term)
        plane = jnp.sum(resid, axis=0)
        tiles = plane.reshape(own_rows, TILE, own_cols, TILE).sum(axis=(1, 3)).reshape(-1)
        rhs = share_tiles(tiles, own_rows, own_cols, flat_tiles).reshape(NPANEL, PANEL) * (restrict_scale / TILE)
        total = smooth(resid, weights, pad_term, inverse)
        if col_count == 2 and outer == ITERS - 1 and drop is not None:
            ports = coarse_pair(rhs, pivots, coupling, total)
        else:
            ports = coarse(rhs, pivots, coupling)
        tile_values = jnp.dot(scatter_ring, ports.reshape(-1), precision=solve_precision).reshape(own_rows + 2, own_cols + 2)
        ring = expand(expand(tile_values, True).T, True).T * prolong_scale
        centre = ring[1:-1, 1:-1]
        lifted = jnp.broadcast_to(centre[None], (local_layers, grid_rows, grid_cols))
        if outer == ITERS - 1 and drop is not None:
            both = lax.all_to_all(jnp.stack((drop, total)), "layer", 1, 2, tiled=True)
            given_values = jnp.dot(given_pick, ports.reshape(-1), precision=solve_precision).reshape(given_rows, given_cols)
            given_field = jnp.repeat(jnp.repeat(given_values, TILE, axis=0), TILE, axis=1) * prolong_scale
            given_lifted = jnp.broadcast_to(given_field[None], both.shape[1:])
            return ((both[0] + given_lifted) + both[1], ports)
        if outer == ITERS - 1:
            drop = (lifted if drop is None else drop + lifted) + total
            break
        lifted_near = [lifted, lifted]
        for part in (ring[2:, 1:-1], ring[:-2, 1:-1], ring[1:-1, 2:], ring[1:-1, :-2]):
            lifted_near.append(jnp.broadcast_to(part[None], (local_layers, grid_rows, grid_cols)))
        total_near = neighbours(total, exchange(total))
        if drop is None:
            drop = lifted + total
            drop_near = [a + b for a, b in zip(lifted_near, total_near)]
        else:
            drop = drop + lifted + total
            drop_near = [(d + a) + b for d, a, b in zip(drop_near, lifted_near, total_near)]
    drop = lax.all_to_all(drop, "layer", 0, 1, tiled=True)
    return (drop, ports)


def solution(mesh):
    placed = (
        P("layer", "row", "col"),
        P("layer", "row", "col"),
        P("layer", "row", "col"),
        P("layer", "row", "col"),
        P("row", "col"),
        P(),
        P(None, "col", None),
        P(None, "col", None),
    )
    return jax.shard_map(
        shards,
        mesh=mesh,
        in_specs=placed,
        out_specs=(P("layer", "row", "col"), P()),
        check_vma=False,
    )
```

```python
import jax
import jax.numpy as jnp
from jax import lax
from jax.sharding import PartitionSpec as P

TILE = 16
PANEL = 512
NPANEL = 4
DEG = 3
ITERS = 2


pad_gain = 8.0
bound_low = 0.1
bound_high = 1.9
restrict_scale = 0.25
prolong_scale = 0.5

highest = lax.Precision.HIGHEST
solve_precision = lax.Precision.HIGH
GRID_AXES = (("layer", 0), ("row", 1), ("col", 2))
ROW_AXES = ("layer", "row")


def axis_count(axis):
    names = axis if isinstance(axis, tuple) else (axis,)
    count = 1
    for name in names:
        count *= lax.axis_size(name)
    return count


def rims(field, axis, dim):
    size = field.shape[dim]
    head = lax.slice_in_dim(field, 0, 1, axis=dim)
    tail = lax.slice_in_dim(field, size - 1, size, axis=dim)
    if axis is None:
        return jnp.zeros_like(head), jnp.zeros_like(tail)
    count = axis_count(axis)
    place = list(range(count))
    if axis == ROW_AXES:
        layers, rows = lax.axis_size("layer"), lax.axis_size("row")
        place = [(b % layers) * rows + b // layers for b in range(count)]
    if count == 2:
        low = lax.axis_index(axis) == 0
        got = lax.ppermute(jnp.where(low, tail, head), axis, [(0, 1), (1, 0)])
        zero = jnp.zeros_like(got)
        return jnp.where(low, got, zero), jnp.where(low, zero, got)
    below = lax.ppermute(tail, axis, [(place[i], place[i + 1]) for i in range(count - 1)])
    above = lax.ppermute(head, axis, [(place[i + 1], place[i]) for i in range(count - 1)])
    return above, below


def neighbours(field, halo):
    out = []
    for (axis, dim), (above, below) in zip(GRID_AXES, halo):
        size = field.shape[dim]
        out.append(jnp.concatenate([lax.slice_in_dim(field, 1, size, axis=dim), above], axis=dim))
        out.append(jnp.concatenate([below, lax.slice_in_dim(field, 0, size - 1, axis=dim)], axis=dim))
    return out


def exchange(field):
    return [rims(field, axis, dim) for axis, dim in ((None, 0), (ROW_AXES, 1), ("col", 2))]


def apply_grid(field, near, weights, pad_term):
    result = pad_term * field
    for weight, other in zip(weights, near):
        result = result + weight * (field - other)
    return result


def smooth(resid, weights, pad_term, inverse):
    theta = (bound_high + bound_low) / 2.0
    delta = (bound_high - bound_low) / 2.0
    sigma = theta / delta
    rho = 1.0 / sigma
    change = inverse * resid / theta
    total = change
    for sweep in range(DEG - 1):
        remain = resid - apply_grid(total, neighbours(total, exchange(total)), weights, pad_term)
        rho_new = 1.0 / (2.0 * sigma - rho)
        change = rho_new * rho * change + 2.0 * rho_new / delta * inverse * remain
        total = total + change
        rho = rho_new
    return total


def all_sum(value):
    for axis, _ in GRID_AXES:
        count = lax.axis_size(axis)
        if count & (count - 1):
            value = lax.psum(value, axis)
            continue
        step = 1
        while step < count:
            value = value + lax.ppermute(value, axis, [(i, i ^ step) for i in range(count)])
            step *= 2
    return value


def share_tiles(tiles, own_rows, own_cols, flat_tiles):
    layers, rows, cols = (lax.axis_size(axis) for axis, _ in GRID_AXES)
    count = layers * rows * cols
    payload = jnp.broadcast_to(tiles.reshape(1, -1), (count, tiles.size))
    got = lax.all_to_all(payload, ("layer", "row", "col"), 0, 0, tiled=True)
    tile_cols = cols * own_cols
    tile_row, tile_col = flat_tiles // tile_cols, flat_tiles % tile_cols
    block = tile_row // own_rows
    device = ((block % layers) * rows + block // layers) * cols + tile_col // own_cols
    slot = (tile_row % own_rows) * own_cols + tile_col % own_cols
    pick_device = (device[:, None] == jnp.arange(count, dtype=jnp.int32)[None, :]).astype(jnp.float32)
    pick_slot = (slot[:, None] == jnp.arange(tiles.size, dtype=jnp.int32)[None, :]).astype(jnp.float32)
    return jnp.sum(jnp.dot(pick_device, got, precision=solve_precision) * pick_slot, axis=1)


def swap_col(value):
    return lax.ppermute(value, "col", [(0, 1), (1, 0)])


def join_halves(mine, other, low):
    return jnp.where(low, jnp.concatenate([mine, other]), jnp.concatenate([other, mine]))


def coarse_pair(rhs, pivots, coupling, tie=None):
    share = pivots.shape[1]
    low = lax.axis_index("col") == 0
    start = lax.axis_index("col") * share
    own = lambda vector: lax.dynamic_slice_in_dim(vector, start, share)
    other_half = lambda vector: lax.dynamic_slice_in_dim(vector, share - start, share)
    full = rhs[0]
    forward = [full]
    for section in range(1, NPANEL):
        piece = own(rhs[section]) - jnp.dot(coupling[section - 1], full, precision=solve_precision)
        full = join_halves(piece, swap_col(piece), low)
        forward.append(full)
    scaled = [jnp.dot(pivots[section], forward[section], precision=solve_precision) for section in range(NPANEL)]
    mine = scaled[NPANEL - 1]
    results = [None] * NPANEL
    if tie is not None:
        mine, _ = lax.optimization_barrier((mine, tie))
    for section in range(NPANEL - 2, 0, -1):
        partial = jnp.dot(mine, coupling[section], precision=solve_precision)
        got = swap_col(jnp.concatenate([other_half(partial), mine]))
        results[section + 1] = join_halves(mine, got[share:], low)
        mine = scaled[section] - (own(partial) + got[:share])
    partial = jnp.dot(mine, coupling[0], precision=solve_precision)
    got = swap_col(jnp.concatenate([partial, scaled[0], mine]))
    results[1] = join_halves(mine, got[PANEL + share:], low)
    first = join_halves(scaled[0], got[PANEL:PANEL + share], low)
    low_part = jnp.where(low, partial, got[:PANEL])
    high_part = jnp.where(low, got[:PANEL], partial)
    results[0] = first - (low_part + high_part)
    return jnp.stack(results)


def coarse_general(rhs, pivots, coupling):
    share = pivots.shape[1]
    start = lax.axis_index("col") * share
    full = rhs[0]
    forward = [full]
    for section in range(1, NPANEL):
        piece = lax.dynamic_slice_in_dim(rhs[section], start, share) - jnp.dot(
            coupling[section - 1], full, precision=solve_precision
        )
        full = lax.all_gather(piece, "col", axis=0, tiled=True)
        forward.append(full)
    scaled = [jnp.dot(pivots[section], forward[section], precision=solve_precision) for section in range(NPANEL)]
    results = [None] * NPANEL
    for section in range(NPANEL - 1, -1, -1):
        placed = lax.dynamic_update_slice_in_dim(jnp.zeros((PANEL,), jnp.float32), scaled[section], start, 0)
        if section < NPANEL - 1:
            later_rows = lax.dynamic_slice_in_dim(results[section + 1], start, share)
            placed = placed - jnp.dot(later_rows, coupling[section], precision=solve_precision)
        results[section] = lax.psum(placed, "col")
    return jnp.stack(results)


def expand(values, edge):
    inner = values[1:-1] if edge else values
    body = jnp.repeat(inner, TILE, axis=0)
    if edge:
        body = jnp.concatenate([values[:1], body, values[-1:]], axis=0)
    return body


def shards(sources, conduct, via_cond, via_map, pad_map, port_tile, pivots, coupling):
    layer_count = lax.axis_size("layer")
    vertical = via_cond * via_map.astype(jnp.float32)
    given_rows = sources.shape[1] // TILE
    given_cols = sources.shape[2] // TILE
    given_tile_cols = given_cols * lax.axis_size("col")
    given_ids = (
        (lax.axis_index("row") * given_rows + jnp.arange(given_rows, dtype=jnp.int32))[:, None] * given_tile_cols
        + (lax.axis_index("col") * given_cols + jnp.arange(given_cols, dtype=jnp.int32))[None, :]
    ).reshape(-1)
    given_pick = (given_ids[:, None] == port_tile.reshape(-1)[None, :]).astype(jnp.float32)
    packed = lax.all_to_all(jnp.stack((conduct, vertical)), "layer", 2, 1, tiled=True)
    conduct, vertical = packed[0], packed[1]
    sources = lax.all_to_all(sources, "layer", 1, 0, tiled=True)
    local_layers, grid_rows, grid_cols = sources.shape
    pad_rows = lax.dynamic_slice_in_dim(pad_map, lax.axis_index("layer") * grid_rows, grid_rows, 0)
    root_plane = jnp.sqrt(conduct)
    root_vert = jnp.sqrt(vertical)
    row_halo = rims(root_plane, ROW_AXES, 1)
    col_halo = rims(root_plane, "col", 2)
    layer_halo = rims(root_vert, None, 0)
    near_vert = neighbours(root_vert, [layer_halo, row_halo, col_halo])
    near_plane = neighbours(root_plane, [layer_halo, row_halo, col_halo])
    weights = (
        root_vert * near_vert[0],
        root_vert * near_vert[1],
        root_plane * near_plane[2],
        root_plane * near_plane[3],
        root_plane * near_plane[4],
        root_plane * near_plane[5],
    )
    top_layer = pad_gain * pad_rows.astype(jnp.float32)
    pad_term = jnp.concatenate(
        (jnp.zeros((local_layers - 1, grid_rows, grid_cols), jnp.float32), top_layer[None]), 0
    )
    diagonal = pad_term
    for weight in weights:
        diagonal = diagonal + weight
    inverse = 1.0 / diagonal

    col_count = lax.axis_size("col")
    tile_cols = grid_cols * col_count // TILE
    tile_rows = grid_rows * axis_count(ROW_AXES) // TILE
    own_rows = grid_rows // TILE
    own_cols = grid_cols // TILE
    first_row = (lax.axis_index("row") * layer_count + lax.axis_index("layer")) * own_rows
    first_col = lax.axis_index("col") * own_cols
    flat_tiles = port_tile.reshape(-1)
    ring_rows = first_row - 1 + jnp.arange(own_rows + 2, dtype=jnp.int32)
    ring_cols = first_col - 1 + jnp.arange(own_cols + 2, dtype=jnp.int32)
    ring_ok = ((ring_rows >= 0) & (ring_rows < tile_rows))[:, None] & ((ring_cols >= 0) & (ring_cols < tile_cols))[None, :]
    ring_ids = jnp.where(ring_ok, ring_rows[:, None] * tile_cols + ring_cols[None, :], -1).reshape(-1)
    scatter_ring = (ring_ids[:, None] == flat_tiles[None, :]).astype(jnp.float32)
    coarse = coarse_pair if col_count == 2 else coarse_general

    drop = None
    drop_near = None
    for outer in range(ITERS):
        if drop is None:
            resid = sources
        else:
            resid = sources - apply_grid(drop, drop_near, weights, pad_term)
        plane = jnp.sum(resid, axis=0)
        tiles = plane.reshape(own_rows, TILE, own_cols, TILE).sum(axis=(1, 3)).reshape(-1)
        rhs = share_tiles(tiles, own_rows, own_cols, flat_tiles).reshape(NPANEL, PANEL) * (restrict_scale / TILE)
        total = smooth(resid, weights, pad_term, inverse)
        if col_count == 2 and outer == ITERS - 1 and drop is not None:
            ports = coarse_pair(rhs, pivots, coupling, total)
        else:
            ports = coarse(rhs, pivots, coupling)
        tile_values = jnp.dot(scatter_ring, ports.reshape(-1), precision=solve_precision).reshape(own_rows + 2, own_cols + 2)
        ring = expand(expand(tile_values, True).T, True).T * prolong_scale
        centre = ring[1:-1, 1:-1]
        lifted = jnp.broadcast_to(centre[None], (local_layers, grid_rows, grid_cols))
        if outer == ITERS - 1 and drop is not None:
            both = lax.all_to_all(jnp.stack((drop, total)), "layer", 1, 2, tiled=True)
            given_values = jnp.dot(given_pick, ports.reshape(-1), precision=solve_precision).reshape(given_rows, given_cols)
            given_field = jnp.repeat(jnp.repeat(given_values, TILE, axis=0), TILE, axis=1) * prolong_scale
            given_lifted = jnp.broadcast_to(given_field[None], both.shape[1:])
            return ((both[0] + given_lifted) + both[1], ports)
        if outer == ITERS - 1:
            drop = (lifted if drop is None else drop + lifted) + total
            break
        lifted_near = [lifted, lifted]
        for part in (ring[2:, 1:-1], ring[:-2, 1:-1], ring[1:-1, 2:], ring[1:-1, :-2]):
            lifted_near.append(jnp.broadcast_to(part[None], (local_layers, grid_rows, grid_cols)))
        total_near = neighbours(total, exchange(total))
        if drop is None:
            drop = lifted + total
            drop_near = [a + b for a, b in zip(lifted_near, total_near)]
        else:
            drop = drop + lifted + total
            drop_near = [(d + a) + b for d, a, b in zip(drop_near, lifted_near, total_near)]
    drop = lax.all_to_all(drop, "layer", 0, 1, tiled=True)
    return (drop, ports)


def solution(mesh):
    placed = (
        P("layer", "row", "col"),
        P("layer", "row", "col"),
        P("layer", "row", "col"),
        P("layer", "row", "col"),
        P("row", "col"),
        P(),
        P(None, "col", None),
        P(None, "col", None),
    )
    return jax.shard_map(
        shards,
        mesh=mesh,
        in_specs=placed,
        out_specs=(P("layer", "row", "col"), P()),
        check_vma=False,
    )
```

```python
import jax
import jax.numpy as jnp
from jax import lax
from jax.sharding import PartitionSpec as P

TILE = 16
PANEL = 512
NPANEL = 4
DEG = 3
ITERS = 2


pad_gain = 8.0
bound_low = 0.1
bound_high = 1.9
restrict_scale = 0.25
prolong_scale = 0.5

highest = lax.Precision.HIGHEST
solve_precision = lax.Precision.HIGH
GRID_AXES = (("layer", 0), ("row", 1), ("col", 2))
ROW_AXES = ("layer", "row")


def axis_count(axis):
    names = axis if isinstance(axis, tuple) else (axis,)
    count = 1
    for name in names:
        count *= lax.axis_size(name)
    return count


def rims(field, axis, dim, ends_free=False):
    size = field.shape[dim]
    head = lax.slice_in_dim(field, 0, 1, axis=dim)
    tail = lax.slice_in_dim(field, size - 1, size, axis=dim)
    if axis is None:
        return jnp.zeros_like(head), jnp.zeros_like(tail)
    count = axis_count(axis)
    place = list(range(count))
    if axis == ROW_AXES:
        layers, rows = lax.axis_size("layer"), lax.axis_size("row")
        place = [(b % layers) * rows + b // layers for b in range(count)]
    if count == 2:
        low = lax.axis_index(axis) == 0
        got = lax.ppermute(jnp.where(low, tail, head), axis, [(0, 1), (1, 0)])
        if ends_free:
            return got, got
        zero = jnp.zeros_like(got)
        return jnp.where(low, got, zero), jnp.where(low, zero, got)
    below = lax.ppermute(tail, axis, [(place[i], place[i + 1]) for i in range(count - 1)])
    above = lax.ppermute(head, axis, [(place[i + 1], place[i]) for i in range(count - 1)])
    return above, below


def neighbours(field, halo):
    out = []
    for (axis, dim), (above, below) in zip(GRID_AXES, halo):
        size = field.shape[dim]
        out.append(jnp.concatenate([lax.slice_in_dim(field, 1, size, axis=dim), above], axis=dim))
        out.append(jnp.concatenate([below, lax.slice_in_dim(field, 0, size - 1, axis=dim)], axis=dim))
    return out


def exchange(field):
    return [rims(field, axis, dim, True) for axis, dim in ((None, 0), (ROW_AXES, 1), ("col", 2))]


def apply_grid(field, near, weights, pad_term):
    result = pad_term * field
    for weight, other in zip(weights, near):
        result = result + weight * (field - other)
    return result


def smooth(resid, weights, pad_term, inverse):
    theta = (bound_high + bound_low) / 2.0
    delta = (bound_high - bound_low) / 2.0
    sigma = theta / delta
    rho = 1.0 / sigma
    change = inverse * resid / theta
    total = change
    for sweep in range(DEG - 1):
        remain = resid - apply_grid(total, neighbours(total, exchange(total)), weights, pad_term)
        rho_new = 1.0 / (2.0 * sigma - rho)
        change = rho_new * rho * change + 2.0 * rho_new / delta * inverse * remain
        total = total + change
        rho = rho_new
    return total


def all_sum(value):
    for axis, _ in GRID_AXES:
        count = lax.axis_size(axis)
        if count & (count - 1):
            value = lax.psum(value, axis)
            continue
        step = 1
        while step < count:
            value = value + lax.ppermute(value, axis, [(i, i ^ step) for i in range(count)])
            step *= 2
    return value


def share_tiles(tiles, own_rows, own_cols, flat_tiles):
    layers, rows, cols = (lax.axis_size(axis) for axis, _ in GRID_AXES)
    count = layers * rows * cols
    payload = jnp.broadcast_to(tiles.reshape(1, -1), (count, tiles.size))
    got = lax.all_to_all(payload, ("layer", "row", "col"), 0, 0, tiled=True)
    tile_cols = cols * own_cols
    tile_row, tile_col = flat_tiles // tile_cols, flat_tiles % tile_cols
    block = tile_row // own_rows
    device = ((block % layers) * rows + block // layers) * cols + tile_col // own_cols
    slot = (tile_row % own_rows) * own_cols + tile_col % own_cols
    pick_device = (device[:, None] == jnp.arange(count, dtype=jnp.int32)[None, :]).astype(jnp.float32)
    pick_slot = (slot[:, None] == jnp.arange(tiles.size, dtype=jnp.int32)[None, :]).astype(jnp.float32)
    return jnp.sum(jnp.dot(pick_device, got, precision=solve_precision) * pick_slot, axis=1)


def swap_col(value):
    return lax.ppermute(value, "col", [(0, 1), (1, 0)])


def join_halves(mine, other, low):
    return jnp.where(low, jnp.concatenate([mine, other]), jnp.concatenate([other, mine]))


def coarse_pair(rhs, pivots, coupling, tie=None):
    share = pivots.shape[1]
    low = lax.axis_index("col") == 0
    start = lax.axis_index("col") * share
    own = lambda vector: lax.dynamic_slice_in_dim(vector, start, share)
    other_half = lambda vector: lax.dynamic_slice_in_dim(vector, share - start, share)
    full = rhs[0]
    forward = [full]
    for section in range(1, NPANEL):
        piece = own(rhs[section]) - jnp.dot(coupling[section - 1], full, precision=solve_precision)
        full = join_halves(piece, swap_col(piece), low)
        forward.append(full)
    scaled = [jnp.dot(pivots[section], forward[section], precision=solve_precision) for section in range(NPANEL)]
    mine = scaled[NPANEL - 1]
    results = [None] * NPANEL
    if tie is not None:
        mine, _ = lax.optimization_barrier((mine, tie))
    for section in range(NPANEL - 2, 0, -1):
        partial = jnp.dot(mine, coupling[section], precision=solve_precision)
        got = swap_col(jnp.concatenate([other_half(partial), mine]))
        results[section + 1] = join_halves(mine, got[share:], low)
        mine = scaled[section] - (own(partial) + got[:share])
    partial = jnp.dot(mine, coupling[0], precision=solve_precision)
    got = swap_col(jnp.concatenate([partial, scaled[0], mine]))
    results[1] = join_halves(mine, got[PANEL + share:], low)
    first = join_halves(scaled[0], got[PANEL:PANEL + share], low)
    low_part = jnp.where(low, partial, got[:PANEL])
    high_part = jnp.where(low, got[:PANEL], partial)
    results[0] = first - (low_part + high_part)
    return jnp.stack(results)


def coarse_general(rhs, pivots, coupling):
    share = pivots.shape[1]
    start = lax.axis_index("col") * share
    full = rhs[0]
    forward = [full]
    for section in range(1, NPANEL):
        piece = lax.dynamic_slice_in_dim(rhs[section], start, share) - jnp.dot(
            coupling[section - 1], full, precision=solve_precision
        )
        full = lax.all_gather(piece, "col", axis=0, tiled=True)
        forward.append(full)
    scaled = [jnp.dot(pivots[section], forward[section], precision=solve_precision) for section in range(NPANEL)]
    results = [None] * NPANEL
    for section in range(NPANEL - 1, -1, -1):
        placed = lax.dynamic_update_slice_in_dim(jnp.zeros((PANEL,), jnp.float32), scaled[section], start, 0)
        if section < NPANEL - 1:
            later_rows = lax.dynamic_slice_in_dim(results[section + 1], start, share)
            placed = placed - jnp.dot(later_rows, coupling[section], precision=solve_precision)
        results[section] = lax.psum(placed, "col")
    return jnp.stack(results)


def expand(values, edge):
    inner = values[1:-1] if edge else values
    body = jnp.repeat(inner, TILE, axis=0)
    if edge:
        body = jnp.concatenate([values[:1], body, values[-1:]], axis=0)
    return body


def shards(sources, conduct, via_cond, via_map, pad_map, port_tile, pivots, coupling):
    layer_count = lax.axis_size("layer")
    vertical = via_cond * via_map.astype(jnp.float32)
    given_rows = sources.shape[1] // TILE
    given_cols = sources.shape[2] // TILE
    given_tile_cols = given_cols * lax.axis_size("col")
    given_ids = (
        (lax.axis_index("row") * given_rows + jnp.arange(given_rows, dtype=jnp.int32))[:, None] * given_tile_cols
        + (lax.axis_index("col") * given_cols + jnp.arange(given_cols, dtype=jnp.int32))[None, :]
    ).reshape(-1)
    given_pick = (given_ids[:, None] == port_tile.reshape(-1)[None, :]).astype(jnp.float32)
    packed = lax.all_to_all(jnp.stack((conduct, vertical)), "layer", 2, 1, tiled=True)
    conduct, vertical = packed[0], packed[1]
    sources = lax.all_to_all(sources, "layer", 1, 0, tiled=True)
    local_layers, grid_rows, grid_cols = sources.shape
    pad_rows = lax.dynamic_slice_in_dim(pad_map, lax.axis_index("layer") * grid_rows, grid_rows, 0)
    root_plane = jnp.sqrt(conduct)
    root_vert = jnp.sqrt(vertical)
    row_halo = rims(root_plane, ROW_AXES, 1)
    col_halo = rims(root_plane, "col", 2)
    layer_halo = rims(root_vert, None, 0)
    near_vert = neighbours(root_vert, [layer_halo, row_halo, col_halo])
    near_plane = neighbours(root_plane, [layer_halo, row_halo, col_halo])
    weights = (
        root_vert * near_vert[0],
        root_vert * near_vert[1],
        root_plane * near_plane[2],
        root_plane * near_plane[3],
        root_plane * near_plane[4],
        root_plane * near_plane[5],
    )
    top_layer = pad_gain * pad_rows.astype(jnp.float32)
    pad_term = jnp.concatenate(
        (jnp.zeros((local_layers - 1, grid_rows, grid_cols), jnp.float32), top_layer[None]), 0
    )
    diagonal = pad_term
    for weight in weights:
        diagonal = diagonal + weight
    inverse = 1.0 / diagonal

    col_count = lax.axis_size("col")
    tile_cols = grid_cols * col_count // TILE
    tile_rows = grid_rows * axis_count(ROW_AXES) // TILE
    own_rows = grid_rows // TILE
    own_cols = grid_cols // TILE
    first_row = (lax.axis_index("row") * layer_count + lax.axis_index("layer")) * own_rows
    first_col = lax.axis_index("col") * own_cols
    flat_tiles = port_tile.reshape(-1)
    ring_rows = first_row - 1 + jnp.arange(own_rows + 2, dtype=jnp.int32)
    ring_cols = first_col - 1 + jnp.arange(own_cols + 2, dtype=jnp.int32)
    ring_ok = ((ring_rows >= 0) & (ring_rows < tile_rows))[:, None] & ((ring_cols >= 0) & (ring_cols < tile_cols))[None, :]
    ring_ids = jnp.where(ring_ok, ring_rows[:, None] * tile_cols + ring_cols[None, :], -1).reshape(-1)
    scatter_ring = (ring_ids[:, None] == flat_tiles[None, :]).astype(jnp.float32)
    coarse = coarse_pair if col_count == 2 else coarse_general

    drop = None
    drop_near = None
    for outer in range(ITERS):
        if drop is None:
            resid = sources
        else:
            resid = sources - apply_grid(drop, drop_near, weights, pad_term)
        plane = jnp.sum(resid, axis=0)
        tiles = plane.reshape(own_rows, TILE, own_cols, TILE).sum(axis=(1, 3)).reshape(-1)
        rhs = share_tiles(tiles, own_rows, own_cols, flat_tiles).reshape(NPANEL, PANEL) * (restrict_scale / TILE)
        total = smooth(resid, weights, pad_term, inverse)
        if col_count == 2 and outer == ITERS - 1 and drop is not None:
            ports = coarse_pair(rhs, pivots, coupling, total)
        else:
            ports = coarse(rhs, pivots, coupling)
        tile_values = jnp.dot(scatter_ring, ports.reshape(-1), precision=solve_precision).reshape(own_rows + 2, own_cols + 2)
        ring = expand(expand(tile_values, True).T, True).T * prolong_scale
        centre = ring[1:-1, 1:-1]
        lifted = jnp.broadcast_to(centre[None], (local_layers, grid_rows, grid_cols))
        if outer == ITERS - 1 and drop is not None:
            both = lax.all_to_all(jnp.stack((drop, total)), "layer", 1, 2, tiled=True)
            given_values = jnp.dot(given_pick, ports.reshape(-1), precision=solve_precision).reshape(given_rows, given_cols)
            given_field = jnp.repeat(jnp.repeat(given_values, TILE, axis=0), TILE, axis=1) * prolong_scale
            given_lifted = jnp.broadcast_to(given_field[None], both.shape[1:])
            return ((both[0] + given_lifted) + both[1], ports)
        if outer == ITERS - 1:
            drop = (lifted if drop is None else drop + lifted) + total
            break
        lifted_near = [lifted, lifted]
        for part in (ring[2:, 1:-1], ring[:-2, 1:-1], ring[1:-1, 2:], ring[1:-1, :-2]):
            lifted_near.append(jnp.broadcast_to(part[None], (local_layers, grid_rows, grid_cols)))
        total_near = neighbours(total, exchange(total))
        if drop is None:
            drop = lifted + total
            drop_near = [a + b for a, b in zip(lifted_near, total_near)]
        else:
            drop = drop + lifted + total
            drop_near = [(d + a) + b for d, a, b in zip(drop_near, lifted_near, total_near)]
    drop = lax.all_to_all(drop, "layer", 0, 1, tiled=True)
    return (drop, ports)


def solution(mesh):
    placed = (
        P("layer", "row", "col"),
        P("layer", "row", "col"),
        P("layer", "row", "col"),
        P("layer", "row", "col"),
        P("row", "col"),
        P(),
        P(None, "col", None),
        P(None, "col", None),
    )
    return jax.shard_map(
        shards,
        mesh=mesh,
        in_specs=placed,
        out_specs=(P("layer", "row", "col"), P()),
        check_vma=False,
    )
```
